32 devices in a mesh: parts: 2 (over x), ref: 16 (over z, y, core).
Axes of the slice: x: 2, y: 2, z: 4, core: 2. Of those that a mesh axis runs over, the one named last changes fastest.
Arguments:
- queries: float32 [4096, 128], P('parts'), parts along dimension 0, may hold values from -15 to 15, as said below
- references: float32 [65536, 128], P(('parts', 'ref')), parts along dimension 0, may hold values from -15 to 15
- query_ids: int32 [4096], P('parts'), parts along dimension 0, may hold values from 0 to 32767, as said below
- spread: float32 [128], replicated, may hold values from 0.5 to 2
- cotangent: float32 [4096], P('parts'), parts along dimension 0, may hold values from -4 to 4
Outputs:
- query_grad: float32 [4096, 128], P(('parts', 'ref')), parts along dimension 0
- reference_grad: float32 [65536, 128], P(('parts', 'ref')), parts along dimension 0
- spread_grad: float32 [256], P('parts'), parts along dimension 0
The draws below stay inside these ranges and needn't reach their ends.
There are 2 independent parts, one for each index of `parts`. The reference program is written for one: setup_inputs(seed, part) draws one part's arguments, and reference() takes and returns one part's arrays. A program takes and returns all parts, laid end to end along the dimension named above; an argument that names none is the same for every part. Nothing has to cross between parts.
Inputs may be any that keep to these rules, and one draw needn't show every extreme that they name: `query_ids`: distinct rows of the references; query i is the reference row query_ids_i. `queries`: row i equals row query_ids_i of references.
All inputs are finite; a program needn't handle non-finite values.
Results may differ from the reference program's by a relative error of at most 0.014.
Values sent between devices are 32-bit elements; how exact they have to be, the bound alone decides.
No kernel may reach another device: no remote copies, remote signals or barrier semaphores. Data moves between devices by JAX's collectives and lax.ppermute only.
A program may use at most 64 MiB of HBM per device.

```python
import math
import jax
import jax.numpy as jnp
from jax import lax

F = 128
NQ = 2048
R_DEV = 2048
NR = 32768
N_REF = 16


def shared_draw(key):
    key_z = jax.random.fold_in(key, 11)
    key_s = jax.random.fold_in(key, 12)
    key_i = jax.random.fold_in(key, 13)
    values = jnp.clip(jax.random.normal(key_z, (NR, F), jnp.float32), -5.0, 5.0)
    scales = jnp.exp(jax.random.uniform(key_s, (NR, 1), jnp.float32, math.log(0.3), math.log(3.0)))
    rows = values * scales
    picked = jax.random.permutation(key_i, NR)[:NQ].astype(jnp.int32)
    return (rows, picked)


def draw_references(key, part):
    rows, picked = shared_draw(key)
    return rows


def draw_queries(key, part):
    rows, picked = shared_draw(key)
    return rows[picked]


def draw_query_ids(key, part):
    rows, picked = shared_draw(key)
    return picked


def gaussian(rng, shape, deviation, reach, held_as=jnp.bfloat16):
    return jnp.clip(deviation * jax.random.normal(rng, shape, jnp.float32), -reach, reach).astype(held_as)


def setup_inputs(seed: int = 0, part: int = 0) -> dict:
    splits = jax.random.split(jax.random.key(seed), 6)
    own_keys = jax.random.split(jax.random.fold_in(splits[5], part), 6)
    return {
        "queries": draw_queries(jax.random.fold_in(jax.random.fold_in(splits[5], part), 71), part),
        "references": draw_references(jax.random.fold_in(jax.random.fold_in(splits[5], part), 71), part),
        "query_ids": draw_query_ids(jax.random.fold_in(jax.random.fold_in(splits[5], part), 71), part),
        "spread": jnp.clip(jnp.exp(jax.random.uniform(splits[3], (F,), jnp.float32, math.log(0.5), math.log(2.0))), 0.5, 2.0),
        "cotangent": gaussian(own_keys[4], (NQ,), 1.0, 4.0, jnp.float32),
    }


def reference(queries, references, query_ids, spread, cotangent):
    inv = 1.0 / (spread * spread)
    scaled = queries * inv
    qnorm = jnp.sum(queries * queries * inv, axis=1)
    ref_blocks = references.reshape(N_REF, R_DEV, F)
    starts = (jnp.arange(N_REF, dtype=jnp.int32) * R_DEV).astype(jnp.int32)
    columns = jnp.arange(R_DEV, dtype=jnp.int32)

    def block_score(block, start):
        cross = jnp.dot(scaled, block.T, precision=lax.Precision.HIGHEST, preferred_element_type=jnp.float32)
        rnorm = jnp.sum(block * block * inv, axis=1)
        score = cross - 0.5 * qnorm[:, None] - 0.5 * rnorm[None, :]
        self_mask = (query_ids - start)[:, None] == columns[None, :]
        return jnp.where(self_mask, -jnp.inf, score), self_mask

    def forward(carry, items):
        peak_now, total_now = carry
        block, start = items
        score, self_mask = block_score(block, start)
        new_peak = jnp.maximum(peak_now, jnp.max(score, axis=1))
        new_total = total_now * jnp.exp(peak_now - new_peak) + jnp.sum(jnp.exp(score - new_peak[:, None]), axis=1)
        return (new_peak, new_total), None

    init = (jnp.full((NQ,), -jnp.inf, jnp.float32), jnp.zeros((NQ,), jnp.float32))
    (peak, total), unused = lax.scan(forward, init, (ref_blocks, starts))
    query_low = queries.astype(jnp.bfloat16)

    def backward(pulled, items):
        block, start = items
        score, self_mask = block_score(block, start)
        weight = jnp.where(self_mask, 0.0, cotangent[:, None] * jnp.exp(score - peak[:, None]) / total[:, None]).astype(jnp.bfloat16)
        pulled = pulled + jnp.dot(weight, block.astype(jnp.bfloat16), preferred_element_type=jnp.float32)
        pushed = jnp.dot(weight.T, query_low, preferred_element_type=jnp.float32)
        column = jnp.sum(weight.astype(jnp.float32), axis=0)
        rgrad = (pushed - block * column[:, None]) * inv
        return pulled, (rgrad, jnp.sum(block * rgrad, axis=0))

    pulled, (rgrads, rdr) = lax.scan(backward, jnp.zeros((NQ, F), jnp.float32), (ref_blocks, starts))
    query_grad = (pulled - queries * cotangent[:, None]) * inv
    reference_grad = rgrads.reshape(NR, F)
    summed = jnp.sum(queries * query_grad, axis=0) + jnp.sum(rdr, axis=0)
    spread_grad = -summed / spread - jnp.sum(cotangent) / spread
    return query_grad, reference_grad, spread_grad
```

```python
import jax
import jax.numpy as jnp
from jax import lax
from jax.sharding import PartitionSpec as P


def block_score(query_block, id_block, references, rnorm, inv, ref_start):
    cross = lax.dot_general(
        query_block * inv,
        references,
        (((1,), (1,)), ((), ())),
        precision=lax.Precision.HIGHEST,
        preferred_element_type=jnp.float32,
    )
    qnorm = jnp.sum(query_block * query_block * inv, axis=1)
    score = cross - 0.5 * qnorm[:, None] - 0.5 * rnorm[None, :]
    local_ids = id_block - ref_start
    self_mask = local_ids[:, None] == lax.iota(jnp.int32, references.shape[0])[None, :]
    return (jnp.where(self_mask, -jnp.inf, score), self_mask)


def exchange(x, n_dev, step):
    return lax.ppermute(x, "ref", [(i, i ^ step) for i in range(n_dev)])


def butterfly_stats(peak, total, n_dev):
    step = 1
    while step < n_dev:
        other_peak, other_total = exchange((peak, total), n_dev, step)
        new_peak = jnp.maximum(peak, other_peak)
        total = total * jnp.exp(peak - new_peak) + other_total * jnp.exp(other_peak - new_peak)
        peak = new_peak
        step *= 2
    return peak, total


def halving_scatter(rows, extra, n_dev):
    me = lax.axis_index("ref")
    n_feat = rows.shape[-1]
    blocks = rows.reshape(n_dev, -1, n_feat)
    step = 1
    while step < n_dev:
        lead = n_dev // (2 * step)
        split = blocks.reshape(lead, 2, -1, n_feat)
        bit = (me // step) % 2
        keep = lax.dynamic_index_in_dim(split, bit, axis=1, keepdims=False)
        send = lax.dynamic_index_in_dim(split, 1 - bit, axis=1, keepdims=False)
        got, got_extra = exchange((send, extra), n_dev, step)
        blocks = keep + got
        extra = extra + got_extra
        step *= 2
    return blocks.reshape(-1, n_feat), extra


def on_device(queries, references, query_ids, spread, cotangent):
    n_query = queries.shape[0]
    n_feat = queries.shape[1]
    n_ref = references.shape[0]
    n_dev = lax.axis_size("ref")
    block_rows = min(512, n_query)
    n_blocks = n_query // block_rows
    inv = 1.0 / (spread * spread)
    rnorm = jnp.sum(references * references * inv, axis=1)
    ref_start = lax.axis_index("ref") * n_ref
    query_blocks = queries.reshape(n_blocks, block_rows, n_feat)
    id_blocks = query_ids.reshape(n_blocks, block_rows)
    weight_blocks = cotangent.reshape(n_blocks, block_rows)

    def local_density(items):
        query_block, id_block = items
        score, self_mask = block_score(query_block, id_block, references, rnorm, inv, ref_start)
        local_peak = jnp.max(score, axis=1)
        local_total = jnp.sum(jnp.exp(score - local_peak[:, None]), axis=1)
        return (local_peak, local_total)

    local_peak, local_total = lax.map(local_density, (query_blocks, id_blocks))
    peak, total = butterfly_stats(local_peak.reshape(n_query), local_total.reshape(n_query), n_dev)
    ref_low = references.astype(jnp.bfloat16)
    query_low_blocks = query_blocks.astype(jnp.bfloat16)

    def backward(carry, items):
        pushed, column = carry
        query_block, query_low, id_block, cot_block, peak_block, total_block = items
        score, self_mask = block_score(query_block, id_block, references, rnorm, inv, ref_start)
        weight = jnp.where(
            self_mask,
            0.0,
            cot_block[:, None] * jnp.exp(score - peak_block[:, None]) / total_block[:, None],
        ).astype(jnp.bfloat16)
        pulled = jnp.dot(weight, ref_low, preferred_element_type=jnp.float32)
        pushed = pushed + lax.dot_general(
            weight, query_low, (((0,), (0,)), ((), ())), preferred_element_type=jnp.float32
        )
        column = column + jnp.sum(weight.astype(jnp.float32), axis=0)
        return ((pushed, column), pulled)

    init = (jnp.zeros((n_ref, n_feat), jnp.float32), jnp.zeros((n_ref,), jnp.float32))
    items = (
        query_blocks,
        query_low_blocks,
        id_blocks,
        weight_blocks,
        peak.reshape(n_blocks, block_rows),
        total.reshape(n_blocks, block_rows),
    )
    (pushed, column), pulled = lax.scan(backward, init, items)
    pulled = pulled.reshape(n_query, n_feat)
    reference_grad = (pushed - references * column[:, None]) * inv
    local_terms = jnp.stack([jnp.sum(queries * pulled, axis=0), jnp.sum(references * reference_grad, axis=0)])
    own_pulled, summed_terms = halving_scatter(pulled, local_terms, n_dev)
    own_rows = n_query // n_dev
    own_start = lax.axis_index("ref") * own_rows
    own_queries = lax.dynamic_slice_in_dim(queries, own_start, own_rows, 0)
    own_cot = lax.dynamic_slice_in_dim(cotangent, own_start, own_rows, 0)
    query_grad = (own_pulled - own_queries * own_cot[:, None]) * inv
    self_terms = jnp.sum(queries * queries * cotangent[:, None], axis=0)
    summed = (summed_terms[0] - self_terms) * inv + summed_terms[1]
    weight_total = jnp.sum(cotangent)
    spread_grad = -summed / spread - weight_total / spread
    return (query_grad, reference_grad, spread_grad)


def solution(mesh):
    placed = (P("parts", None), P(("parts", "ref"), None), P("parts"), P(), P("parts"))
    return jax.shard_map(
        on_device,
        mesh=mesh,
        in_specs=placed,
        out_specs=(P(("parts", "ref"), None), P(("parts", "ref"), None), P("parts")),
        check_vma=False,
    )
```

```python
import jax
import jax.numpy as jnp
from jax import lax
from jax.sharding import PartitionSpec as P


def block_score(query_block, id_block, references, rnorm, inv, ref_start):
    cross = lax.dot_general(
        query_block * inv,
        references,
        (((1,), (1,)), ((), ())),
        precision=lax.Precision.HIGHEST,
        preferred_element_type=jnp.float32,
    )
    qnorm = jnp.sum(query_block * query_block * inv, axis=1)
    score = cross - 0.5 * qnorm[:, None] - 0.5 * rnorm[None, :]
    local_ids = id_block - ref_start
    self_mask = local_ids[:, None] == lax.iota(jnp.int32, references.shape[0])[None, :]
    return jnp.where(self_mask, -jnp.inf, score)


def exchange(x, n_dev, step):
    return lax.ppermute(x, "ref", [(i, i ^ step) for i in range(n_dev)])


def butterfly_stats(peak, total, n_dev):
    step = 1
    while step < n_dev:
        other_peak, other_total = exchange((peak, total), n_dev, step)
        new_peak = jnp.maximum(peak, other_peak)
        total = total * jnp.exp(peak - new_peak) + other_total * jnp.exp(other_peak - new_peak)
        peak = new_peak
        step *= 2
    return peak, total


def butterfly_sum(x, n_dev):
    step = 1
    while step < n_dev:
        x = x + exchange(x, n_dev, step)
        step *= 2
    return x


def halving_scatter(rows, n_dev):
    me = lax.axis_index("ref")
    n_feat = rows.shape[-1]
    blocks = rows.reshape(n_dev, -1, n_feat)
    step = 1
    while step < n_dev:
        lead = n_dev // (2 * step)
        split = blocks.reshape(lead, 2, -1, n_feat)
        bit = (me // step) % 2
        keep = lax.dynamic_index_in_dim(split, bit, axis=1, keepdims=False)
        send = lax.dynamic_index_in_dim(split, 1 - bit, axis=1, keepdims=False)
        blocks = keep + exchange(send, n_dev, step)
        step *= 2
    return blocks.reshape(-1, n_feat)


def on_device(queries, references, query_ids, spread, cotangent):
    n_query = queries.shape[0]
    n_feat = queries.shape[1]
    n_ref = references.shape[0]
    n_dev = lax.axis_size("ref")
    own_rows = n_query // n_dev
    n_blocks = 4 if own_rows % 4 == 0 else 1
    part_rows = own_rows // n_blocks
    inv = 1.0 / (spread * spread)
    rnorm = jnp.sum(references * references * inv, axis=1)
    ref_start = lax.axis_index("ref") * n_ref
    ref_low = references.astype(jnp.bfloat16)

    def interleave(x):
        tail = x.shape[1:]
        x = x.reshape((n_dev, n_blocks, part_rows) + tail)
        return jnp.moveaxis(x, 1, 0).reshape((n_blocks, n_dev * part_rows) + tail)

    query_blocks = interleave(queries)
    id_blocks = interleave(query_ids)
    cot_blocks = interleave(cotangent)

    kept = []
    for b in range(n_blocks):
        score = block_score(query_blocks[b], id_blocks[b], references, rnorm, inv, ref_start)
        local_peak = jnp.max(score, axis=1)
        expd = jnp.exp(score - local_peak[:, None])
        local_total = jnp.sum(expd, axis=1)
        expd_low = expd.astype(jnp.bfloat16)
        unscaled = jnp.dot(expd_low, ref_low, preferred_element_type=jnp.float32)
        peak, total = butterfly_stats(local_peak, local_total, n_dev)
        scale = cot_blocks[b] * jnp.exp(local_peak - peak) / total
        kept.append((expd_low, unscaled, scale))

    pushed = jnp.zeros((n_ref, n_feat), jnp.float32)
    column = jnp.zeros((n_ref,), jnp.float32)
    own_parts = []
    pull_terms = jnp.zeros((n_feat,), jnp.float32)
    for b in range(n_blocks):
        expd_low, unscaled, scale = kept[b]
        pulled = unscaled * scale[:, None]
        pull_terms = pull_terms + jnp.sum(query_blocks[b] * pulled, axis=0)
        own_parts.append(halving_scatter(pulled, n_dev))
        weight = (expd_low.astype(jnp.float32) * scale[:, None]).astype(jnp.bfloat16)
        pushed = pushed + lax.dot_general(
            weight, query_blocks[b].astype(jnp.bfloat16), (((0,), (0,)), ((), ())),
            preferred_element_type=jnp.float32,
        )
        column = column + jnp.sum(weight.astype(jnp.float32), axis=0)

    reference_grad = (pushed - references * column[:, None]) * inv
    local_terms = jnp.stack([pull_terms, jnp.sum(references * reference_grad, axis=0)])
    summed_terms = butterfly_sum(local_terms, n_dev)
    own_pulled = jnp.stack(own_parts).reshape(own_rows, n_feat)
    own_start = lax.axis_index("ref") * own_rows
    own_queries = lax.dynamic_slice_in_dim(queries, own_start, own_rows, 0)
    own_cot = lax.dynamic_slice_in_dim(cotangent, own_start, own_rows, 0)
    query_grad = (own_pulled - own_queries * own_cot[:, None]) * inv
    self_terms = jnp.sum(queries * queries * cotangent[:, None], axis=0)
    summed = (summed_terms[0] - self_terms) * inv + summed_terms[1]
    weight_total = jnp.sum(cotangent)
    spread_grad = -summed / spread - weight_total / spread
    return (query_grad, reference_grad, spread_grad)


def solution(mesh):
    placed = (P("parts", None), P(("parts", "ref"), None), P("parts"), P(), P("parts"))
    return jax.shard_map(
        on_device,
        mesh=mesh,
        in_specs=placed,
        out_specs=(P(("parts", "ref"), None), P(("parts", "ref"), None), P("parts")),
        check_vma=False,
    )
```

```python
import jax
import jax.numpy as jnp
from jax import lax
from jax.experimental import pallas as pl
from jax.experimental.pallas import tpu as pltpu
from jax.sharding import PartitionSpec as P

TILE = 256


def forward_kernel(qs_ref, qn_ref, id_ref, r_ref, rn_ref, rlow_ref, e_ref, u_ref, p_ref, t_ref):
    cross = lax.dot_general(
        qs_ref[...], r_ref[...], (((1,), (1,)), ((), ())),
        precision=lax.Precision.HIGHEST, preferred_element_type=jnp.float32,
    )
    score = cross - qn_ref[...] - rn_ref[...]
    col = lax.broadcasted_iota(jnp.int32, score.shape, 1)
    score = jnp.where(col == id_ref[...], -jnp.inf, score)
    peak = jnp.max(score, axis=1, keepdims=True)
    expd = jnp.exp(score - peak)
    p_ref[...] = peak
    t_ref[...] = jnp.sum(expd, axis=1, keepdims=True)
    expd_low = expd.astype(jnp.bfloat16)
    e_ref[...] = expd_low
    u_ref[...] = jnp.dot(expd_low, rlow_ref[...], preferred_element_type=jnp.float32)


def backward_kernel(e_ref, sc_ref, qlt_ref, pt_ref, col_ref):
    @pl.when(pl.program_id(0) == 0)
    def _():
        pt_ref[...] = jnp.zeros_like(pt_ref)
        col_ref[...] = jnp.zeros_like(col_ref)

    weight = (e_ref[...].astype(jnp.float32) * sc_ref[...]).astype(jnp.bfloat16)
    pt_ref[...] += jnp.dot(qlt_ref[...], weight, preferred_element_type=jnp.float32)
    col_ref[...] += jnp.sum(weight.astype(jnp.float32), axis=0, keepdims=True)


def local_forward(scaled, half_qnorm, local_ids, references, half_rnorm, ref_low):
    n_query, n_feat = scaled.shape
    n_ref = references.shape[0]
    tile = min(TILE, n_query)
    row = lambda i: (i, 0)
    whole = lambda i: (0, 0)
    return pl.pallas_call(
        forward_kernel,
        grid=(n_query // tile,),
        in_specs=[
            pl.BlockSpec((tile, n_feat), row),
            pl.BlockSpec((tile, 1), row),
            pl.BlockSpec((tile, 1), row),
            pl.BlockSpec((n_ref, n_feat), whole),
            pl.BlockSpec((1, n_ref), whole),
            pl.BlockSpec((n_ref, n_feat), whole),
        ],
        out_specs=[
            pl.BlockSpec((tile, n_ref), row),
            pl.BlockSpec((tile, n_feat), row),
            pl.BlockSpec((tile, 1), row),
            pl.BlockSpec((tile, 1), row),
        ],
        out_shape=[
            jax.ShapeDtypeStruct((n_query, n_ref), jnp.bfloat16),
            jax.ShapeDtypeStruct((n_query, n_feat), jnp.float32),
            jax.ShapeDtypeStruct((n_query, 1), jnp.float32),
            jax.ShapeDtypeStruct((n_query, 1), jnp.float32),
        ],
        compiler_params=pltpu.CompilerParams(dimension_semantics=("arbitrary",)),
    )(scaled, half_qnorm, local_ids, references, half_rnorm, ref_low)


def local_backward(expd_low, scale, query_low_t):
    n_query, n_ref = expd_low.shape
    n_feat = query_low_t.shape[0]
    tile = min(TILE, n_query)
    return pl.pallas_call(
        backward_kernel,
        grid=(n_query // tile,),
        in_specs=[
            pl.BlockSpec((tile, n_ref), lambda i: (i, 0)),
            pl.BlockSpec((tile, 1), lambda i: (i, 0)),
            pl.BlockSpec((n_feat, tile), lambda i: (0, i)),
        ],
        out_specs=[
            pl.BlockSpec((n_feat, n_ref), lambda i: (0, 0)),
            pl.BlockSpec((1, n_ref), lambda i: (0, 0)),
        ],
        out_shape=[
            jax.ShapeDtypeStruct((n_feat, n_ref), jnp.float32),
            jax.ShapeDtypeStruct((1, n_ref), jnp.float32),
        ],
        compiler_params=pltpu.CompilerParams(dimension_semantics=("arbitrary",)),
    )(expd_low, scale, query_low_t)


def exchange(x, n_dev, step):
    return lax.ppermute(x, "ref", [(i, i ^ step) for i in range(n_dev)])


def butterfly_stats(peak, total, n_dev):
    step = 1
    while step < n_dev:
        other_peak, other_total = exchange((peak, total), n_dev, step)
        new_peak = jnp.maximum(peak, other_peak)
        total = total * jnp.exp(peak - new_peak) + other_total * jnp.exp(other_peak - new_peak)
        peak = new_peak
        step *= 2
    return peak, total


def halving_scatter(rows, extra, n_dev):
    me = lax.axis_index("ref")
    n_feat = rows.shape[-1]
    blocks = rows.reshape(n_dev, -1, n_feat)
    step = 1
    while step < n_dev:
        lead = n_dev // (2 * step)
        split = blocks.reshape(lead, 2, -1, n_feat)
        bit = (me // step) % 2
        keep = lax.dynamic_index_in_dim(split, bit, axis=1, keepdims=False)
        send = lax.dynamic_index_in_dim(split, 1 - bit, axis=1, keepdims=False)
        got, got_extra = exchange((send, extra), n_dev, step)
        blocks = keep + got
        extra = extra + got_extra
        step *= 2
    return blocks.reshape(-1, n_feat), extra


def on_device(queries, references, query_ids, spread, cotangent):
    n_query = queries.shape[0]
    n_feat = queries.shape[1]
    n_ref = references.shape[0]
    n_dev = lax.axis_size("ref")
    inv = 1.0 / (spread * spread)
    rnorm = jnp.sum(references * references * inv, axis=1)
    qnorm = jnp.sum(queries * queries * inv, axis=1)
    ref_start = lax.axis_index("ref") * n_ref
    ref_low = references.astype(jnp.bfloat16)
    local_ids = (query_ids - ref_start)[:, None]

    expd_low, unscaled, local_peak, local_total = local_forward(
        queries * inv, (0.5 * qnorm)[:, None], local_ids, references, (0.5 * rnorm)[None, :], ref_low
    )
    peak, total = butterfly_stats(local_peak[:, 0], local_total[:, 0], n_dev)
    scale = cotangent * jnp.exp(local_peak[:, 0] - peak) / total
    pulled = unscaled * scale[:, None]
    pushed_t, column = local_backward(expd_low, scale[:, None], queries.astype(jnp.bfloat16).T)
    reference_grad = (pushed_t.T - references * column[0][:, None]) * inv
    local_terms = jnp.stack([jnp.sum(queries * pulled, axis=0), jnp.sum(references * reference_grad, axis=0)])
    own_pulled, summed_terms = halving_scatter(pulled, local_terms, n_dev)
    own_rows = n_query // n_dev
    own_start = lax.axis_index("ref") * own_rows
    own_queries = lax.dynamic_slice_in_dim(queries, own_start, own_rows, 0)
    own_cot = lax.dynamic_slice_in_dim(cotangent, own_start, own_rows, 0)
    query_grad = (own_pulled - own_queries * own_cot[:, None]) * inv
    self_terms = jnp.sum(queries * queries * cotangent[:, None], axis=0)
    summed = (summed_terms[0] - self_terms) * inv + summed_terms[1]
    weight_total = jnp.sum(cotangent)
    spread_grad = -summed / spread - weight_total / spread
    return (query_grad, reference_grad, spread_grad)


def solution(mesh):
    placed = (P("parts", None), P(("parts", "ref"), None), P("parts"), P(), P("parts"))
    return jax.shard_map(
        on_device,
        mesh=mesh,
        in_specs=placed,
        out_specs=(P(("parts", "ref"), None), P(("parts", "ref"), None), P("parts")),
        check_vma=False,
    )
```

```python
import jax
import jax.numpy as jnp
from jax import lax
from jax.experimental import pallas as pl
from jax.experimental.pallas import tpu as pltpu
from jax.sharding import PartitionSpec as P

TILE = 256


def forward_kernel(q_ref, inv_ref, lid_ref, r_ref, e_ref, ut_ref, p_ref, t_ref, rn_sc, rlt_sc):
    inv = inv_ref[...]

    @pl.when(pl.program_id(0) == 0)
    def _():
        refs = r_ref[...]
        rn_sc[...] = 0.5 * jnp.sum(refs * refs * inv, axis=1, keepdims=True)
        rlt_sc[...] = refs.T.astype(jnp.bfloat16)

    q = q_ref[...]
    ones = jnp.ones((8, q.shape[1]), jnp.float32)
    qnorm = lax.dot_general(
        ones, q * q * inv, (((1,), (1,)), ((), ())),
        precision=lax.Precision.HIGHEST, preferred_element_type=jnp.float32,
    )[0:1, :]
    cross = lax.dot_general(
        r_ref[...], q * inv, (((1,), (1,)), ((), ())),
        precision=lax.Precision.HIGHEST, preferred_element_type=jnp.float32,
    )
    score = cross - 0.5 * qnorm - rn_sc[...]
    row = lax.broadcasted_iota(jnp.int32, score.shape, 0)
    score = jnp.where(row == lid_ref[...], -jnp.inf, score)
    peak = jnp.max(score, axis=0, keepdims=True)
    expd = jnp.exp(score - peak)
    p_ref[...] = peak
    t_ref[...] = jnp.sum(expd, axis=0, keepdims=True)
    expd_low = expd.astype(jnp.bfloat16)
    e_ref[...] = expd_low
    ut_ref[...] = jnp.dot(rlt_sc[...], expd_low, preferred_element_type=jnp.float32)


def backward_kernel(e_ref, sc_ref, qa_ref, pa_ref):
    @pl.when(pl.program_id(0) == 0)
    def _():
        pa_ref[...] = jnp.zeros_like(pa_ref)

    weight = (e_ref[...].astype(jnp.float32) * sc_ref[...]).astype(jnp.bfloat16)
    pa_ref[...] += jnp.dot(weight, qa_ref[...], preferred_element_type=jnp.float32)


def local_forward(queries, inv, local_ids, references):
    n_query, n_feat = queries.shape
    n_ref = references.shape[0]
    tile = min(TILE, n_query)
    return pl.pallas_call(
        forward_kernel,
        grid=(n_query // tile,),
        in_specs=[
            pl.BlockSpec((tile, n_feat), lambda i: (i, 0)),
            pl.BlockSpec((1, n_feat), lambda i: (0, 0)),
            pl.BlockSpec((1, tile), lambda i: (0, i)),
            pl.BlockSpec((n_ref, n_feat), lambda i: (0, 0)),
        ],
        out_specs=[
            pl.BlockSpec((n_ref, tile), lambda i: (0, i)),
            pl.BlockSpec((n_feat, tile), lambda i: (0, i)),
            pl.BlockSpec((1, tile), lambda i: (0, i)),
            pl.BlockSpec((1, tile), lambda i: (0, i)),
        ],
        out_shape=[
            jax.ShapeDtypeStruct((n_ref, n_query), jnp.bfloat16),
            jax.ShapeDtypeStruct((n_feat, n_query), jnp.float32),
            jax.ShapeDtypeStruct((1, n_query), jnp.float32),
            jax.ShapeDtypeStruct((1, n_query), jnp.float32),
        ],
        scratch_shapes=[
            pltpu.VMEM((n_ref, 1), jnp.float32),
            pltpu.VMEM((n_feat, n_ref), jnp.bfloat16),
        ],
        compiler_params=pltpu.CompilerParams(dimension_semantics=("arbitrary",)),
    )(queries, inv, local_ids, references)


def local_backward(expd_low, scale, query_aug):
    n_ref, n_query = expd_low.shape
    width = query_aug.shape[1]
    tile = min(TILE, n_query)
    return pl.pallas_call(
        backward_kernel,
        grid=(n_query // tile,),
        in_specs=[
            pl.BlockSpec((n_ref, tile), lambda i: (0, i)),
            pl.BlockSpec((1, tile), lambda i: (0, i)),
            pl.BlockSpec((tile, width), lambda i: (i, 0)),
        ],
        out_specs=pl.BlockSpec((n_ref, width), lambda i: (0, 0)),
        out_shape=jax.ShapeDtypeStruct((n_ref, width), jnp.float32),
        compiler_params=pltpu.CompilerParams(dimension_semantics=("arbitrary",)),
    )(expd_low, scale, query_aug)


def exchange(x, n_dev, step):
    return lax.ppermute(x, "ref", [(i, i ^ step) for i in range(n_dev)])


def butterfly_stats(peak, total, n_dev):
    step = 1
    while step < n_dev:
        other_peak, other_total = exchange((peak, total), n_dev, step)
        new_peak = jnp.maximum(peak, other_peak)
        total = total * jnp.exp(peak - new_peak) + other_total * jnp.exp(other_peak - new_peak)
        peak = new_peak
        step *= 2
    return peak, total


def halving_scatter(rows, extra, n_dev):
    me = lax.axis_index("ref")
    n_feat = rows.shape[-1]
    blocks = rows.reshape(n_dev, -1, n_feat)
    step = 1
    while step < n_dev:
        lead = n_dev // (2 * step)
        split = blocks.reshape(lead, 2, -1, n_feat)
        bit = (me // step) % 2
        keep = lax.dynamic_index_in_dim(split, bit, axis=1, keepdims=False)
        send = lax.dynamic_index_in_dim(split, 1 - bit, axis=1, keepdims=False)
        got, got_extra = exchange((send, extra), n_dev, step)
        blocks = keep + got
        extra = extra + got_extra
        step *= 2
    return blocks.reshape(-1, n_feat), extra


def on_device(queries, references, query_ids, spread, cotangent):
    n_query = queries.shape[0]
    n_feat = queries.shape[1]
    n_ref = references.shape[0]
    n_dev = lax.axis_size("ref")
    inv = 1.0 / (spread * spread)
    ref_start = lax.axis_index("ref") * n_ref
    local_ids = (query_ids - ref_start)[None, :]
    expd_low, unscaled_t, local_peak, local_total = local_forward(queries, inv[None, :], local_ids, references)
    peak, total = butterfly_stats(local_peak[0], local_total[0], n_dev)
    scale = cotangent * jnp.exp(local_peak[0] - peak) / total
    pulled = (unscaled_t * scale[None, :]).T
    query_low = queries.astype(jnp.bfloat16)
    query_aug = jnp.concatenate(
        [query_low, jnp.ones((n_query, 1), jnp.bfloat16), jnp.zeros((n_query, n_feat - 1), jnp.bfloat16)], axis=1
    )
    pushed_aug = local_backward(expd_low, scale[None, :], query_aug)
    pushed = pushed_aug[:, :n_feat]
    column = pushed_aug[:, n_feat]
    reference_grad = (pushed - references * column[:, None]) * inv
    local_terms = jnp.stack([jnp.sum(queries * pulled, axis=0), jnp.sum(references * reference_grad, axis=0)])
    own_pulled, summed_terms = halving_scatter(pulled, local_terms, n_dev)
    own_rows = n_query // n_dev
    own_start = lax.axis_index("ref") * own_rows
    own_queries = lax.dynamic_slice_in_dim(queries, own_start, own_rows, 0)
    own_cot = lax.dynamic_slice_in_dim(cotangent, own_start, own_rows, 0)
    query_grad = (own_pulled - own_queries * own_cot[:, None]) * inv
    self_terms = jnp.sum(queries * queries * cotangent[:, None], axis=0)
    summed = (summed_terms[0] - self_terms) * inv + summed_terms[1]
    weight_total = jnp.sum(cotangent)
    spread_grad = -summed / spread - weight_total / spread
    return (query_grad, reference_grad, spread_grad)


def solution(mesh):
    placed = (P("parts", None), P(("parts", "ref"), None), P("parts"), P(), P("parts"))
    return jax.shard_map(
        on_device,
        mesh=mesh,
        in_specs=placed,
        out_specs=(P(("parts", "ref"), None), P(("parts", "ref"), None), P("parts")),
        check_vma=False,
    )
```

```python
import jax
import jax.numpy as jnp
from jax import lax
from jax.experimental import pallas as pl
from jax.experimental.pallas import tpu as pltpu
from jax.sharding import PartitionSpec as P

TILE = 512


def split3(x):
    x1 = x.astype(jnp.bfloat16)
    rest = x - x1.astype(jnp.float32)
    x2 = rest.astype(jnp.bfloat16)
    x3 = (rest - x2.astype(jnp.float32)).astype(jnp.bfloat16)
    return x1, x2, x3


def forward_kernel(q_ref, inv_ref, lid_ref, r_ref, e_ref, ut_ref, p_ref, t_ref, rn_sc, rlt_sc, rs_sc):
    inv = inv_ref[...]

    @pl.when(pl.program_id(0) == 0)
    def _():
        refs = r_ref[...]
        rn_sc[...] = 0.5 * jnp.sum(refs * refs * inv, axis=1, keepdims=True)
        rlt_sc[...] = refs.T.astype(jnp.bfloat16)
        r1, r2, r3 = split3(refs)
        rs_sc[...] = jnp.concatenate([r1, r1, r1, r2, r2, r3], axis=1)

    q = q_ref[...]
    ones = jnp.ones((8, q.shape[1]), jnp.float32)
    qnorm = lax.dot_general(
        ones, q * q * inv, (((1,), (1,)), ((), ())),
        precision=lax.Precision.HIGHEST, preferred_element_type=jnp.float32,
    )[0:1, :]
    q1, q2, q3 = split3(q * inv)
    cross = lax.dot_general(
        rs_sc[...], jnp.concatenate([q1, q2, q3, q1, q2, q1], axis=1), (((1,), (1,)), ((), ())),
        preferred_element_type=jnp.float32,
    )
    score = cross - 0.5 * qnorm - rn_sc[...]
    row = lax.broadcasted_iota(jnp.int32, score.shape, 0)
    score = jnp.where(row == lid_ref[...], -jnp.inf, score)
    peak = jnp.max(score, axis=0, keepdims=True)
    expd = jnp.exp(score - peak)
    p_ref[...] = peak
    t_ref[...] = jnp.sum(expd, axis=0, keepdims=True)
    expd_low = expd.astype(jnp.bfloat16)
    e_ref[...] = expd_low
    ut_ref[...] = jnp.dot(rlt_sc[...], expd_low, preferred_element_type=jnp.float32)


def backward_kernel(e_ref, sc_ref, qa_ref, pa_ref):
    @pl.when(pl.program_id(0) == 0)
    def _():
        pa_ref[...] = jnp.zeros_like(pa_ref)

    weight = (e_ref[...].astype(jnp.float32) * sc_ref[...]).astype(jnp.bfloat16)
    pa_ref[...] += jnp.dot(weight, qa_ref[...], preferred_element_type=jnp.float32)


def local_forward(queries, inv, local_ids, references):
    n_query, n_feat = queries.shape
    n_ref = references.shape[0]
    tile = min(TILE, n_query)
    return pl.pallas_call(
        forward_kernel,
        grid=(n_query // tile,),
        in_specs=[
            pl.BlockSpec((tile, n_feat), lambda i: (i, 0)),
            pl.BlockSpec((1, n_feat), lambda i: (0, 0)),
            pl.BlockSpec((1, tile), lambda i: (0, i)),
            pl.BlockSpec((n_ref, n_feat), lambda i: (0, 0)),
        ],
        out_specs=[
            pl.BlockSpec((n_ref, tile), lambda i: (0, i)),
            pl.BlockSpec((n_feat, tile), lambda i: (0, i)),
            pl.BlockSpec((1, tile), lambda i: (0, i)),
            pl.BlockSpec((1, tile), lambda i: (0, i)),
        ],
        out_shape=[
            jax.ShapeDtypeStruct((n_ref, n_query), jnp.bfloat16),
            jax.ShapeDtypeStruct((n_feat, n_query), jnp.float32),
            jax.ShapeDtypeStruct((1, n_query), jnp.float32),
            jax.ShapeDtypeStruct((1, n_query), jnp.float32),
        ],
        scratch_shapes=[
            pltpu.VMEM((n_ref, 1), jnp.float32),
            pltpu.VMEM((n_feat, n_ref), jnp.bfloat16),
            pltpu.VMEM((n_ref, 6 * n_feat), jnp.bfloat16),
        ],
        compiler_params=pltpu.CompilerParams(dimension_semantics=("arbitrary",)),
    )(queries, inv, local_ids, references)


def local_backward(expd_low, scale, query_aug):
    n_ref, n_query = expd_low.shape
    width = query_aug.shape[1]
    tile = min(TILE, n_query)
    return pl.pallas_call(
        backward_kernel,
        grid=(n_query // tile,),
        in_specs=[
            pl.BlockSpec((n_ref, tile), lambda i: (0, i)),
            pl.BlockSpec((1, tile), lambda i: (0, i)),
            pl.BlockSpec((tile, width), lambda i: (i, 0)),
        ],
        out_specs=pl.BlockSpec((n_ref, width), lambda i: (0, 0)),
        out_shape=jax.ShapeDtypeStruct((n_ref, width), jnp.float32),
        compiler_params=pltpu.CompilerParams(dimension_semantics=("arbitrary",)),
    )(expd_low, scale, query_aug)


def exchange(x, n_dev, step):
    return lax.ppermute(x, "ref", [(i, i ^ step) for i in range(n_dev)])


def butterfly_stats(peak, total, n_dev):
    step = 1
    while step < n_dev:
        other_peak, other_total = exchange((peak, total), n_dev, step)
        new_peak = jnp.maximum(peak, other_peak)
        total = total * jnp.exp(peak - new_peak) + other_total * jnp.exp(other_peak - new_peak)
        peak = new_peak
        step *= 2
    return peak, total


def halving_scatter(rows, extra, n_dev):
    me = lax.axis_index("ref")
    n_feat = rows.shape[-1]
    blocks = rows.reshape(n_dev, -1, n_feat)
    step = 1
    while step < n_dev:
        lead = n_dev // (2 * step)
        split = blocks.reshape(lead, 2, -1, n_feat)
        bit = (me // step) % 2
        keep = lax.dynamic_index_in_dim(split, bit, axis=1, keepdims=False)
        send = lax.dynamic_index_in_dim(split, 1 - bit, axis=1, keepdims=False)
        got, got_extra = exchange((send, extra), n_dev, step)
        blocks = keep + got
        extra = extra + got_extra
        step *= 2
    return blocks.reshape(-1, n_feat), extra


def on_device(queries, references, query_ids, spread, cotangent):
    n_query = queries.shape[0]
    n_feat = queries.shape[1]
    n_ref = references.shape[0]
    n_dev = lax.axis_size("ref")
    inv = 1.0 / (spread * spread)
    ref_start = lax.axis_index("ref") * n_ref
    local_ids = (query_ids - ref_start)[None, :]
    expd_low, unscaled_t, local_peak, local_total = local_forward(queries, inv[None, :], local_ids, references)
    peak, total = butterfly_stats(local_peak[0], local_total[0], n_dev)
    scale = cotangent * jnp.exp(local_peak[0] - peak) / total
    pulled = (unscaled_t * scale[None, :]).T
    query_low = queries.astype(jnp.bfloat16)
    query_aug = jnp.concatenate(
        [query_low, jnp.ones((n_query, 1), jnp.bfloat16), jnp.zeros((n_query, n_feat - 1), jnp.bfloat16)], axis=1
    )
    pushed_aug = local_backward(expd_low, scale[None, :], query_aug)
    pushed = pushed_aug[:, :n_feat]
    column = pushed_aug[:, n_feat]
    reference_grad = (pushed - references * column[:, None]) * inv
    local_terms = jnp.stack([jnp.sum(queries * pulled, axis=0), jnp.sum(references * reference_grad, axis=0)])
    own_pulled, summed_terms = halving_scatter(pulled, local_terms, n_dev)
    own_rows = n_query // n_dev
    own_start = lax.axis_index("ref") * own_rows
    own_queries = lax.dynamic_slice_in_dim(queries, own_start, own_rows, 0)
    own_cot = lax.dynamic_slice_in_dim(cotangent, own_start, own_rows, 0)
    query_grad = (own_pulled - own_queries * own_cot[:, None]) * inv
    self_terms = jnp.sum(queries * queries * cotangent[:, None], axis=0)
    summed = (summed_terms[0] - self_terms) * inv + summed_terms[1]
    weight_total = jnp.sum(cotangent)
    spread_grad = -summed / spread - weight_total / spread
    return (query_grad, reference_grad, spread_grad)


def solution(mesh):
    placed = (P("parts", None), P(("parts", "ref"), None), P("parts"), P(), P("parts"))
    return jax.shard_map(
        on_device,
        mesh=mesh,
        in_specs=placed,
        out_specs=(P(("parts", "ref"), None), P(("parts", "ref"), None), P("parts")),
        check_vma=False,
    )
```

```python
import jax
import jax.numpy as jnp
from jax import lax
from jax.experimental import pallas as pl
from jax.experimental.pallas import tpu as pltpu
from jax.sharding import PartitionSpec as P

TILE = 512


def split3(x):
    x1 = x.astype(jnp.bfloat16)
    rest = x - x1.astype(jnp.float32)
    x2 = rest.astype(jnp.bfloat16)
    x3 = (rest - x2.astype(jnp.float32)).astype(jnp.bfloat16)
    return x1, x2, x3


def forward_kernel(q_ref, inv_ref, lid_ref, r_ref, e_ref, ut_ref, p_ref, t_ref, rn_sc, rlt_sc, rs_sc):
    inv = inv_ref[...]

    @pl.when(pl.program_id(0) == 0)
    def _():
        refs = r_ref[...]
        rn_sc[...] = 0.5 * jnp.sum(refs * refs * inv, axis=1, keepdims=True)
        rlt_sc[...] = refs.T.astype(jnp.bfloat16)
        r1, r2, r3 = split3(refs)
        rs_sc[...] = jnp.concatenate([r1, r1, r1, r2, r2, r3], axis=1)

    q = q_ref[...]
    ones = jnp.ones((8, q.shape[1]), jnp.float32)
    qnorm = lax.dot_general(
        ones, q * q * inv, (((1,), (1,)), ((), ())),
        precision=lax.Precision.HIGHEST, preferred_element_type=jnp.float32,
    )[0:1, :]
    q1, q2, q3 = split3(q * inv)
    cross = lax.dot_general(
        rs_sc[...], jnp.concatenate([q1, q2, q3, q1, q2, q1], axis=1), (((1,), (1,)), ((), ())),
        preferred_element_type=jnp.float32,
    )
    score = cross - 0.5 * qnorm - rn_sc[...]
    row = lax.broadcasted_iota(jnp.int32, score.shape, 0)
    score = jnp.where(row == lid_ref[...], -jnp.inf, score)
    peak = jnp.max(score, axis=0, keepdims=True)
    expd = jnp.exp(score - peak)
    p_ref[...] = peak
    t_ref[...] = jnp.sum(expd, axis=0, keepdims=True)
    expd_low = expd.astype(jnp.bfloat16)
    e_ref[...] = expd_low
    ut_ref[...] = jnp.dot(rlt_sc[...], expd_low, preferred_element_type=jnp.float32)


def backward_kernel(e_ref, sc_ref, qa_ref, pa_ref):
    @pl.when(pl.program_id(0) == 0)
    def _():
        pa_ref[...] = jnp.zeros_like(pa_ref)

    weight = (e_ref[...].astype(jnp.float32) * sc_ref[...]).astype(jnp.bfloat16)
    pa_ref[...] += jnp.dot(weight, qa_ref[...], preferred_element_type=jnp.float32)


def local_forward(queries, inv, local_ids, references):
    n_query, n_feat = queries.shape
    n_ref = references.shape[0]
    tile = min(TILE, n_query)
    return pl.pallas_call(
        forward_kernel,
        grid=(n_query // tile,),
        in_specs=[
            pl.BlockSpec((tile, n_feat), lambda i: (i, 0)),
            pl.BlockSpec((1, n_feat), lambda i: (0, 0)),
            pl.BlockSpec((1, tile), lambda i: (0, i)),
            pl.BlockSpec((n_ref, n_feat), lambda i: (0, 0)),
        ],
        out_specs=[
            pl.BlockSpec((n_ref, tile), lambda i: (0, i)),
            pl.BlockSpec((n_feat, tile), lambda i: (0, i)),
            pl.BlockSpec((1, tile), lambda i: (0, i)),
            pl.BlockSpec((1, tile), lambda i: (0, i)),
        ],
        out_shape=[
            jax.ShapeDtypeStruct((n_ref, n_query), jnp.bfloat16),
            jax.ShapeDtypeStruct((n_feat, n_query), jnp.float32),
            jax.ShapeDtypeStruct((1, n_query), jnp.float32),
            jax.ShapeDtypeStruct((1, n_query), jnp.float32),
        ],
        scratch_shapes=[
            pltpu.VMEM((n_ref, 1), jnp.float32),
            pltpu.VMEM((n_feat, n_ref), jnp.bfloat16),
            pltpu.VMEM((n_ref, 6 * n_feat), jnp.bfloat16),
        ],
        compiler_params=pltpu.CompilerParams(dimension_semantics=("arbitrary",)),
    )(queries, inv, local_ids, references)


def local_backward(expd_low, scale, query_aug):
    n_ref, n_query = expd_low.shape
    width = query_aug.shape[1]
    tile = min(TILE, n_query)
    return pl.pallas_call(
        backward_kernel,
        grid=(n_query // tile,),
        in_specs=[
            pl.BlockSpec((n_ref, tile), lambda i: (0, i)),
            pl.BlockSpec((1, tile), lambda i: (0, i)),
            pl.BlockSpec((tile, width), lambda i: (i, 0)),
        ],
        out_specs=pl.BlockSpec((n_ref, width), lambda i: (0, 0)),
        out_shape=jax.ShapeDtypeStruct((n_ref, width), jnp.float32),
        compiler_params=pltpu.CompilerParams(dimension_semantics=("arbitrary",)),
    )(expd_low, scale, query_aug)


def exchange(x, n_dev, step):
    return lax.ppermute(x, "ref", [(i, i ^ step) for i in range(n_dev)])


def butterfly_stats(peak, total, n_dev):
    step = 1
    while step < n_dev:
        other = exchange(jnp.stack([peak, total]), n_dev, step)
        other_peak, other_total = other[0], other[1]
        new_peak = jnp.maximum(peak, other_peak)
        total = total * jnp.exp(peak - new_peak) + other_total * jnp.exp(other_peak - new_peak)
        peak = new_peak
        step *= 2
    return peak, total


def halving_scatter(rows, extra, n_dev):
    me = lax.axis_index("ref")
    n_feat = rows.shape[-1]
    blocks = rows.reshape(n_dev, -1, n_feat)
    step = 1
    while step < n_dev:
        lead = n_dev // (2 * step)
        split = blocks.reshape(lead, 2, -1, n_feat)
        bit = (me // step) % 2
        keep = lax.dynamic_index_in_dim(split, bit, axis=1, keepdims=False)
        send = lax.dynamic_index_in_dim(split, 1 - bit, axis=1, keepdims=False)
        n_send = send.shape[0] * send.shape[1]
        got = exchange(jnp.concatenate([send.reshape(n_send, n_feat), extra]), n_dev, step)
        blocks = keep + got[:n_send].reshape(keep.shape)
        extra = extra + got[n_send:]
        step *= 2
    return blocks.reshape(-1, n_feat), extra


def on_device(queries, references, query_ids, spread, cotangent):
    n_query = queries.shape[0]
    n_feat = queries.shape[1]
    n_ref = references.shape[0]
    n_dev = lax.axis_size("ref")
    inv = 1.0 / (spread * spread)
    ref_start = lax.axis_index("ref") * n_ref
    local_ids = (query_ids - ref_start)[None, :]
    expd_low, unscaled_t, local_peak, local_total = local_forward(queries, inv[None, :], local_ids, references)
    peak, total = butterfly_stats(local_peak[0], local_total[0], n_dev)
    scale = cotangent * jnp.exp(local_peak[0] - peak) / total
    pulled = (unscaled_t * scale[None, :]).T
    query_low = queries.astype(jnp.bfloat16)
    query_aug = jnp.concatenate(
        [query_low, jnp.ones((n_query, 1), jnp.bfloat16), jnp.zeros((n_query, n_feat - 1), jnp.bfloat16)], axis=1
    )
    pushed_aug = local_backward(expd_low, scale[None, :], query_aug)
    pushed = pushed_aug[:, :n_feat]
    column = pushed_aug[:, n_feat]
    reference_grad = (pushed - references * column[:, None]) * inv
    local_terms = jnp.stack([jnp.sum(queries * pulled, axis=0), jnp.sum(references * reference_grad, axis=0)])
    own_pulled, summed_terms = halving_scatter(pulled, local_terms, n_dev)
    own_rows = n_query // n_dev
    own_start = lax.axis_index("ref") * own_rows
    own_queries = lax.dynamic_slice_in_dim(queries, own_start, own_rows, 0)
    own_cot = lax.dynamic_slice_in_dim(cotangent, own_start, own_rows, 0)
    query_grad = (own_pulled - own_queries * own_cot[:, None]) * inv
    self_terms = jnp.sum(queries * queries * cotangent[:, None], axis=0)
    summed = (summed_terms[0] - self_terms) * inv + summed_terms[1]
    weight_total = jnp.sum(cotangent)
    spread_grad = -summed / spread - weight_total / spread
    return (query_grad, reference_grad, spread_grad)


def solution(mesh):
    placed = (P("parts", None), P(("parts", "ref"), None), P("parts"), P(), P("parts"))
    return jax.shard_map(
        on_device,
        mesh=mesh,
        in_specs=placed,
        out_specs=(P(("parts", "ref"), None), P(("parts", "ref"), None), P("parts")),
        check_vma=False,
    )
```

```python
import numpy as np
import jax
import jax.numpy as jnp
from jax import lax
from jax.experimental import pallas as pl
from jax.experimental.pallas import tpu as pltpu
from jax.sharding import PartitionSpec as P

TILE = 512


def split3(x):
    x1 = x.astype(jnp.bfloat16)
    rest = x - x1.astype(jnp.float32)
    x2 = rest.astype(jnp.bfloat16)
    x3 = (rest - x2.astype(jnp.float32)).astype(jnp.bfloat16)
    return x1, x2, x3


def forward_kernel(q_ref, inv_ref, lid_ref, r_ref, e_ref, ut_ref, p_ref, t_ref, rn_sc, rlt_sc, rs_sc):
    inv = inv_ref[...]

    @pl.when(pl.program_id(0) == 0)
    def _():
        refs = r_ref[...]
        rn_sc[...] = 0.5 * jnp.sum(refs * refs * inv, axis=1, keepdims=True)
        rlt_sc[...] = refs.T.astype(jnp.bfloat16)
        r1, r2, r3 = split3(refs)
        rs_sc[...] = jnp.concatenate([r1, r1, r1, r2, r2, r3], axis=1)

    q = q_ref[...]
    ones = jnp.ones((8, q.shape[1]), jnp.float32)
    qnorm = lax.dot_general(
        ones, q * q * inv, (((1,), (1,)), ((), ())),
        precision=lax.Precision.HIGHEST, preferred_element_type=jnp.float32,
    )[0:1, :]
    q1, q2, q3 = split3(q * inv)
    cross = lax.dot_general(
        rs_sc[...], jnp.concatenate([q1, q2, q3, q1, q2, q1], axis=1), (((1,), (1,)), ((), ())),
        preferred_element_type=jnp.float32,
    )
    score = cross - 0.5 * qnorm - rn_sc[...]
    row = lax.broadcasted_iota(jnp.int32, score.shape, 0)
    score = jnp.where(row == lid_ref[...], -jnp.inf, score)
    peak = jnp.max(score, axis=0, keepdims=True)
    expd = jnp.exp(score - peak)
    p_ref[...] = peak
    t_ref[...] = jnp.sum(expd, axis=0, keepdims=True)
    expd_low = expd.astype(jnp.bfloat16)
    e_ref[...] = expd_low
    ut_ref[...] = jnp.dot(rlt_sc[...], expd_low, preferred_element_type=jnp.float32)


def backward_kernel(e_ref, sc_ref, qa_ref, pa_ref):
    @pl.when(pl.program_id(0) == 0)
    def _():
        pa_ref[...] = jnp.zeros_like(pa_ref)

    weight = (e_ref[...].astype(jnp.float32) * sc_ref[...]).astype(jnp.bfloat16)
    pa_ref[...] += jnp.dot(weight, qa_ref[...], preferred_element_type=jnp.float32)


def local_forward(queries, inv, local_ids, references):
    n_query, n_feat = queries.shape
    n_ref = references.shape[0]
    tile = min(TILE, n_query)
    return pl.pallas_call(
        forward_kernel,
        grid=(n_query // tile,),
        in_specs=[
            pl.BlockSpec((tile, n_feat), lambda i: (i, 0)),
            pl.BlockSpec((1, n_feat), lambda i: (0, 0)),
            pl.BlockSpec((1, tile), lambda i: (0, i)),
            pl.BlockSpec((n_ref, n_feat), lambda i: (0, 0)),
        ],
        out_specs=[
            pl.BlockSpec((n_ref, tile), lambda i: (0, i)),
            pl.BlockSpec((n_feat, tile), lambda i: (0, i)),
            pl.BlockSpec((1, tile), lambda i: (0, i)),
            pl.BlockSpec((1, tile), lambda i: (0, i)),
        ],
        out_shape=[
            jax.ShapeDtypeStruct((n_ref, n_query), jnp.bfloat16),
            jax.ShapeDtypeStruct((n_feat, n_query), jnp.float32),
            jax.ShapeDtypeStruct((1, n_query), jnp.float32),
            jax.ShapeDtypeStruct((1, n_query), jnp.float32),
        ],
        scratch_shapes=[
            pltpu.VMEM((n_ref, 1), jnp.float32),
            pltpu.VMEM((n_feat, n_ref), jnp.bfloat16),
            pltpu.VMEM((n_ref, 6 * n_feat), jnp.bfloat16),
        ],
        compiler_params=pltpu.CompilerParams(dimension_semantics=("arbitrary",)),
    )(queries, inv, local_ids, references)


def local_backward(expd_low, scale, query_aug):
    n_ref, n_query = expd_low.shape
    width = query_aug.shape[1]
    tile = min(TILE, n_query)
    return pl.pallas_call(
        backward_kernel,
        grid=(n_query // tile,),
        in_specs=[
            pl.BlockSpec((n_ref, tile), lambda i: (0, i)),
            pl.BlockSpec((1, tile), lambda i: (0, i)),
            pl.BlockSpec((tile, width), lambda i: (i, 0)),
        ],
        out_specs=pl.BlockSpec((n_ref, width), lambda i: (0, 0)),
        out_shape=jax.ShapeDtypeStruct((n_ref, width), jnp.float32),
        compiler_params=pltpu.CompilerParams(dimension_semantics=("arbitrary",)),
    )(expd_low, scale, query_aug)


def bit_reversed(n):
    bits = n.bit_length() - 1
    return np.array([int(format(p, f"0{bits}b")[::-1], 2) if bits else 0 for p in range(n)], np.int32)


def exchange(x, n_dev, step):
    return lax.ppermute(x, "ref", [(i, i ^ step) for i in range(n_dev)])


def butterfly_stats(peak, total, n_dev):
    step = 1
    while step < n_dev:
        other = exchange(jnp.stack([peak, total]), n_dev, step)
        other_peak, other_total = other[0], other[1]
        new_peak = jnp.maximum(peak, other_peak)
        total = total * jnp.exp(peak - new_peak) + other_total * jnp.exp(other_peak - new_peak)
        peak = new_peak
        step *= 2
    return peak, total


def halving_scatter(rows, extra, n_dev):
    me = lax.axis_index("ref")
    n_feat = rows.shape[-1]
    blocks = rows.reshape(n_dev, -1, n_feat)
    step = 1
    while step < n_dev:
        half = blocks.shape[0] // 2
        bit = (me // step) % 2
        keep = lax.dynamic_slice_in_dim(blocks, bit * half, half, 0)
        send = lax.dynamic_slice_in_dim(blocks, (1 - bit) * half, half, 0)
        n_send = send.shape[0] * send.shape[1]
        got = exchange(jnp.concatenate([send.reshape(n_send, n_feat), extra]), n_dev, step)
        blocks = keep + got[:n_send].reshape(keep.shape)
        extra = extra + got[n_send:]
        step *= 2
    return blocks.reshape(-1, n_feat), extra


def on_device(queries, references, query_ids, spread, cotangent):
    n_query = queries.shape[0]
    n_feat = queries.shape[1]
    n_ref = references.shape[0]
    n_dev = lax.axis_size("ref")
    own_rows = n_query // n_dev
    order = bit_reversed(n_dev)
    reorder = lambda x: x.reshape((n_dev, own_rows) + x.shape[1:])[order].reshape(x.shape)
    all_queries, all_cotangent = queries, cotangent
    queries, query_ids, cotangent = reorder(queries), reorder(query_ids), reorder(cotangent)
    inv = 1.0 / (spread * spread)
    ref_start = lax.axis_index("ref") * n_ref
    local_ids = (query_ids - ref_start)[None, :]
    expd_low, unscaled_t, local_peak, local_total = local_forward(queries, inv[None, :], local_ids, references)
    peak, total = butterfly_stats(local_peak[0], local_total[0], n_dev)
    scale = cotangent * jnp.exp(local_peak[0] - peak) / total
    pulled = (unscaled_t * scale[None, :]).T
    query_low = queries.astype(jnp.bfloat16)
    query_aug = jnp.concatenate(
        [query_low, jnp.ones((n_query, 1), jnp.bfloat16), jnp.zeros((n_query, n_feat - 1), jnp.bfloat16)], axis=1
    )
    pushed_aug = local_backward(expd_low, scale[None, :], query_aug)
    pushed = pushed_aug[:, :n_feat]
    column = pushed_aug[:, n_feat]
    reference_grad = (pushed - references * column[:, None]) * inv
    local_terms = jnp.stack([jnp.sum(queries * pulled, axis=0), jnp.sum(references * reference_grad, axis=0)])
    own_pulled, summed_terms = halving_scatter(pulled, local_terms, n_dev)
    own_start = lax.axis_index("ref") * own_rows
    own_queries = lax.dynamic_slice_in_dim(all_queries, own_start, own_rows, 0)
    own_cot = lax.dynamic_slice_in_dim(all_cotangent, own_start, own_rows, 0)
    query_grad = (own_pulled - own_queries * own_cot[:, None]) * inv
    self_terms = jnp.sum(queries * queries * cotangent[:, None], axis=0)
    summed = (summed_terms[0] - self_terms) * inv + summed_terms[1]
    weight_total = jnp.sum(cotangent)
    spread_grad = -summed / spread - weight_total / spread
    return (query_grad, reference_grad, spread_grad)


def solution(mesh):
    placed = (P("parts", None), P(("parts", "ref"), None), P("parts"), P(), P("parts"))
    return jax.shard_map(
        on_device,
        mesh=mesh,
        in_specs=placed,
        out_specs=(P(("parts", "ref"), None), P(("parts", "ref"), None), P("parts")),
        check_vma=False,
    )
```

```python
import numpy as np
import jax
import jax.numpy as jnp
from jax import lax
from jax.experimental import pallas as pl
from jax.experimental.pallas import tpu as pltpu
from jax.sharding import PartitionSpec as P

TILE = 512


def split3(x):
    x1 = x.astype(jnp.bfloat16)
    rest = x - x1.astype(jnp.float32)
    x2 = rest.astype(jnp.bfloat16)
    x3 = (rest - x2.astype(jnp.float32)).astype(jnp.bfloat16)
    return x1, x2, x3


def forward_kernel(q_ref, inv_ref, lid_ref, r_ref, e_ref, ut_ref, p_ref, t_ref, rn_sc, rlt_sc, rs_sc):
    inv = inv_ref[...]

    @pl.when(pl.program_id(0) == 0)
    def _():
        refs = r_ref[...]
        rn_sc[...] = 0.5 * jnp.sum(refs * refs * inv, axis=1, keepdims=True)
        rlt_sc[...] = refs.T.astype(jnp.bfloat16)
        r1, r2, r3 = split3(refs)
        rs_sc[...] = jnp.concatenate([r1, r1, r1, r2, r2, r3], axis=1)

    q = q_ref[...]
    ones = jnp.ones((8, q.shape[1]), jnp.float32)
    qnorm = lax.dot_general(
        ones, q * q * inv, (((1,), (1,)), ((), ())),
        precision=lax.Precision.HIGHEST, preferred_element_type=jnp.float32,
    )[0:1, :]
    q1, q2, q3 = split3(q * inv)
    cross = lax.dot_general(
        rs_sc[...], jnp.concatenate([q1, q2, q3, q1, q2, q1], axis=1), (((1,), (1,)), ((), ())),
        preferred_element_type=jnp.float32,
    )
    shifted = cross - rn_sc[...]
    row = lax.broadcasted_iota(jnp.int32, shifted.shape, 0)
    shifted = jnp.where(row == lid_ref[...], -jnp.inf, shifted)
    top = jnp.max(shifted, axis=0, keepdims=True)
    expd = jnp.exp(shifted - top)
    p_ref[...] = top - 0.5 * qnorm
    t_ref[...] = jnp.sum(expd, axis=0, keepdims=True)
    expd_low = expd.astype(jnp.bfloat16)
    e_ref[...] = expd_low
    ut_ref[...] = jnp.dot(rlt_sc[...], expd_low, preferred_element_type=jnp.float32)


def backward_kernel(e_ref, sc_ref, qa_ref, ut_ref, q_ref, r_ref, inv_ref, rg_ref, pull_ref, terms_ref, acc_sc, qt_sc):
    step = pl.program_id(0)
    n_feat = q_ref.shape[1]

    @pl.when(step == 0)
    def _():
        acc_sc[...] = jnp.zeros_like(acc_sc)
        qt_sc[...] = jnp.zeros_like(qt_sc)

    scale = sc_ref[...]
    weight = (e_ref[...].astype(jnp.float32) * scale).astype(jnp.bfloat16)
    acc_sc[...] += jnp.dot(weight, qa_ref[...], preferred_element_type=jnp.float32)
    pulled = (ut_ref[...] * scale).T
    pull_ref[...] = pulled
    qt_sc[...] += jnp.sum(q_ref[...] * pulled, axis=0, keepdims=True)

    @pl.when(step == pl.num_programs(0) - 1)
    def _():
        acc = acc_sc[...]
        refs = r_ref[...]
        rgrad = (acc[:, :n_feat] - refs * acc[:, n_feat:n_feat + 1]) * inv_ref[...]
        rg_ref[...] = rgrad
        rterm = jnp.sum(refs * rgrad, axis=0, keepdims=True)
        terms_ref[...] = jnp.concatenate([qt_sc[...], rterm, jnp.zeros((6, n_feat), jnp.float32)], axis=0)


def local_forward(queries, inv, local_ids, references):
    n_query, n_feat = queries.shape
    n_ref = references.shape[0]
    tile = min(TILE, n_query)
    return pl.pallas_call(
        forward_kernel,
        grid=(n_query // tile,),
        in_specs=[
            pl.BlockSpec((tile, n_feat), lambda i: (i, 0)),
            pl.BlockSpec((1, n_feat), lambda i: (0, 0)),
            pl.BlockSpec((1, tile), lambda i: (0, i)),
            pl.BlockSpec((n_ref, n_feat), lambda i: (0, 0)),
        ],
        out_specs=[
            pl.BlockSpec((n_ref, tile), lambda i: (0, i)),
            pl.BlockSpec((n_feat, tile), lambda i: (0, i)),
            pl.BlockSpec((1, tile), lambda i: (0, i)),
            pl.BlockSpec((1, tile), lambda i: (0, i)),
        ],
        out_shape=[
            jax.ShapeDtypeStruct((n_ref, n_query), jnp.bfloat16),
            jax.ShapeDtypeStruct((n_feat, n_query), jnp.float32),
            jax.ShapeDtypeStruct((1, n_query), jnp.float32),
            jax.ShapeDtypeStruct((1, n_query), jnp.float32),
        ],
        scratch_shapes=[
            pltpu.VMEM((n_ref, 1), jnp.float32),
            pltpu.VMEM((n_feat, n_ref), jnp.bfloat16),
            pltpu.VMEM((n_ref, 6 * n_feat), jnp.bfloat16),
        ],
        compiler_params=pltpu.CompilerParams(dimension_semantics=("arbitrary",)),
    )(queries, inv, local_ids, references)


def local_backward(expd_low, scale, query_aug, unscaled_t, queries, references, inv):
    n_ref, n_query = expd_low.shape
    n_feat = queries.shape[1]
    width = query_aug.shape[1]
    tile = min(TILE, n_query)
    whole = lambda i: (0, 0)
    return pl.pallas_call(
        backward_kernel,
        grid=(n_query // tile,),
        in_specs=[
            pl.BlockSpec((n_ref, tile), lambda i: (0, i)),
            pl.BlockSpec((1, tile), lambda i: (0, i)),
            pl.BlockSpec((tile, width), lambda i: (i, 0)),
            pl.BlockSpec((n_feat, tile), lambda i: (0, i)),
            pl.BlockSpec((tile, n_feat), lambda i: (i, 0)),
            pl.BlockSpec((n_ref, n_feat), whole),
            pl.BlockSpec((1, n_feat), whole),
        ],
        out_specs=[
            pl.BlockSpec((n_ref, n_feat), whole),
            pl.BlockSpec((tile, n_feat), lambda i: (i, 0)),
            pl.BlockSpec((8, n_feat), whole),
        ],
        out_shape=[
            jax.ShapeDtypeStruct((n_ref, n_feat), jnp.float32),
            jax.ShapeDtypeStruct((n_query, n_feat), jnp.float32),
            jax.ShapeDtypeStruct((8, n_feat), jnp.float32),
        ],
        scratch_shapes=[
            pltpu.VMEM((n_ref, width), jnp.float32),
            pltpu.VMEM((1, n_feat), jnp.float32),
        ],
        compiler_params=pltpu.CompilerParams(dimension_semantics=("arbitrary",)),
    )(expd_low, scale, query_aug, unscaled_t, queries, references, inv)


def bit_reversed(n):
    bits = n.bit_length() - 1
    return np.array([int(format(p, f"0{bits}b")[::-1], 2) if bits else 0 for p in range(n)], np.int32)


def exchange(x, n_dev, step):
    return lax.ppermute(x, "ref", [(i, i ^ step) for i in range(n_dev)])


def butterfly_stats(peak, total, n_dev):
    step = 1
    while step < n_dev:
        other = exchange(jnp.stack([peak, total]), n_dev, step)
        other_peak, other_total = other[0], other[1]
        new_peak = jnp.maximum(peak, other_peak)
        total = total * jnp.exp(peak - new_peak) + other_total * jnp.exp(other_peak - new_peak)
        peak = new_peak
        step *= 2
    return peak, total


def halving_scatter(rows, extra, n_dev):
    me = lax.axis_index("ref")
    n_feat = rows.shape[-1]
    blocks = rows.reshape(n_dev, -1, n_feat)
    step = 1
    while step < n_dev:
        half = blocks.shape[0] // 2
        bit = (me // step) % 2
        keep = lax.dynamic_slice_in_dim(blocks, bit * half, half, 0)
        send = lax.dynamic_slice_in_dim(blocks, (1 - bit) * half, half, 0)
        n_send = send.shape[0] * send.shape[1]
        got = exchange(jnp.concatenate([send.reshape(n_send, n_feat), extra]), n_dev, step)
        blocks = keep + got[:n_send].reshape(keep.shape)
        extra = extra + got[n_send:]
        step *= 2
    return blocks.reshape(-1, n_feat), extra


def on_device(queries, references, query_ids, spread, cotangent):
    n_query = queries.shape[0]
    n_feat = queries.shape[1]
    n_ref = references.shape[0]
    n_dev = lax.axis_size("ref")
    own_rows = n_query // n_dev
    order = bit_reversed(n_dev)
    reorder = lambda x: x.reshape((n_dev, own_rows) + x.shape[1:])[order].reshape(x.shape)
    all_queries, all_cotangent = queries, cotangent
    queries, query_ids, cotangent = reorder(queries), reorder(query_ids), reorder(cotangent)
    inv = 1.0 / (spread * spread)
    ref_start = lax.axis_index("ref") * n_ref
    local_ids = (query_ids - ref_start)[None, :]
    expd_low, unscaled_t, local_peak, local_total = local_forward(queries, inv[None, :], local_ids, references)
    peak, total = butterfly_stats(local_peak[0], local_total[0], n_dev)
    scale = cotangent * jnp.exp(local_peak[0] - peak) / total
    query_low = queries.astype(jnp.bfloat16)
    query_aug = jnp.concatenate(
        [query_low, jnp.ones((n_query, 1), jnp.bfloat16), jnp.zeros((n_query, n_feat - 1), jnp.bfloat16)], axis=1
    )
    reference_grad, pulled, local_terms = local_backward(
        expd_low, scale[None, :], query_aug, unscaled_t, queries, references, inv[None, :]
    )
    own_pulled, summed_terms = halving_scatter(pulled, local_terms, n_dev)
    own_start = lax.axis_index("ref") * own_rows
    own_queries = lax.dynamic_slice_in_dim(all_queries, own_start, own_rows, 0)
    own_cot = lax.dynamic_slice_in_dim(all_cotangent, own_start, own_rows, 0)
    query_grad = (own_pulled - own_queries * own_cot[:, None]) * inv
    self_terms = jnp.sum(queries * queries * cotangent[:, None], axis=0)
    summed = (summed_terms[0] - self_terms) * inv + summed_terms[1]
    weight_total = jnp.sum(cotangent)
    spread_grad = -summed / spread - weight_total / spread
    return (query_grad, reference_grad, spread_grad)


def solution(mesh):
    placed = (P("parts", None), P(("parts", "ref"), None), P("parts"), P(), P("parts"))
    return jax.shard_map(
        on_device,
        mesh=mesh,
        in_specs=placed,
        out_specs=(P(("parts", "ref"), None), P(("parts", "ref"), None), P("parts")),
        check_vma=False,
    )
```

```python
import functools

import numpy as np
import jax
import jax.numpy as jnp
from jax import lax
from jax.experimental import pallas as pl
from jax.experimental.pallas import tpu as pltpu
from jax.sharding import PartitionSpec as P

TILE = 512


def split3(x):
    x1 = x.astype(jnp.bfloat16)
    rest = x - x1.astype(jnp.float32)
    x2 = rest.astype(jnp.bfloat16)
    x3 = (rest - x2.astype(jnp.float32)).astype(jnp.bfloat16)
    return x1, x2, x3


def forward_kernel(q_ref, inv_ref, lid_ref, r_ref, e_ref, ut_ref, p_ref, t_ref, rn_sc, rlt_sc, rs_sc):
    inv = inv_ref[...]

    @pl.when(pl.program_id(0) == 0)
    def _():
        refs = r_ref[...]
        rn_sc[...] = 0.5 * jnp.sum(refs * refs * inv, axis=1, keepdims=True)
        rlt_sc[...] = refs.T.astype(jnp.bfloat16)
        r1, r2, r3 = split3(refs)
        rs_sc[...] = jnp.concatenate([r1, r1, r1, r2, r2, r3], axis=1)

    q = q_ref[...]
    ones = jnp.ones((8, q.shape[1]), jnp.float32)
    qnorm = lax.dot_general(
        ones, q * q * inv, (((1,), (1,)), ((), ())),
        precision=lax.Precision.HIGHEST, preferred_element_type=jnp.float32,
    )[0:1, :]
    q1, q2, q3 = split3(q * inv)
    cross = lax.dot_general(
        rs_sc[...], jnp.concatenate([q1, q2, q3, q1, q2, q1], axis=1), (((1,), (1,)), ((), ())),
        preferred_element_type=jnp.float32,
    )
    shifted = cross - rn_sc[...]
    row = lax.broadcasted_iota(jnp.int32, shifted.shape, 0)
    shifted = jnp.where(row == lid_ref[...], -jnp.inf, shifted)
    top = jnp.max(shifted, axis=0, keepdims=True)
    expd = jnp.exp(shifted - top)
    p_ref[...] = top - 0.5 * qnorm
    t_ref[...] = jnp.sum(expd, axis=0, keepdims=True)
    expd_low = expd.astype(jnp.bfloat16)
    e_ref[...] = expd_low
    ut_ref[...] = jnp.dot(rlt_sc[...], expd_low, preferred_element_type=jnp.float32)


def backward_kernel(final, e_ref, sc_ref, qa_ref, ut_ref, q_ref, r_ref, inv_ref, acc_ref, qt_ref, *rest):
    if final:
        rg_ref, pull_ref, terms_ref, acc_sc, qt_sc = rest
    else:
        pull_ref, acc_out, qt_out, acc_sc, qt_sc = rest
    step = pl.program_id(0)
    n_feat = q_ref.shape[1]

    @pl.when(step == 0)
    def _():
        acc_sc[...] = acc_ref[...]
        qt_sc[...] = qt_ref[...]

    scale = sc_ref[...]
    weight = (e_ref[...].astype(jnp.float32) * scale).astype(jnp.bfloat16)
    acc_sc[...] += jnp.dot(weight, qa_ref[...], preferred_element_type=jnp.float32)
    pulled = (ut_ref[...] * scale).T
    pull_ref[...] = pulled
    qt_sc[...] += jnp.sum(q_ref[...] * pulled, axis=0, keepdims=True)

    @pl.when(step == pl.num_programs(0) - 1)
    def _():
        if final:
            acc = acc_sc[...]
            refs = r_ref[...]
            rgrad = (acc[:, :n_feat] - refs * acc[:, n_feat:n_feat + 1]) * inv_ref[...]
            rg_ref[...] = rgrad
            rterm = jnp.sum(refs * rgrad, axis=0, keepdims=True)
            terms_ref[...] = jnp.concatenate([qt_sc[...], rterm, jnp.zeros((6, n_feat), jnp.float32)], axis=0)
        else:
            acc_out[...] = acc_sc[...]
            qt_out[...] = qt_sc[...]


def local_forward(queries, inv, local_ids, references):
    n_query, n_feat = queries.shape
    n_ref = references.shape[0]
    tile = min(TILE, n_query)
    return pl.pallas_call(
        forward_kernel,
        grid=(n_query // tile,),
        in_specs=[
            pl.BlockSpec((tile, n_feat), lambda i: (i, 0)),
            pl.BlockSpec((1, n_feat), lambda i: (0, 0)),
            pl.BlockSpec((1, tile), lambda i: (0, i)),
            pl.BlockSpec((n_ref, n_feat), lambda i: (0, 0)),
        ],
        out_specs=[
            pl.BlockSpec((n_ref, tile), lambda i: (0, i)),
            pl.BlockSpec((n_feat, tile), lambda i: (0, i)),
            pl.BlockSpec((1, tile), lambda i: (0, i)),
            pl.BlockSpec((1, tile), lambda i: (0, i)),
        ],
        out_shape=[
            jax.ShapeDtypeStruct((n_ref, n_query), jnp.bfloat16),
            jax.ShapeDtypeStruct((n_feat, n_query), jnp.float32),
            jax.ShapeDtypeStruct((1, n_query), jnp.float32),
            jax.ShapeDtypeStruct((1, n_query), jnp.float32),
        ],
        scratch_shapes=[
            pltpu.VMEM((n_ref, 1), jnp.float32),
            pltpu.VMEM((n_feat, n_ref), jnp.bfloat16),
            pltpu.VMEM((n_ref, 6 * n_feat), jnp.bfloat16),
        ],
        compiler_params=pltpu.CompilerParams(dimension_semantics=("arbitrary",)),
    )(queries, inv, local_ids, references)


def local_backward(final, expd_low, scale, query_aug, unscaled_t, queries, references, inv, acc, qterm):
    n_ref, n_query = expd_low.shape
    n_feat = queries.shape[1]
    width = query_aug.shape[1]
    tile = min(TILE, n_query)
    whole = lambda i: (0, 0)
    if final:
        out_specs = [pl.BlockSpec((n_ref, n_feat), whole), pl.BlockSpec((tile, n_feat), lambda i: (i, 0)),
                     pl.BlockSpec((8, n_feat), whole)]
        out_shape = [jax.ShapeDtypeStruct((n_ref, n_feat), jnp.float32),
                     jax.ShapeDtypeStruct((n_query, n_feat), jnp.float32),
                     jax.ShapeDtypeStruct((8, n_feat), jnp.float32)]
    else:
        out_specs = [pl.BlockSpec((tile, n_feat), lambda i: (i, 0)), pl.BlockSpec((n_ref, width), whole),
                     pl.BlockSpec((1, n_feat), whole)]
        out_shape = [jax.ShapeDtypeStruct((n_query, n_feat), jnp.float32),
                     jax.ShapeDtypeStruct((n_ref, width), jnp.float32),
                     jax.ShapeDtypeStruct((1, n_feat), jnp.float32)]
    return pl.pallas_call(
        functools.partial(backward_kernel, final),
        grid=(n_query // tile,),
        in_specs=[
            pl.BlockSpec((n_ref, tile), lambda i: (0, i)),
            pl.BlockSpec((1, tile), lambda i: (0, i)),
            pl.BlockSpec((tile, width), lambda i: (i, 0)),
            pl.BlockSpec((n_feat, tile), lambda i: (0, i)),
            pl.BlockSpec((tile, n_feat), lambda i: (i, 0)),
            pl.BlockSpec((n_ref, n_feat), whole),
            pl.BlockSpec((1, n_feat), whole),
            pl.BlockSpec((n_ref, width), whole),
            pl.BlockSpec((1, n_feat), whole),
        ],
        out_specs=out_specs,
        out_shape=out_shape,
        scratch_shapes=[
            pltpu.VMEM((n_ref, width), jnp.float32),
            pltpu.VMEM((1, n_feat), jnp.float32),
        ],
        compiler_params=pltpu.CompilerParams(dimension_semantics=("arbitrary",)),
    )(expd_low, scale, query_aug, unscaled_t, queries, references, inv, acc, qterm)


def bit_reversed(n):
    bits = n.bit_length() - 1
    return np.array([int(format(p, f"0{bits}b")[::-1], 2) if bits else 0 for p in range(n)], np.int32)


def exchange(x, n_dev, step):
    return lax.ppermute(x, "ref", [(i, i ^ step) for i in range(n_dev)])


def butterfly_stats(peak, total, n_dev):
    step = 1
    while step < n_dev:
        other = exchange(jnp.stack([peak, total]), n_dev, step)
        other_peak, other_total = other[0], other[1]
        new_peak = jnp.maximum(peak, other_peak)
        total = total * jnp.exp(peak - new_peak) + other_total * jnp.exp(other_peak - new_peak)
        peak = new_peak
        step *= 2
    return peak, total


def halving_scatter(rows, extra, n_dev):
    me = lax.axis_index("ref")
    n_feat = rows.shape[-1]
    blocks = rows.reshape(n_dev, -1, n_feat)
    step = 1
    while step < n_dev:
        half = blocks.shape[0] // 2
        bit = (me // step) % 2
        keep = lax.dynamic_slice_in_dim(blocks, bit * half, half, 0)
        send = lax.dynamic_slice_in_dim(blocks, (1 - bit) * half, half, 0)
        n_send = send.shape[0] * send.shape[1]
        got = exchange(jnp.concatenate([send.reshape(n_send, n_feat), extra]), n_dev, step)
        blocks = keep + got[:n_send].reshape(keep.shape)
        extra = extra + got[n_send:]
        step *= 2
    return blocks.reshape(-1, n_feat), extra


def on_device(queries, references, query_ids, spread, cotangent):
    n_query = queries.shape[0]
    n_feat = queries.shape[1]
    n_ref = references.shape[0]
    n_dev = lax.axis_size("ref")
    own_rows = n_query // n_dev
    order = bit_reversed(n_dev)
    reorder = lambda x: x.reshape((n_dev, own_rows) + x.shape[1:])[order].reshape(x.shape)
    all_queries, all_cotangent = queries, cotangent
    queries, query_ids, cotangent = reorder(queries), reorder(query_ids), reorder(cotangent)
    inv = 1.0 / (spread * spread)
    ref_start = lax.axis_index("ref") * n_ref
    local_ids = (query_ids - ref_start)[None, :]
    query_low = queries.astype(jnp.bfloat16)
    query_aug = jnp.concatenate(
        [query_low, jnp.ones((n_query, 1), jnp.bfloat16), jnp.zeros((n_query, n_feat - 1), jnp.bfloat16)], axis=1
    )
    n_half = 2 if n_query % (2 * TILE) == 0 else 1
    rows = n_query // n_half
    halves = [slice(h * rows, (h + 1) * rows) for h in range(n_half)]
    forwards = [local_forward(queries[part], inv[None, :], local_ids[:, part], references) for part in halves]
    acc = jnp.zeros((n_ref, query_aug.shape[1]), jnp.float32)
    qterm = jnp.zeros((1, n_feat), jnp.float32)
    pulled_parts = []
    for h, part in enumerate(halves):
        expd_low, unscaled_t, local_peak, local_total = forwards[h]
        peak, total = butterfly_stats(local_peak[0], local_total[0], n_dev)
        scale = cotangent[part] * jnp.exp(local_peak[0] - peak) / total
        outs = local_backward(
            h == n_half - 1, expd_low, scale[None, :], query_aug[part], unscaled_t, queries[part],
            references, inv[None, :], acc, qterm,
        )
        if h == n_half - 1:
            reference_grad, pulled_part, local_terms = outs
        else:
            pulled_part, acc, qterm = outs
        pulled_parts.append(pulled_part)
    pulled = jnp.concatenate(pulled_parts, axis=0)
    own_pulled, summed_terms = halving_scatter(pulled, local_terms, n_dev)
    own_start = lax.axis_index("ref") * own_rows
    own_queries = lax.dynamic_slice_in_dim(all_queries, own_start, own_rows, 0)
    own_cot = lax.dynamic_slice_in_dim(all_cotangent, own_start, own_rows, 0)
    query_grad = (own_pulled - own_queries * own_cot[:, None]) * inv
    self_terms = jnp.sum(queries * queries * cotangent[:, None], axis=0)
    summed = (summed_terms[0] - self_terms) * inv + summed_terms[1]
    weight_total = jnp.sum(cotangent)
    spread_grad = -summed / spread - weight_total / spread
    return (query_grad, reference_grad, spread_grad)


def solution(mesh):
    placed = (P("parts", None), P(("parts", "ref"), None), P("parts"), P(), P("parts"))
    return jax.shard_map(
        on_device,
        mesh=mesh,
        in_specs=placed,
        out_specs=(P(("parts", "ref"), None), P(("parts", "ref"), None), P("parts")),
        check_vma=False,
    )
```

```python
import numpy as np
import jax
import jax.numpy as jnp
from jax import lax
from jax.experimental import pallas as pl
from jax.experimental.pallas import tpu as pltpu
from jax.sharding import PartitionSpec as P

TILE = 512


def split3(x):
    x1 = x.astype(jnp.bfloat16)
    rest = x - x1.astype(jnp.float32)
    x2 = rest.astype(jnp.bfloat16)
    x3 = (rest - x2.astype(jnp.float32)).astype(jnp.bfloat16)
    return x1, x2, x3


def forward_kernel(q_ref, inv_ref, lid_ref, r_ref, e_ref, ut_ref, p_ref, t_ref, rn_sc, rlt_sc, rs_sc):
    inv = inv_ref[...]

    @pl.when(pl.program_id(0) == 0)
    def _():
        refs = r_ref[...]
        rn_sc[...] = 0.5 * jnp.sum(refs * refs * inv, axis=1, keepdims=True)
        rlt_sc[...] = refs.T.astype(jnp.bfloat16)
        r1, r2, r3 = split3(refs)
        rs_sc[...] = jnp.concatenate([r1, r1, r1, r2, r2, r3], axis=1)

    q = q_ref[...]
    ones = jnp.ones((8, q.shape[1]), jnp.float32)
    qnorm = lax.dot_general(
        ones, q * q * inv, (((1,), (1,)), ((), ())),
        precision=lax.Precision.HIGHEST, preferred_element_type=jnp.float32,
    )[0:1, :]
    q1, q2, q3 = split3(q * inv)
    cross = lax.dot_general(
        rs_sc[...], jnp.concatenate([q1, q2, q3, q1, q2, q1], axis=1), (((1,), (1,)), ((), ())),
        preferred_element_type=jnp.float32,
    )
    shifted = cross - rn_sc[...]
    row = lax.broadcasted_iota(jnp.int32, shifted.shape, 0)
    shifted = jnp.where(row == lid_ref[...], -jnp.inf, shifted)
    top = jnp.max(shifted, axis=0, keepdims=True)
    expd = jnp.exp(shifted - top)
    p_ref[...] = top - 0.5 * qnorm
    t_ref[...] = jnp.sum(expd, axis=0, keepdims=True)
    expd_low = expd.astype(jnp.bfloat16)
    e_ref[...] = expd_low
    ut_ref[...] = jnp.dot(rlt_sc[...], expd_low, preferred_element_type=jnp.float32)


def backward_kernel(e_ref, sc_ref, qa_ref, ut_ref, q_ref, r_ref, inv_ref, rg_ref, pull_ref, terms_ref, acc_sc, qt_sc):
    step = pl.program_id(0)
    n_feat = q_ref.shape[1]

    @pl.when(step == 0)
    def _():
        acc_sc[...] = jnp.zeros_like(acc_sc)
        qt_sc[...] = jnp.zeros_like(qt_sc)

    scale = sc_ref[...]
    acc_sc[...] += jnp.dot(e_ref[...], qa_ref[...], preferred_element_type=jnp.float32)
    pulled = (ut_ref[...] * scale).T
    pull_ref[...] = pulled
    qt_sc[...] += jnp.sum(q_ref[...] * pulled, axis=0, keepdims=True)

    @pl.when(step == pl.num_programs(0) - 1)
    def _():
        acc = acc_sc[...]
        refs = r_ref[...]
        column = acc[:, n_feat:n_feat + 1] + acc[:, n_feat + 1:n_feat + 2]
        rgrad = (acc[:, :n_feat] - refs * column) * inv_ref[...]
        rg_ref[...] = rgrad
        rterm = jnp.sum(refs * rgrad, axis=0, keepdims=True)
        terms_ref[...] = jnp.concatenate([qt_sc[...], rterm, jnp.zeros((6, n_feat), jnp.float32)], axis=0)


def local_forward(queries, inv, local_ids, references):
    n_query, n_feat = queries.shape
    n_ref = references.shape[0]
    tile = min(TILE, n_query)
    return pl.pallas_call(
        forward_kernel,
        grid=(n_query // tile,),
        in_specs=[
            pl.BlockSpec((tile, n_feat), lambda i: (i, 0)),
            pl.BlockSpec((1, n_feat), lambda i: (0, 0)),
            pl.BlockSpec((1, tile), lambda i: (0, i)),
            pl.BlockSpec((n_ref, n_feat), lambda i: (0, 0)),
        ],
        out_specs=[
            pl.BlockSpec((n_ref, tile), lambda i: (0, i)),
            pl.BlockSpec((n_feat, tile), lambda i: (0, i)),
            pl.BlockSpec((1, tile), lambda i: (0, i)),
            pl.BlockSpec((1, tile), lambda i: (0, i)),
        ],
        out_shape=[
            jax.ShapeDtypeStruct((n_ref, n_query), jnp.bfloat16),
            jax.ShapeDtypeStruct((n_feat, n_query), jnp.float32),
            jax.ShapeDtypeStruct((1, n_query), jnp.float32),
            jax.ShapeDtypeStruct((1, n_query), jnp.float32),
        ],
        scratch_shapes=[
            pltpu.VMEM((n_ref, 1), jnp.float32),
            pltpu.VMEM((n_feat, n_ref), jnp.bfloat16),
            pltpu.VMEM((n_ref, 6 * n_feat), jnp.bfloat16),
        ],
        compiler_params=pltpu.CompilerParams(dimension_semantics=("arbitrary",)),
    )(queries, inv, local_ids, references)


def local_backward(expd_low, scale, query_aug, unscaled_t, queries, references, inv):
    n_ref, n_query = expd_low.shape
    n_feat = queries.shape[1]
    width = query_aug.shape[1]
    tile = min(TILE, n_query)
    whole = lambda i: (0, 0)
    return pl.pallas_call(
        backward_kernel,
        grid=(n_query // tile,),
        in_specs=[
            pl.BlockSpec((n_ref, tile), lambda i: (0, i)),
            pl.BlockSpec((1, tile), lambda i: (0, i)),
            pl.BlockSpec((tile, width), lambda i: (i, 0)),
            pl.BlockSpec((n_feat, tile), lambda i: (0, i)),
            pl.BlockSpec((tile, n_feat), lambda i: (i, 0)),
            pl.BlockSpec((n_ref, n_feat), whole),
            pl.BlockSpec((1, n_feat), whole),
        ],
        out_specs=[
            pl.BlockSpec((n_ref, n_feat), whole),
            pl.BlockSpec((tile, n_feat), lambda i: (i, 0)),
            pl.BlockSpec((8, n_feat), whole),
        ],
        out_shape=[
            jax.ShapeDtypeStruct((n_ref, n_feat), jnp.float32),
            jax.ShapeDtypeStruct((n_query, n_feat), jnp.float32),
            jax.ShapeDtypeStruct((8, n_feat), jnp.float32),
        ],
        scratch_shapes=[
            pltpu.VMEM((n_ref, width), jnp.float32),
            pltpu.VMEM((1, n_feat), jnp.float32),
        ],
        compiler_params=pltpu.CompilerParams(dimension_semantics=("arbitrary",)),
    )(expd_low, scale, query_aug, unscaled_t, queries, references, inv)


def bit_reversed(n):
    bits = n.bit_length() - 1
    return np.array([int(format(p, f"0{bits}b")[::-1], 2) if bits else 0 for p in range(n)], np.int32)


def exchange(x, n_dev, step):
    return lax.ppermute(x, "ref", [(i, i ^ step) for i in range(n_dev)])


def butterfly_stats(peak, total, n_dev):
    step = 1
    while step < n_dev:
        other = exchange(jnp.stack([peak, total]), n_dev, step)
        other_peak, other_total = other[0], other[1]
        new_peak = jnp.maximum(peak, other_peak)
        total = total * jnp.exp(peak - new_peak) + other_total * jnp.exp(other_peak - new_peak)
        peak = new_peak
        step *= 2
    return peak, total


def halving_scatter(rows, extra, n_dev):
    me = lax.axis_index("ref")
    n_feat = rows.shape[-1]
    blocks = rows.reshape(n_dev, -1, n_feat)
    step = 1
    while step < n_dev:
        half = blocks.shape[0] // 2
        bit = (me // step) % 2
        keep = lax.dynamic_slice_in_dim(blocks, bit * half, half, 0)
        send = lax.dynamic_slice_in_dim(blocks, (1 - bit) * half, half, 0)
        n_send = send.shape[0] * send.shape[1]
        got = exchange(jnp.concatenate([send.reshape(n_send, n_feat), extra]), n_dev, step)
        blocks = keep + got[:n_send].reshape(keep.shape)
        extra = extra + got[n_send:]
        step *= 2
    return blocks.reshape(-1, n_feat), extra


def on_device(queries, references, query_ids, spread, cotangent):
    n_query = queries.shape[0]
    n_feat = queries.shape[1]
    n_ref = references.shape[0]
    n_dev = lax.axis_size("ref")
    own_rows = n_query // n_dev
    n_bits = n_dev.bit_length() - 1
    flip = tuple(reversed(range(n_bits)))
    reorder = lambda x: jnp.transpose(
        x.reshape((2,) * n_bits + (own_rows,) + x.shape[1:]), flip + tuple(range(n_bits, x.ndim + n_bits))
    ).reshape(x.shape)
    all_queries, all_cotangent = queries, cotangent
    queries, query_ids, cotangent = reorder(queries), reorder(query_ids), reorder(cotangent)
    inv = 1.0 / (spread * spread)
    ref_start = lax.axis_index("ref") * n_ref
    local_ids = (query_ids - ref_start)[None, :]
    expd_low, unscaled_t, local_peak, local_total = local_forward(queries, inv[None, :], local_ids, references)
    peak, total = butterfly_stats(local_peak[0], local_total[0], n_dev)
    scale = cotangent * jnp.exp(local_peak[0] - peak) / total
    scale_hi = scale.astype(jnp.bfloat16)
    scale_lo = (scale - scale_hi.astype(jnp.float32)).astype(jnp.bfloat16)
    query_aug = jnp.concatenate(
        [(queries * scale[:, None]).astype(jnp.bfloat16), scale_hi[:, None], scale_lo[:, None],
         jnp.zeros((n_query, n_feat - 2), jnp.bfloat16)], axis=1
    )
    reference_grad, pulled, local_terms = local_backward(
        expd_low, scale[None, :], query_aug, unscaled_t, queries, references, inv[None, :]
    )
    own_pulled, summed_terms = halving_scatter(pulled, local_terms, n_dev)
    own_start = lax.axis_index("ref") * own_rows
    own_queries = lax.dynamic_slice_in_dim(all_queries, own_start, own_rows, 0)
    own_cot = lax.dynamic_slice_in_dim(all_cotangent, own_start, own_rows, 0)
    query_grad = (own_pulled - own_queries * own_cot[:, None]) * inv
    self_terms = jnp.sum(queries * queries * cotangent[:, None], axis=0)
    summed = (summed_terms[0] - self_terms) * inv + summed_terms[1]
    weight_total = jnp.sum(cotangent)
    spread_grad = -summed / spread - weight_total / spread
    return (query_grad, reference_grad, spread_grad)


def solution(mesh):
    placed = (P("parts", None), P(("parts", "ref"), None), P("parts"), P(), P("parts"))
    return jax.shard_map(
        on_device,
        mesh=mesh,
        in_specs=placed,
        out_specs=(P(("parts", "ref"), None), P(("parts", "ref"), None), P("parts")),
        check_vma=False,
    )
```

```python
import numpy as np
import jax
import jax.numpy as jnp
from jax import lax
from jax.experimental import pallas as pl
from jax.experimental.pallas import tpu as pltpu
from jax.sharding import PartitionSpec as P

TILE = 512


def split3(x):
    x1 = x.astype(jnp.bfloat16)
    rest = x - x1.astype(jnp.float32)
    x2 = rest.astype(jnp.bfloat16)
    x3 = (rest - x2.astype(jnp.float32)).astype(jnp.bfloat16)
    return x1, x2, x3


def forward_kernel(q_ref, inv_ref, lid_ref, r_ref, e_ref, ut_ref, p_ref, t_ref, rn_sc, rlt_sc, rs_sc):
    inv = inv_ref[...]

    @pl.when(pl.program_id(0) == 0)
    def _():
        refs = r_ref[...]
        rn_sc[...] = 0.5 * jnp.sum(refs * refs * inv, axis=1, keepdims=True)
        rlt_sc[...] = refs.T.astype(jnp.bfloat16)
        r1, r2, r3 = split3(refs)
        rs_sc[...] = jnp.concatenate([r1, r1, r1, r2, r2, r3], axis=1)

    q = q_ref[...]
    ones = jnp.ones((8, q.shape[1]), jnp.float32)
    qnorm = lax.dot_general(
        ones, q * q * inv, (((1,), (1,)), ((), ())),
        precision=lax.Precision.HIGHEST, preferred_element_type=jnp.float32,
    )[0:1, :]
    q1, q2, q3 = split3(q * inv)
    cross = lax.dot_general(
        rs_sc[...], jnp.concatenate([q1, q2, q3, q1, q2, q1], axis=1), (((1,), (1,)), ((), ())),
        preferred_element_type=jnp.float32,
    )
    shifted = cross - rn_sc[...]
    row = lax.broadcasted_iota(jnp.int32, shifted.shape, 0)
    shifted = jnp.where(row == lid_ref[...], -jnp.inf, shifted)
    top = jnp.max(shifted, axis=0, keepdims=True)
    expd = jnp.exp(shifted - top)
    p_ref[...] = top - 0.5 * qnorm
    t_ref[...] = jnp.sum(expd, axis=0, keepdims=True)
    expd_low = expd.astype(jnp.bfloat16)
    e_ref[...] = expd_low
    ut_ref[...] = jnp.dot(rlt_sc[...], expd_low, preferred_element_type=jnp.float32)


def backward_kernel(e_ref, sc_ref, qa_ref, ut_ref, q_ref, r_ref, inv_ref, rg_ref, pull_ref, terms_ref, acc_sc, qt_sc,
                    pull_sc):
    step, part = pl.program_id(0), pl.program_id(1)
    n_feat = q_ref.shape[1]
    sub = pull_ref.shape[0]

    @pl.when((step == 0) & (part == 0))
    def _():
        acc_sc[...] = jnp.zeros_like(acc_sc)
        qt_sc[...] = jnp.zeros_like(qt_sc)

    @pl.when(part == 0)
    def _():
        scale = sc_ref[...]
        weight = (e_ref[...].astype(jnp.float32) * scale).astype(jnp.bfloat16)
        acc_sc[...] += jnp.dot(weight, qa_ref[...], preferred_element_type=jnp.float32)
        pulled = (ut_ref[...] * scale).T
        pull_sc[...] = pulled
        qt_sc[...] += jnp.sum(q_ref[...] * pulled, axis=0, keepdims=True)

    pull_ref[...] = pull_sc[pl.ds(pl.multiple_of(part * sub, sub), sub), :]

    @pl.when((step == pl.num_programs(0) - 1) & (part == pl.num_programs(1) - 1))
    def _():
        acc = acc_sc[...]
        refs = r_ref[...]
        rgrad = (acc[:, :n_feat] - refs * acc[:, n_feat:n_feat + 1]) * inv_ref[...]
        rg_ref[...] = rgrad
        rterm = jnp.sum(refs * rgrad, axis=0, keepdims=True)
        terms_ref[...] = jnp.concatenate([qt_sc[...], rterm, jnp.zeros((6, n_feat), jnp.float32)], axis=0)


def local_forward(queries, inv, local_ids, references):
    n_query, n_feat = queries.shape
    n_ref = references.shape[0]
    tile = min(TILE, n_query)
    return pl.pallas_call(
        forward_kernel,
        grid=(n_query // tile,),
        in_specs=[
            pl.BlockSpec((tile, n_feat), lambda i: (i, 0)),
            pl.BlockSpec((1, n_feat), lambda i: (0, 0)),
            pl.BlockSpec((1, tile), lambda i: (0, i)),
            pl.BlockSpec((n_ref, n_feat), lambda i: (0, 0)),
        ],
        out_specs=[
            pl.BlockSpec((n_ref, tile), lambda i: (0, i)),
            pl.BlockSpec((n_feat, tile), lambda i: (0, i)),
            pl.BlockSpec((1, tile), lambda i: (0, i)),
            pl.BlockSpec((1, tile), lambda i: (0, i)),
        ],
        out_shape=[
            jax.ShapeDtypeStruct((n_ref, n_query), jnp.bfloat16),
            jax.ShapeDtypeStruct((n_feat, n_query), jnp.float32),
            jax.ShapeDtypeStruct((1, n_query), jnp.float32),
            jax.ShapeDtypeStruct((1, n_query), jnp.float32),
        ],
        scratch_shapes=[
            pltpu.VMEM((n_ref, 1), jnp.float32),
            pltpu.VMEM((n_feat, n_ref), jnp.bfloat16),
            pltpu.VMEM((n_ref, 6 * n_feat), jnp.bfloat16),
        ],
        compiler_params=pltpu.CompilerParams(dimension_semantics=("arbitrary",)),
    )(queries, inv, local_ids, references)


def bit_reversed_index(p, n_bits):
    out = 0
    for b in range(n_bits):
        out = out + (p // (2 ** b)) % 2 * (2 ** (n_bits - 1 - b))
    return out


def local_backward(expd_low, scale, query_aug, unscaled_t, queries, references, inv, n_dev):
    n_ref, n_query = expd_low.shape
    n_feat = queries.shape[1]
    width = query_aug.shape[1]
    tile = min(TILE, n_query)
    sub = n_query // n_dev
    per = tile // sub
    n_bits = n_dev.bit_length() - 1
    whole = lambda i, j: (0, 0)
    return pl.pallas_call(
        backward_kernel,
        grid=(n_query // tile, per),
        in_specs=[
            pl.BlockSpec((n_ref, tile), lambda i, j: (0, i)),
            pl.BlockSpec((1, tile), lambda i, j: (0, i)),
            pl.BlockSpec((tile, width), lambda i, j: (i, 0)),
            pl.BlockSpec((n_feat, tile), lambda i, j: (0, i)),
            pl.BlockSpec((tile, n_feat), lambda i, j: (i, 0)),
            pl.BlockSpec((n_ref, n_feat), whole),
            pl.BlockSpec((1, n_feat), whole),
        ],
        out_specs=[
            pl.BlockSpec((n_ref, n_feat), whole),
            pl.BlockSpec((sub, n_feat), lambda i, j: (bit_reversed_index(i * per + j, n_bits), 0)),
            pl.BlockSpec((8, n_feat), whole),
        ],
        out_shape=[
            jax.ShapeDtypeStruct((n_ref, n_feat), jnp.float32),
            jax.ShapeDtypeStruct((n_query, n_feat), jnp.float32),
            jax.ShapeDtypeStruct((8, n_feat), jnp.float32),
        ],
        scratch_shapes=[
            pltpu.VMEM((n_ref, width), jnp.float32),
            pltpu.VMEM((1, n_feat), jnp.float32),
            pltpu.VMEM((tile, n_feat), jnp.float32),
        ],
        compiler_params=pltpu.CompilerParams(dimension_semantics=("arbitrary", "arbitrary")),
    )(expd_low, scale, query_aug, unscaled_t, queries, references, inv)


def bit_reversed(n):
    bits = n.bit_length() - 1
    return np.array([int(format(p, f"0{bits}b")[::-1], 2) if bits else 0 for p in range(n)], np.int32)


def exchange(x, n_dev, step):
    return lax.ppermute(x, "ref", [(i, i ^ step) for i in range(n_dev)])


def butterfly_stats(peak, total, n_dev):
    step = 1
    while step < n_dev:
        other = exchange(jnp.stack([peak, total]), n_dev, step)
        other_peak, other_total = other[0], other[1]
        new_peak = jnp.maximum(peak, other_peak)
        total = total * jnp.exp(peak - new_peak) + other_total * jnp.exp(other_peak - new_peak)
        peak = new_peak
        step *= 2
    return peak, total


def halving_scatter(rows, extra, n_dev):
    me = lax.axis_index("ref")
    n_feat = rows.shape[-1]
    blocks = rows.reshape(n_dev, -1, n_feat)
    step = 1
    while step < n_dev:
        half = blocks.shape[0] // 2
        bit = (me // step) % 2
        keep = lax.dynamic_slice_in_dim(blocks, bit * half, half, 0)
        send = lax.dynamic_slice_in_dim(blocks, (1 - bit) * half, half, 0)
        n_send = send.shape[0] * send.shape[1]
        got = exchange(jnp.concatenate([send.reshape(n_send, n_feat), extra]), n_dev, step)
        blocks = keep + got[:n_send].reshape(keep.shape)
        extra = extra + got[n_send:]
        step *= 2
    return blocks.reshape(-1, n_feat), extra


def on_device(queries, references, query_ids, spread, cotangent):
    n_query = queries.shape[0]
    n_feat = queries.shape[1]
    n_ref = references.shape[0]
    n_dev = lax.axis_size("ref")
    own_rows = n_query // n_dev
    inv = 1.0 / (spread * spread)
    ref_start = lax.axis_index("ref") * n_ref
    local_ids = (query_ids - ref_start)[None, :]
    expd_low, unscaled_t, local_peak, local_total = local_forward(queries, inv[None, :], local_ids, references)
    peak, total = butterfly_stats(local_peak[0], local_total[0], n_dev)
    scale = cotangent * jnp.exp(local_peak[0] - peak) / total
    query_low = queries.astype(jnp.bfloat16)
    query_aug = jnp.concatenate(
        [query_low, jnp.ones((n_query, 1), jnp.bfloat16), jnp.zeros((n_query, n_feat - 1), jnp.bfloat16)], axis=1
    )
    reference_grad, pulled, local_terms = local_backward(
        expd_low, scale[None, :], query_aug, unscaled_t, queries, references, inv[None, :], n_dev
    )
    own_pulled, summed_terms = halving_scatter(pulled, local_terms, n_dev)
    own_start = lax.axis_index("ref") * own_rows
    own_queries = lax.dynamic_slice_in_dim(queries, own_start, own_rows, 0)
    own_cot = lax.dynamic_slice_in_dim(cotangent, own_start, own_rows, 0)
    query_grad = (own_pulled - own_queries * own_cot[:, None]) * inv
    self_terms = jnp.sum(queries * queries * cotangent[:, None], axis=0)
    summed = (summed_terms[0] - self_terms) * inv + summed_terms[1]
    weight_total = jnp.sum(cotangent)
    spread_grad = -summed / spread - weight_total / spread
    return (query_grad, reference_grad, spread_grad)


def solution(mesh):
    placed = (P("parts", None), P(("parts", "ref"), None), P("parts"), P(), P("parts"))
    return jax.shard_map(
        on_device,
        mesh=mesh,
        in_specs=placed,
        out_specs=(P(("parts", "ref"), None), P(("parts", "ref"), None), P("parts")),
        check_vma=False,
    )
```

```python
import functools

import numpy as np
import jax
import jax.numpy as jnp
from jax import lax
from jax.experimental import pallas as pl
from jax.experimental.pallas import tpu as pltpu
from jax.sharding import PartitionSpec as P

TILE = 512


def split3(x):
    x1 = x.astype(jnp.bfloat16)
    rest = x - x1.astype(jnp.float32)
    x2 = rest.astype(jnp.bfloat16)
    x3 = (rest - x2.astype(jnp.float32)).astype(jnp.bfloat16)
    return x1, x2, x3


def forward_kernel(q_ref, inv_ref, lid_ref, r_ref, e_ref, ut_ref, p_ref, t_ref, rn_sc, rlt_sc, rs_sc):
    inv = inv_ref[...]

    @pl.when(pl.program_id(0) == 0)
    def _():
        refs = r_ref[...]
        rn_sc[...] = 0.5 * jnp.sum(refs * refs * inv, axis=1, keepdims=True)
        rlt_sc[...] = refs.T.astype(jnp.bfloat16)
        r1, r2, r3 = split3(refs)
        rs_sc[...] = jnp.concatenate([r1, r1, r1, r2, r2, r3], axis=1)

    q = q_ref[...]
    ones = jnp.ones((8, q.shape[1]), jnp.float32)
    qnorm = lax.dot_general(
        ones, q * q * inv, (((1,), (1,)), ((), ())),
        precision=lax.Precision.HIGHEST, preferred_element_type=jnp.float32,
    )[0:1, :]
    q1, q2, q3 = split3(q * inv)
    cross = lax.dot_general(
        rs_sc[...], jnp.concatenate([q1, q2, q3, q1, q2, q1], axis=1), (((1,), (1,)), ((), ())),
        preferred_element_type=jnp.float32,
    )
    shifted = cross - rn_sc[...]
    row = lax.broadcasted_iota(jnp.int32, shifted.shape, 0)
    shifted = jnp.where(row == lid_ref[...], -jnp.inf, shifted)
    top = jnp.max(shifted, axis=0, keepdims=True)
    expd = jnp.exp(shifted - top)
    p_ref[...] = top - 0.5 * qnorm
    t_ref[...] = jnp.sum(expd, axis=0, keepdims=True)
    expd_low = expd.astype(jnp.bfloat16)
    e_ref[...] = expd_low
    ut_ref[...] = jnp.dot(rlt_sc[...], expd_low, preferred_element_type=jnp.float32)


def backward_kernel(n_bits, e_ref, sc_ref, qa_ref, ut_ref, q_ref, r_ref, inv_ref, rg_ref, pull_hbm, terms_ref,
                    acc_sc, qt_sc, pull_sc, sems):
    step = pl.program_id(0)
    n_feat = q_ref.shape[1]
    tile = pull_sc.shape[0]
    sub = pull_hbm.shape[0] // (2 ** n_bits)
    per = tile // sub

    @pl.when(step == 0)
    def _():
        acc_sc[...] = jnp.zeros_like(acc_sc)
        qt_sc[...] = jnp.zeros_like(qt_sc)

    scale = sc_ref[...]
    pulled = (ut_ref[...] * scale).T
    pull_sc[...] = pulled
    copies = []
    for j in range(per):
        dst = bit_reversed_index(step * per + j, n_bits) * sub
        copy = pltpu.make_async_copy(
            pull_sc.at[pl.ds(j * sub, sub)], pull_hbm.at[pl.ds(pl.multiple_of(dst, sub), sub)], sems.at[j]
        )
        copy.start()
        copies.append(copy)
    weight = (e_ref[...].astype(jnp.float32) * scale).astype(jnp.bfloat16)
    acc_sc[...] += jnp.dot(weight, qa_ref[...], preferred_element_type=jnp.float32)
    qt_sc[...] += jnp.sum(q_ref[...] * pulled, axis=0, keepdims=True)
    for copy in copies:
        copy.wait()

    @pl.when(step == pl.num_programs(0) - 1)
    def _():
        acc = acc_sc[...]
        refs = r_ref[...]
        rgrad = (acc[:, :n_feat] - refs * acc[:, n_feat:n_feat + 1]) * inv_ref[...]
        rg_ref[...] = rgrad
        rterm = jnp.sum(refs * rgrad, axis=0, keepdims=True)
        terms_ref[...] = jnp.concatenate([qt_sc[...], rterm, jnp.zeros((6, n_feat), jnp.float32)], axis=0)


def local_forward(queries, inv, local_ids, references):
    n_query, n_feat = queries.shape
    n_ref = references.shape[0]
    tile = min(TILE, n_query)
    return pl.pallas_call(
        forward_kernel,
        grid=(n_query // tile,),
        in_specs=[
            pl.BlockSpec((tile, n_feat), lambda i: (i, 0)),
            pl.BlockSpec((1, n_feat), lambda i: (0, 0)),
            pl.BlockSpec((1, tile), lambda i: (0, i)),
            pl.BlockSpec((n_ref, n_feat), lambda i: (0, 0)),
        ],
        out_specs=[
            pl.BlockSpec((n_ref, tile), lambda i: (0, i)),
            pl.BlockSpec((n_feat, tile), lambda i: (0, i)),
            pl.BlockSpec((1, tile), lambda i: (0, i)),
            pl.BlockSpec((1, tile), lambda i: (0, i)),
        ],
        out_shape=[
            jax.ShapeDtypeStruct((n_ref, n_query), jnp.bfloat16),
            jax.ShapeDtypeStruct((n_feat, n_query), jnp.float32),
            jax.ShapeDtypeStruct((1, n_query), jnp.float32),
            jax.ShapeDtypeStruct((1, n_query), jnp.float32),
        ],
        scratch_shapes=[
            pltpu.VMEM((n_ref, 1), jnp.float32),
            pltpu.VMEM((n_feat, n_ref), jnp.bfloat16),
            pltpu.VMEM((n_ref, 6 * n_feat), jnp.bfloat16),
        ],
        compiler_params=pltpu.CompilerParams(dimension_semantics=("arbitrary",)),
    )(queries, inv, local_ids, references)


def bit_reversed_index(p, n_bits):
    out = 0
    for b in range(n_bits):
        out = out + (p // (2 ** b)) % 2 * (2 ** (n_bits - 1 - b))
    return out


def local_backward(expd_low, scale, query_aug, unscaled_t, queries, references, inv, n_dev):
    n_ref, n_query = expd_low.shape
    n_feat = queries.shape[1]
    width = query_aug.shape[1]
    tile = min(TILE, n_query)
    sub = n_query // n_dev
    n_bits = n_dev.bit_length() - 1
    whole = lambda i: (0, 0)
    return pl.pallas_call(
        functools.partial(backward_kernel, n_bits),
        grid=(n_query // tile,),
        in_specs=[
            pl.BlockSpec((n_ref, tile), lambda i: (0, i)),
            pl.BlockSpec((1, tile), lambda i: (0, i)),
            pl.BlockSpec((tile, width), lambda i: (i, 0)),
            pl.BlockSpec((n_feat, tile), lambda i: (0, i)),
            pl.BlockSpec((tile, n_feat), lambda i: (i, 0)),
            pl.BlockSpec((n_ref, n_feat), whole),
            pl.BlockSpec((1, n_feat), whole),
        ],
        out_specs=[
            pl.BlockSpec((n_ref, n_feat), whole),
            pl.BlockSpec(memory_space=pl.ANY),
            pl.BlockSpec((8, n_feat), whole),
        ],
        out_shape=[
            jax.ShapeDtypeStruct((n_ref, n_feat), jnp.float32),
            jax.ShapeDtypeStruct((n_query, n_feat), jnp.float32),
            jax.ShapeDtypeStruct((8, n_feat), jnp.float32),
        ],
        scratch_shapes=[
            pltpu.VMEM((n_ref, width), jnp.float32),
            pltpu.VMEM((1, n_feat), jnp.float32),
            pltpu.VMEM((tile, n_feat), jnp.float32),
            pltpu.SemaphoreType.DMA((tile // sub,)),
        ],
        compiler_params=pltpu.CompilerParams(dimension_semantics=("arbitrary",)),
    )(expd_low, scale, query_aug, unscaled_t, queries, references, inv)


def bit_reversed(n):
    bits = n.bit_length() - 1
    return np.array([int(format(p, f"0{bits}b")[::-1], 2) if bits else 0 for p in range(n)], np.int32)


def exchange(x, n_dev, step):
    return lax.ppermute(x, "ref", [(i, i ^ step) for i in range(n_dev)])


def butterfly_stats(peak, total, n_dev):
    step = 1
    while step < n_dev:
        other = exchange(jnp.stack([peak, total]), n_dev, step)
        other_peak, other_total = other[0], other[1]
        new_peak = jnp.maximum(peak, other_peak)
        total = total * jnp.exp(peak - new_peak) + other_total * jnp.exp(other_peak - new_peak)
        peak = new_peak
        step *= 2
    return peak, total


def halving_scatter(rows, extra, n_dev):
    me = lax.axis_index("ref")
    n_feat = rows.shape[-1]
    blocks = rows.reshape(n_dev, -1, n_feat)
    step = 1
    while step < n_dev:
        half = blocks.shape[0] // 2
        bit = (me // step) % 2
        keep = lax.dynamic_slice_in_dim(blocks, bit * half, half, 0)
        send = lax.dynamic_slice_in_dim(blocks, (1 - bit) * half, half, 0)
        n_send = send.shape[0] * send.shape[1]
        got = exchange(jnp.concatenate([send.reshape(n_send, n_feat), extra]), n_dev, step)
        blocks = keep + got[:n_send].reshape(keep.shape)
        extra = extra + got[n_send:]
        step *= 2
    return blocks.reshape(-1, n_feat), extra


def on_device(queries, references, query_ids, spread, cotangent):
    n_query = queries.shape[0]
    n_feat = queries.shape[1]
    n_ref = references.shape[0]
    n_dev = lax.axis_size("ref")
    own_rows = n_query // n_dev
    inv = 1.0 / (spread * spread)
    ref_start = lax.axis_index("ref") * n_ref
    local_ids = (query_ids - ref_start)[None, :]
    expd_low, unscaled_t, local_peak, local_total = local_forward(queries, inv[None, :], local_ids, references)
    peak, total = butterfly_stats(local_peak[0], local_total[0], n_dev)
    scale = cotangent * jnp.exp(local_peak[0] - peak) / total
    query_low = queries.astype(jnp.bfloat16)
    query_aug = jnp.concatenate(
        [query_low, jnp.ones((n_query, 1), jnp.bfloat16), jnp.zeros((n_query, n_feat - 1), jnp.bfloat16)], axis=1
    )
    reference_grad, pulled, local_terms = local_backward(
        expd_low, scale[None, :], query_aug, unscaled_t, queries, references, inv[None, :], n_dev
    )
    own_pulled, summed_terms = halving_scatter(pulled, local_terms, n_dev)
    own_start = lax.axis_index("ref") * own_rows
    own_queries = lax.dynamic_slice_in_dim(queries, own_start, own_rows, 0)
    own_cot = lax.dynamic_slice_in_dim(cotangent, own_start, own_rows, 0)
    query_grad = (own_pulled - own_queries * own_cot[:, None]) * inv
    self_terms = jnp.sum(queries * queries * cotangent[:, None], axis=0)
    summed = (summed_terms[0] - self_terms) * inv + summed_terms[1]
    weight_total = jnp.sum(cotangent)
    spread_grad = -summed / spread - weight_total / spread
    return (query_grad, reference_grad, spread_grad)


def solution(mesh):
    placed = (P("parts", None), P(("parts", "ref"), None), P("parts"), P(), P("parts"))
    return jax.shard_map(
        on_device,
        mesh=mesh,
        in_specs=placed,
        out_specs=(P(("parts", "ref"), None), P(("parts", "ref"), None), P("parts")),
        check_vma=False,
    )
```

```python
import functools

import numpy as np
import jax
import jax.numpy as jnp
from jax import lax
from jax.experimental import pallas as pl
from jax.experimental.pallas import tpu as pltpu
from jax.sharding import PartitionSpec as P

TILE = 512


def split3(x):
    x1 = x.astype(jnp.bfloat16)
    rest = x - x1.astype(jnp.float32)
    x2 = rest.astype(jnp.bfloat16)
    x3 = (rest - x2.astype(jnp.float32)).astype(jnp.bfloat16)
    return x1, x2, x3


def forward_kernel(q_ref, inv_ref, lid_ref, r_ref, e_ref, ut_ref, st_ref, rn_sc, rlt_sc, rs_sc):
    inv = inv_ref[...]

    @pl.when(pl.program_id(0) == 0)
    def _():
        refs = r_ref[...]
        rn_sc[...] = 0.5 * jnp.sum(refs * refs * inv, axis=1, keepdims=True)
        rlt_sc[...] = refs.T.astype(jnp.bfloat16)
        r1, r2, r3 = split3(refs)
        rs_sc[...] = jnp.concatenate([r1, r1, r1, r2, r2, r3], axis=1)

    q = q_ref[...]
    ones = jnp.ones((8, q.shape[1]), jnp.float32)
    qnorm = lax.dot_general(
        ones, q * q * inv, (((1,), (1,)), ((), ())),
        precision=lax.Precision.HIGHEST, preferred_element_type=jnp.float32,
    )[0:1, :]
    q1, q2, q3 = split3(q * inv)
    cross = lax.dot_general(
        rs_sc[...], jnp.concatenate([q1, q2, q3, q1, q2, q1], axis=1), (((1,), (1,)), ((), ())),
        preferred_element_type=jnp.float32,
    )
    shifted = cross - rn_sc[...]
    row = lax.broadcasted_iota(jnp.int32, shifted.shape, 0)
    shifted = jnp.where(row == lid_ref[...], -jnp.inf, shifted)
    top = jnp.max(shifted, axis=0, keepdims=True)
    expd = jnp.exp(shifted - top)
    st_ref[0:1, :] = top - 0.5 * qnorm
    st_ref[1:2, :] = jnp.sum(expd, axis=0, keepdims=True)
    expd_low = expd.astype(jnp.bfloat16)
    e_ref[...] = expd_low
    ut_ref[...] = jnp.dot(rlt_sc[...], expd_low, preferred_element_type=jnp.float32)


def backward_kernel(n_bits, e_ref, sc_ref, ut_ref, q_ref, r_ref, inv_ref, rg_ref, pull_hbm, terms_ref,
                    acc_sc, qt_sc, pull_sc, sems):
    step = pl.program_id(0)
    n_feat = q_ref.shape[1]
    tile = pull_sc.shape[0]
    sub = pull_hbm.shape[0] // (2 ** n_bits)
    per = tile // sub

    @pl.when(step == 0)
    def _():
        acc_sc[...] = jnp.zeros_like(acc_sc)
        qt_sc[...] = jnp.zeros_like(qt_sc)

    scale = sc_ref[...]
    pulled = (ut_ref[...] * scale).T
    pull_sc[...] = pulled
    copies = []
    for j in range(per):
        dst = bit_reversed_index(step * per + j, n_bits) * sub
        copy = pltpu.make_async_copy(
            pull_sc.at[pl.ds(j * sub, sub)], pull_hbm.at[pl.ds(pl.multiple_of(dst, sub), sub)], sems.at[j]
        )
        copy.start()
        copies.append(copy)
    weight = (e_ref[...].astype(jnp.float32) * scale).astype(jnp.bfloat16)
    q = q_ref[...]
    lane = lax.broadcasted_iota(jnp.int32, q.shape, 1)
    query_aug = jnp.concatenate([q.astype(jnp.bfloat16), jnp.where(lane == 0, 1.0, 0.0).astype(jnp.bfloat16)], axis=1)
    acc_sc[...] += jnp.dot(weight, query_aug, preferred_element_type=jnp.float32)
    qt_sc[...] += jnp.sum(q * pulled, axis=0, keepdims=True)
    for copy in copies:
        copy.wait()

    @pl.when(step == pl.num_programs(0) - 1)
    def _():
        acc = acc_sc[...]
        refs = r_ref[...]
        rgrad = (acc[:, :n_feat] - refs * acc[:, n_feat:n_feat + 1]) * inv_ref[...]
        rg_ref[...] = rgrad
        rterm = jnp.sum(refs * rgrad, axis=0, keepdims=True)
        terms_ref[...] = jnp.concatenate([qt_sc[...], rterm, jnp.zeros((6, n_feat), jnp.float32)], axis=0)


def local_forward(queries, inv, local_ids, references):
    n_query, n_feat = queries.shape
    n_ref = references.shape[0]
    tile = min(TILE, n_query)
    return pl.pallas_call(
        forward_kernel,
        grid=(n_query // tile,),
        in_specs=[
            pl.BlockSpec((tile, n_feat), lambda i: (i, 0)),
            pl.BlockSpec((1, n_feat), lambda i: (0, 0)),
            pl.BlockSpec((1, tile), lambda i: (0, i)),
            pl.BlockSpec((n_ref, n_feat), lambda i: (0, 0)),
        ],
        out_specs=[
            pl.BlockSpec((n_ref, tile), lambda i: (0, i)),
            pl.BlockSpec((n_feat, tile), lambda i: (0, i)),
            pl.BlockSpec((2, tile), lambda i: (0, i)),
        ],
        out_shape=[
            jax.ShapeDtypeStruct((n_ref, n_query), jnp.bfloat16),
            jax.ShapeDtypeStruct((n_feat, n_query), jnp.float32),
            jax.ShapeDtypeStruct((2, n_query), jnp.float32),
        ],
        scratch_shapes=[
            pltpu.VMEM((n_ref, 1), jnp.float32),
            pltpu.VMEM((n_feat, n_ref), jnp.bfloat16),
            pltpu.VMEM((n_ref, 6 * n_feat), jnp.bfloat16),
        ],
        compiler_params=pltpu.CompilerParams(dimension_semantics=("arbitrary",)),
    )(queries, inv, local_ids, references)


def bit_reversed_index(p, n_bits):
    out = 0
    for b in range(n_bits):
        out = out + (p // (2 ** b)) % 2 * (2 ** (n_bits - 1 - b))
    return out


def local_backward(expd_low, scale, unscaled_t, queries, references, inv, n_dev):
    n_ref, n_query = expd_low.shape
    n_feat = queries.shape[1]
    width = 2 * queries.shape[1]
    tile = min(TILE, n_query)
    sub = n_query // n_dev
    n_bits = n_dev.bit_length() - 1
    whole = lambda i: (0, 0)
    return pl.pallas_call(
        functools.partial(backward_kernel, n_bits),
        grid=(n_query // tile,),
        in_specs=[
            pl.BlockSpec((n_ref, tile), lambda i: (0, i)),
            pl.BlockSpec((1, tile), lambda i: (0, i)),
            pl.BlockSpec((n_feat, tile), lambda i: (0, i)),
            pl.BlockSpec((tile, n_feat), lambda i: (i, 0)),
            pl.BlockSpec((n_ref, n_feat), whole),
            pl.BlockSpec((1, n_feat), whole),
        ],
        out_specs=[
            pl.BlockSpec((n_ref, n_feat), whole),
            pl.BlockSpec(memory_space=pl.ANY),
            pl.BlockSpec((8, n_feat), whole),
        ],
        out_shape=[
            jax.ShapeDtypeStruct((n_ref, n_feat), jnp.float32),
            jax.ShapeDtypeStruct((n_query, n_feat), jnp.float32),
            jax.ShapeDtypeStruct((8, n_feat), jnp.float32),
        ],
        scratch_shapes=[
            pltpu.VMEM((n_ref, width), jnp.float32),
            pltpu.VMEM((1, n_feat), jnp.float32),
            pltpu.VMEM((tile, n_feat), jnp.float32),
            pltpu.SemaphoreType.DMA((tile // sub,)),
        ],
        compiler_params=pltpu.CompilerParams(dimension_semantics=("arbitrary",)),
    )(expd_low, scale, unscaled_t, queries, references, inv)


def bit_reversed(n):
    bits = n.bit_length() - 1
    return np.array([int(format(p, f"0{bits}b")[::-1], 2) if bits else 0 for p in range(n)], np.int32)


def exchange(x, n_dev, step):
    return lax.ppermute(x, "ref", [(i, i ^ step) for i in range(n_dev)])


def butterfly_stats(stats, n_dev):
    step = 1
    while step < n_dev:
        other = exchange(stats, n_dev, step)
        peak, total, other_peak, other_total = stats[0], stats[1], other[0], other[1]
        new_peak = jnp.maximum(peak, other_peak)
        total = total * jnp.exp(peak - new_peak) + other_total * jnp.exp(other_peak - new_peak)
        stats = jnp.stack([new_peak, total])
        step *= 2
    return stats[0], stats[1]


def halving_scatter(rows, extra, n_dev):
    me = lax.axis_index("ref")
    n_feat = rows.shape[-1]
    blocks = rows.reshape(n_dev, -1, n_feat)
    step = 1
    while step < n_dev:
        half = blocks.shape[0] // 2
        bit = (me // step) % 2
        keep = lax.dynamic_slice_in_dim(blocks, bit * half, half, 0)
        send = lax.dynamic_slice_in_dim(blocks, (1 - bit) * half, half, 0)
        n_send = send.shape[0] * send.shape[1]
        got = exchange(jnp.concatenate([send.reshape(n_send, n_feat), extra]), n_dev, step)
        blocks = keep + got[:n_send].reshape(keep.shape)
        extra = extra + got[n_send:]
        step *= 2
    return blocks.reshape(-1, n_feat), extra


def on_device(queries, references, query_ids, spread, cotangent):
    n_query = queries.shape[0]
    n_feat = queries.shape[1]
    n_ref = references.shape[0]
    n_dev = lax.axis_size("ref")
    own_rows = n_query // n_dev
    inv = 1.0 / (spread * spread)
    ref_start = lax.axis_index("ref") * n_ref
    local_ids = (query_ids - ref_start)[None, :]
    expd_low, unscaled_t, local_stats = local_forward(queries, inv[None, :], local_ids, references)
    peak, total = butterfly_stats(local_stats, n_dev)
    scale = cotangent * jnp.exp(local_stats[0] - peak) / total
    reference_grad, pulled, local_terms = local_backward(
        expd_low, scale[None, :], unscaled_t, queries, references, inv[None, :], n_dev
    )
    own_pulled, summed_terms = halving_scatter(pulled, local_terms, n_dev)
    own_start = lax.axis_index("ref") * own_rows
    own_queries = lax.dynamic_slice_in_dim(queries, own_start, own_rows, 0)
    own_cot = lax.dynamic_slice_in_dim(cotangent, own_start, own_rows, 0)
    query_grad = (own_pulled - own_queries * own_cot[:, None]) * inv
    self_terms = jnp.sum(queries * queries * cotangent[:, None], axis=0)
    summed = (summed_terms[0] - self_terms) * inv + summed_terms[1]
    weight_total = jnp.sum(cotangent)
    spread_grad = -summed / spread - weight_total / spread
    return (query_grad, reference_grad, spread_grad)


def solution(mesh):
    placed = (P("parts", None), P(("parts", "ref"), None), P("parts"), P(), P("parts"))
    return jax.shard_map(
        on_device,
        mesh=mesh,
        in_specs=placed,
        out_specs=(P(("parts", "ref"), None), P(("parts", "ref"), None), P("parts")),
        check_vma=False,
    )
```

```python
import functools

import numpy as np
import jax
import jax.numpy as jnp
from jax import lax
from jax.experimental import pallas as pl
from jax.experimental.pallas import tpu as pltpu
from jax.sharding import PartitionSpec as P

TILE = 512


def split3(x):
    x1 = x.astype(jnp.bfloat16)
    rest = x - x1.astype(jnp.float32)
    x2 = rest.astype(jnp.bfloat16)
    x3 = (rest - x2.astype(jnp.float32)).astype(jnp.bfloat16)
    return x1, x2, x3


def forward_kernel(q_ref, sp_ref, id_ref, r_ref, e_ref, ut_ref, p_ref, t_ref, rn_sc, rlt_sc, rs_sc):
    spread = sp_ref[...]
    inv = 1.0 / (spread * spread)

    @pl.when(pl.program_id(0) == 0)
    def _():
        refs = r_ref[...]
        rn_sc[...] = 0.5 * jnp.sum(refs * refs * inv, axis=1, keepdims=True)
        rlt_sc[...] = refs.T.astype(jnp.bfloat16)
        r1, r2, r3 = split3(refs)
        rs_sc[...] = jnp.concatenate([r1, r1, r1, r2, r2, r3], axis=1)

    q = q_ref[...]
    ones = jnp.ones((8, q.shape[1]), jnp.float32)
    qnorm = lax.dot_general(
        ones, q * q * inv, (((1,), (1,)), ((), ())),
        precision=lax.Precision.HIGHEST, preferred_element_type=jnp.float32,
    )[0:1, :]
    q1, q2, q3 = split3(q * inv)
    cross = lax.dot_general(
        rs_sc[...], jnp.concatenate([q1, q2, q3, q1, q2, q1], axis=1), (((1,), (1,)), ((), ())),
        preferred_element_type=jnp.float32,
    )
    shifted = cross - rn_sc[...]
    row = lax.broadcasted_iota(jnp.int32, shifted.shape, 0)
    local_ids = id_ref[...] - lax.axis_index("ref") * shifted.shape[0]
    shifted = jnp.where(row == local_ids, -jnp.inf, shifted)
    top = jnp.max(shifted, axis=0, keepdims=True)
    expd = jnp.exp(shifted - top)
    p_ref[...] = top - 0.5 * qnorm
    t_ref[...] = jnp.sum(expd, axis=0, keepdims=True)
    expd_low = expd.astype(jnp.bfloat16)
    e_ref[...] = expd_low
    ut_ref[...] = jnp.dot(rlt_sc[...], expd_low, preferred_element_type=jnp.float32)


def backward_kernel(n_bits, e_ref, sc_ref, qa_ref, ut_ref, q_ref, r_ref, inv_ref, rg_ref, pull_hbm, terms_ref,
                    acc_sc, qt_sc, pull_sc, sems):
    step = pl.program_id(0)
    n_feat = q_ref.shape[1]
    tile = pull_sc.shape[0]
    sub = pull_hbm.shape[0] // (2 ** n_bits)
    per = tile // sub

    @pl.when(step == 0)
    def _():
        acc_sc[...] = jnp.zeros_like(acc_sc)
        qt_sc[...] = jnp.zeros_like(qt_sc)

    scale = sc_ref[...]
    pulled = (ut_ref[...] * scale).T
    pull_sc[...] = pulled
    copies = []
    for j in range(per):
        dst = bit_reversed_index(step * per + j, n_bits) * sub
        copy = pltpu.make_async_copy(
            pull_sc.at[pl.ds(j * sub, sub)], pull_hbm.at[pl.ds(pl.multiple_of(dst, sub), sub)], sems.at[j]
        )
        copy.start()
        copies.append(copy)
    weight = (e_ref[...].astype(jnp.float32) * scale).astype(jnp.bfloat16)
    acc_sc[...] += jnp.dot(weight, qa_ref[...], preferred_element_type=jnp.float32)
    qt_sc[...] += jnp.sum(q_ref[...] * pulled, axis=0, keepdims=True)
    for copy in copies:
        copy.wait()

    @pl.when(step == pl.num_programs(0) - 1)
    def _():
        acc = acc_sc[...]
        refs = r_ref[...]
        rgrad = (acc[:, :n_feat] - refs * acc[:, n_feat:n_feat + 1]) * inv_ref[...]
        rg_ref[...] = rgrad
        rterm = jnp.sum(refs * rgrad, axis=0, keepdims=True)
        terms_ref[...] = jnp.concatenate([qt_sc[...], rterm, jnp.zeros((6, n_feat), jnp.float32)], axis=0)


def local_forward(queries, spread, query_ids, references):
    n_query, n_feat = queries.shape
    n_ref = references.shape[0]
    tile = min(TILE, n_query)
    return pl.pallas_call(
        forward_kernel,
        grid=(n_query // tile,),
        in_specs=[
            pl.BlockSpec((tile, n_feat), lambda i: (i, 0)),
            pl.BlockSpec((1, n_feat), lambda i: (0, 0)),
            pl.BlockSpec((1, tile), lambda i: (0, i)),
            pl.BlockSpec((n_ref, n_feat), lambda i: (0, 0)),
        ],
        out_specs=[
            pl.BlockSpec((n_ref, tile), lambda i: (0, i)),
            pl.BlockSpec((n_feat, tile), lambda i: (0, i)),
            pl.BlockSpec((1, tile), lambda i: (0, i)),
            pl.BlockSpec((1, tile), lambda i: (0, i)),
        ],
        out_shape=[
            jax.ShapeDtypeStruct((n_ref, n_query), jnp.bfloat16),
            jax.ShapeDtypeStruct((n_feat, n_query), jnp.float32),
            jax.ShapeDtypeStruct((1, n_query), jnp.float32),
            jax.ShapeDtypeStruct((1, n_query), jnp.float32),
        ],
        scratch_shapes=[
            pltpu.VMEM((n_ref, 1), jnp.float32),
            pltpu.VMEM((n_feat, n_ref), jnp.bfloat16),
            pltpu.VMEM((n_ref, 6 * n_feat), jnp.bfloat16),
        ],
        compiler_params=pltpu.CompilerParams(dimension_semantics=("arbitrary",)),
    )(queries, spread, query_ids, references)


def bit_reversed_index(p, n_bits):
    out = 0
    for b in range(n_bits):
        out = out + (p // (2 ** b)) % 2 * (2 ** (n_bits - 1 - b))
    return out


def local_backward(expd_low, scale, query_aug, unscaled_t, queries, references, inv, n_dev):
    n_ref, n_query = expd_low.shape
    n_feat = queries.shape[1]
    width = query_aug.shape[1]
    tile = min(TILE, n_query)
    sub = n_query // n_dev
    n_bits = n_dev.bit_length() - 1
    whole = lambda i: (0, 0)
    return pl.pallas_call(
        functools.partial(backward_kernel, n_bits),
        grid=(n_query // tile,),
        in_specs=[
            pl.BlockSpec((n_ref, tile), lambda i: (0, i)),
            pl.BlockSpec((1, tile), lambda i: (0, i)),
            pl.BlockSpec((tile, width), lambda i: (i, 0)),
            pl.BlockSpec((n_feat, tile), lambda i: (0, i)),
            pl.BlockSpec((tile, n_feat), lambda i: (i, 0)),
            pl.BlockSpec((n_ref, n_feat), whole),
            pl.BlockSpec((1, n_feat), whole),
        ],
        out_specs=[
            pl.BlockSpec((n_ref, n_feat), whole),
            pl.BlockSpec(memory_space=pl.ANY),
            pl.BlockSpec((8, n_feat), whole),
        ],
        out_shape=[
            jax.ShapeDtypeStruct((n_ref, n_feat), jnp.float32),
            jax.ShapeDtypeStruct((n_query, n_feat), jnp.float32),
            jax.ShapeDtypeStruct((8, n_feat), jnp.float32),
        ],
        scratch_shapes=[
            pltpu.VMEM((n_ref, width), jnp.float32),
            pltpu.VMEM((1, n_feat), jnp.float32),
            pltpu.VMEM((tile, n_feat), jnp.float32),
            pltpu.SemaphoreType.DMA((tile // sub,)),
        ],
        compiler_params=pltpu.CompilerParams(dimension_semantics=("arbitrary",)),
    )(expd_low, scale, query_aug, unscaled_t, queries, references, inv)


def bit_reversed(n):
    bits = n.bit_length() - 1
    return np.array([int(format(p, f"0{bits}b")[::-1], 2) if bits else 0 for p in range(n)], np.int32)


def exchange(x, n_dev, step):
    return lax.ppermute(x, "ref", [(i, i ^ step) for i in range(n_dev)])


def butterfly_stats(peak, total, n_dev):
    step = 1
    while step < n_dev:
        other = exchange(jnp.stack([peak, total]), n_dev, step)
        other_peak, other_total = other[0], other[1]
        new_peak = jnp.maximum(peak, other_peak)
        total = total * jnp.exp(peak - new_peak) + other_total * jnp.exp(other_peak - new_peak)
        peak = new_peak
        step *= 2
    return peak, total


def halving_scatter(rows, extra, n_dev):
    me = lax.axis_index("ref")
    n_feat = rows.shape[-1]
    blocks = rows.reshape(n_dev, -1, n_feat)
    step = 1
    while step < n_dev:
        half = blocks.shape[0] // 2
        bit = (me // step) % 2
        keep = lax.dynamic_slice_in_dim(blocks, bit * half, half, 0)
        send = lax.dynamic_slice_in_dim(blocks, (1 - bit) * half, half, 0)
        n_send = send.shape[0] * send.shape[1]
        got = exchange(jnp.concatenate([send.reshape(n_send, n_feat), extra]), n_dev, step)
        blocks = keep + got[:n_send].reshape(keep.shape)
        extra = extra + got[n_send:]
        step *= 2
    return blocks.reshape(-1, n_feat), extra


def on_device(queries, references, query_ids, spread, cotangent):
    n_query = queries.shape[0]
    n_feat = queries.shape[1]
    n_ref = references.shape[0]
    n_dev = lax.axis_size("ref")
    own_rows = n_query // n_dev
    inv = 1.0 / (spread * spread)
    expd_low, unscaled_t, local_peak, local_total = local_forward(queries, spread[None, :], query_ids[None, :], references)
    peak, total = butterfly_stats(local_peak[0], local_total[0], n_dev)
    scale = cotangent * jnp.exp(local_peak[0] - peak) / total
    query_low = queries.astype(jnp.bfloat16)
    query_aug = jnp.concatenate(
        [query_low, jnp.ones((n_query, 1), jnp.bfloat16), jnp.zeros((n_query, n_feat - 1), jnp.bfloat16)], axis=1
    )
    reference_grad, pulled, local_terms = local_backward(
        expd_low, scale[None, :], query_aug, unscaled_t, queries, references, inv[None, :], n_dev
    )
    own_pulled, summed_terms = halving_scatter(pulled, local_terms, n_dev)
    own_start = lax.axis_index("ref") * own_rows
    own_queries = lax.dynamic_slice_in_dim(queries, own_start, own_rows, 0)
    own_cot = lax.dynamic_slice_in_dim(cotangent, own_start, own_rows, 0)
    query_grad = (own_pulled - own_queries * own_cot[:, None]) * inv
    self_terms = jnp.sum(queries * queries * cotangent[:, None], axis=0)
    summed = (summed_terms[0] - self_terms) * inv + summed_terms[1]
    weight_total = jnp.sum(cotangent)
    spread_grad = -summed / spread - weight_total / spread
    return (query_grad, reference_grad, spread_grad)


def solution(mesh):
    placed = (P("parts", None), P(("parts", "ref"), None), P("parts"), P(), P("parts"))
    return jax.shard_map(
        on_device,
        mesh=mesh,
        in_specs=placed,
        out_specs=(P(("parts", "ref"), None), P(("parts", "ref"), None), P("parts")),
        check_vma=False,
    )
```

```python
import functools

import numpy as np
import jax
import jax.numpy as jnp
from jax import lax
from jax.experimental import pallas as pl
from jax.experimental.pallas import tpu as pltpu
from jax.sharding import PartitionSpec as P

TILE = 512


def split3(x):
    x1 = x.astype(jnp.bfloat16)
    rest = x - x1.astype(jnp.float32)
    x2 = rest.astype(jnp.bfloat16)
    x3 = (rest - x2.astype(jnp.float32)).astype(jnp.bfloat16)
    return x1, x2, x3


def forward_kernel(q_ref, sp_ref, id_ref, r_ref, e_ref, ut_ref, p_ref, t_ref, rn_sc, rlt_sc, rs_sc):
    spread = sp_ref[...]
    inv = 1.0 / (spread * spread)

    @pl.when(pl.program_id(0) == 0)
    def _():
        refs = r_ref[...]
        rn_sc[...] = 0.5 * jnp.sum(refs * refs * inv, axis=1, keepdims=True)
        rlt_sc[...] = refs.T.astype(jnp.bfloat16)
        r1, r2, r3 = split3(refs)
        rs_sc[...] = jnp.concatenate([r1, r1, r1, r2, r2, r3], axis=1)

    q = q_ref[...]
    ones = jnp.ones((8, q.shape[1]), jnp.float32)
    qnorm = lax.dot_general(
        ones, q * q * inv, (((1,), (1,)), ((), ())),
        precision=lax.Precision.HIGHEST, preferred_element_type=jnp.float32,
    )[0:1, :]
    q1, q2, q3 = split3(q * inv)
    cross = lax.dot_general(
        rs_sc[...], jnp.concatenate([q1, q2, q3, q1, q2, q1], axis=1), (((1,), (1,)), ((), ())),
        preferred_element_type=jnp.float32,
    )
    shifted = cross - rn_sc[...]
    row = lax.broadcasted_iota(jnp.int32, shifted.shape, 0)
    local_ids = id_ref[...] - lax.axis_index("ref") * shifted.shape[0]
    shifted = jnp.where(row == local_ids, -jnp.inf, shifted)
    top = jnp.max(shifted, axis=0, keepdims=True)
    expd = jnp.exp(shifted - top)
    p_ref[...] = top - 0.5 * qnorm
    t_ref[...] = jnp.sum(expd, axis=0, keepdims=True)
    expd_low = expd.astype(jnp.bfloat16)
    e_ref[...] = expd_low
    ut_ref[...] = jnp.dot(rlt_sc[...], expd_low, preferred_element_type=jnp.float32)


def backward_kernel(n_bits, e_ref, sc_ref, qa_ref, ut_ref, q_ref, r_ref, inv_ref, rg_ref, pull_hbm,
                    acc_sc, qt_sc, pull_sc, terms_sc, sems, terms_sem):
    step = pl.program_id(0)
    n_feat = q_ref.shape[1]
    tile = pull_sc.shape[0]
    n_rows = pull_hbm.shape[0] - terms_sc.shape[0]
    n_dev = 2 ** n_bits
    sub = n_rows // n_dev
    per = tile // sub
    flip = (lax.axis_index("ref") % 2) * (n_dev // 2)

    @pl.when(step == 0)
    def _():
        acc_sc[...] = jnp.zeros_like(acc_sc)
        qt_sc[...] = jnp.zeros_like(qt_sc)

    scale = sc_ref[...]
    pulled = (ut_ref[...] * scale).T
    pull_sc[...] = pulled
    copies = []
    for j in range(per):
        dst = (bit_reversed_index(step * per + j, n_bits) + flip) % n_dev * sub
        copy = pltpu.make_async_copy(
            pull_sc.at[pl.ds(j * sub, sub)], pull_hbm.at[pl.ds(pl.multiple_of(dst, sub), sub)], sems.at[j]
        )
        copy.start()
        copies.append(copy)
    weight = (e_ref[...].astype(jnp.float32) * scale).astype(jnp.bfloat16)
    acc_sc[...] += jnp.dot(weight, qa_ref[...], preferred_element_type=jnp.float32)
    qt_sc[...] += jnp.sum(q_ref[...] * pulled, axis=0, keepdims=True)
    for copy in copies:
        copy.wait()

    @pl.when(step == pl.num_programs(0) - 1)
    def _():
        acc = acc_sc[...]
        refs = r_ref[...]
        rgrad = (acc[:, :n_feat] - refs * acc[:, n_feat:n_feat + 1]) * inv_ref[...]
        rg_ref[...] = rgrad
        rterm = jnp.sum(refs * rgrad, axis=0, keepdims=True)
        terms_sc[...] = jnp.concatenate([qt_sc[...], rterm, jnp.zeros((6, n_feat), jnp.float32)], axis=0)
        copy = pltpu.make_async_copy(terms_sc, pull_hbm.at[pl.ds(n_rows, terms_sc.shape[0])], terms_sem)
        copy.start()
        copy.wait()


def local_forward(queries, spread, query_ids, references):
    n_query, n_feat = queries.shape
    n_ref = references.shape[0]
    tile = min(TILE, n_query)
    return pl.pallas_call(
        forward_kernel,
        grid=(n_query // tile,),
        in_specs=[
            pl.BlockSpec((tile, n_feat), lambda i: (i, 0)),
            pl.BlockSpec((1, n_feat), lambda i: (0, 0)),
            pl.BlockSpec((1, tile), lambda i: (0, i)),
            pl.BlockSpec((n_ref, n_feat), lambda i: (0, 0)),
        ],
        out_specs=[
            pl.BlockSpec((n_ref, tile), lambda i: (0, i)),
            pl.BlockSpec((n_feat, tile), lambda i: (0, i)),
            pl.BlockSpec((1, tile), lambda i: (0, i)),
            pl.BlockSpec((1, tile), lambda i: (0, i)),
        ],
        out_shape=[
            jax.ShapeDtypeStruct((n_ref, n_query), jnp.bfloat16),
            jax.ShapeDtypeStruct((n_feat, n_query), jnp.float32),
            jax.ShapeDtypeStruct((1, n_query), jnp.float32),
            jax.ShapeDtypeStruct((1, n_query), jnp.float32),
        ],
        scratch_shapes=[
            pltpu.VMEM((n_ref, 1), jnp.float32),
            pltpu.VMEM((n_feat, n_ref), jnp.bfloat16),
            pltpu.VMEM((n_ref, 6 * n_feat), jnp.bfloat16),
        ],
        compiler_params=pltpu.CompilerParams(dimension_semantics=("arbitrary",)),
    )(queries, spread, query_ids, references)


def bit_reversed_index(p, n_bits):
    out = 0
    for b in range(n_bits):
        out = out + (p // (2 ** b)) % 2 * (2 ** (n_bits - 1 - b))
    return out


def local_backward(expd_low, scale, query_aug, unscaled_t, queries, references, inv, n_dev):
    n_ref, n_query = expd_low.shape
    n_feat = queries.shape[1]
    width = query_aug.shape[1]
    tile = min(TILE, n_query)
    sub = n_query // n_dev
    n_bits = n_dev.bit_length() - 1
    whole = lambda i: (0, 0)
    return pl.pallas_call(
        functools.partial(backward_kernel, n_bits),
        grid=(n_query // tile,),
        in_specs=[
            pl.BlockSpec((n_ref, tile), lambda i: (0, i)),
            pl.BlockSpec((1, tile), lambda i: (0, i)),
            pl.BlockSpec((tile, width), lambda i: (i, 0)),
            pl.BlockSpec((n_feat, tile), lambda i: (0, i)),
            pl.BlockSpec((tile, n_feat), lambda i: (i, 0)),
            pl.BlockSpec((n_ref, n_feat), whole),
            pl.BlockSpec((1, n_feat), whole),
        ],
        out_specs=[
            pl.BlockSpec((n_ref, n_feat), whole),
            pl.BlockSpec(memory_space=pl.ANY),
        ],
        out_shape=[
            jax.ShapeDtypeStruct((n_ref, n_feat), jnp.float32),
            jax.ShapeDtypeStruct((n_query + 8, n_feat), jnp.float32),
        ],
        scratch_shapes=[
            pltpu.VMEM((n_ref, width), jnp.float32),
            pltpu.VMEM((1, n_feat), jnp.float32),
            pltpu.VMEM((tile, n_feat), jnp.float32),
            pltpu.VMEM((8, n_feat), jnp.float32),
            pltpu.SemaphoreType.DMA((tile // sub,)),
            pltpu.SemaphoreType.DMA(()),
        ],
        compiler_params=pltpu.CompilerParams(dimension_semantics=("arbitrary",)),
    )(expd_low, scale, query_aug, unscaled_t, queries, references, inv)


def bit_reversed(n):
    bits = n.bit_length() - 1
    return np.array([int(format(p, f"0{bits}b")[::-1], 2) if bits else 0 for p in range(n)], np.int32)


def exchange(x, n_dev, step):
    return lax.ppermute(x, "ref", [(i, i ^ step) for i in range(n_dev)])


def butterfly_stats(peak, total, n_dev):
    step = 1
    while step < n_dev:
        other = exchange(jnp.stack([peak, total]), n_dev, step)
        other_peak, other_total = other[0], other[1]
        new_peak = jnp.maximum(peak, other_peak)
        total = total * jnp.exp(peak - new_peak) + other_total * jnp.exp(other_peak - new_peak)
        peak = new_peak
        step *= 2
    return peak, total


def halving_scatter(packed, n_extra, n_dev):
    me = lax.axis_index("ref")
    n_feat = packed.shape[-1]
    n_rows = packed.shape[0] - n_extra
    half = n_rows // 2
    got = exchange(packed[half:], n_dev, 1)
    blocks = (packed[:half] + got[:half]).reshape(n_dev // 2, -1, n_feat)
    extra = packed[n_rows:] + got[half:]
    step = 2
    while step < n_dev:
        half = blocks.shape[0] // 2
        bit = (me // step) % 2
        keep = lax.dynamic_slice_in_dim(blocks, bit * half, half, 0)
        send = lax.dynamic_slice_in_dim(blocks, (1 - bit) * half, half, 0)
        n_send = send.shape[0] * send.shape[1]
        got = exchange(jnp.concatenate([send.reshape(n_send, n_feat), extra]), n_dev, step)
        blocks = keep + got[:n_send].reshape(keep.shape)
        extra = extra + got[n_send:]
        step *= 2
    return blocks.reshape(-1, n_feat), extra


def on_device(queries, references, query_ids, spread, cotangent):
    n_query = queries.shape[0]
    n_feat = queries.shape[1]
    n_ref = references.shape[0]
    n_dev = lax.axis_size("ref")
    own_rows = n_query // n_dev
    inv = 1.0 / (spread * spread)
    expd_low, unscaled_t, local_peak, local_total = local_forward(queries, spread[None, :], query_ids[None, :], references)
    peak, total = butterfly_stats(local_peak[0], local_total[0], n_dev)
    scale = cotangent * jnp.exp(local_peak[0] - peak) / total
    query_low = queries.astype(jnp.bfloat16)
    query_aug = jnp.concatenate(
        [query_low, jnp.ones((n_query, 1), jnp.bfloat16), jnp.zeros((n_query, n_feat - 1), jnp.bfloat16)], axis=1
    )
    reference_grad, packed = local_backward(
        expd_low, scale[None, :], query_aug, unscaled_t, queries, references, inv[None, :], n_dev
    )
    own_pulled, summed_terms = halving_scatter(packed, 8, n_dev)
    own_start = lax.axis_index("ref") * own_rows
    own_queries = lax.dynamic_slice_in_dim(queries, own_start, own_rows, 0)
    own_cot = lax.dynamic_slice_in_dim(cotangent, own_start, own_rows, 0)
    query_grad = (own_pulled - own_queries * own_cot[:, None]) * inv
    self_terms = jnp.sum(queries * queries * cotangent[:, None], axis=0)
    summed = (summed_terms[0] - self_terms) * inv + summed_terms[1]
    weight_total = jnp.sum(cotangent)
    spread_grad = -summed / spread - weight_total / spread
    return (query_grad, reference_grad, spread_grad)


def solution(mesh):
    placed = (P("parts", None), P(("parts", "ref"), None), P("parts"), P(), P("parts"))
    return jax.shard_map(
        on_device,
        mesh=mesh,
        in_specs=placed,
        out_specs=(P(("parts", "ref"), None), P(("parts", "ref"), None), P("parts")),
        check_vma=False,
    )
```

```python
import functools

import numpy as np
import jax
import jax.numpy as jnp
from jax import lax
from jax.experimental import pallas as pl
from jax.experimental.pallas import tpu as pltpu
from jax.sharding import PartitionSpec as P

TILE = 1024


def split3(x):
    x1 = x.astype(jnp.bfloat16)
    rest = x - x1.astype(jnp.float32)
    x2 = rest.astype(jnp.bfloat16)
    x3 = (rest - x2.astype(jnp.float32)).astype(jnp.bfloat16)
    return x1, x2, x3


def forward_kernel(q_ref, sp_ref, id_ref, r_ref, e_ref, ut_ref, p_ref, t_ref, rn_sc, rlt_sc, rs_sc):
    spread = sp_ref[...]
    inv = 1.0 / (spread * spread)

    @pl.when(pl.program_id(0) == 0)
    def _():
        refs = r_ref[...]
        rn_sc[...] = 0.5 * jnp.sum(refs * refs * inv, axis=1, keepdims=True)
        rlt_sc[...] = refs.T.astype(jnp.bfloat16)
        r1, r2, r3 = split3(refs)
        rs_sc[...] = jnp.concatenate([r1, r1, r1, r2, r2, r3], axis=1)

    q = q_ref[...]
    ones = jnp.ones((8, q.shape[1]), jnp.float32)
    qnorm = lax.dot_general(
        ones, q * q * inv, (((1,), (1,)), ((), ())),
        precision=lax.Precision.HIGHEST, preferred_element_type=jnp.float32,
    )[0:1, :]
    q1, q2, q3 = split3(q * inv)
    cross = lax.dot_general(
        rs_sc[...], jnp.concatenate([q1, q2, q3, q1, q2, q1], axis=1), (((1,), (1,)), ((), ())),
        preferred_element_type=jnp.float32,
    )
    shifted = cross - rn_sc[...]
    row = lax.broadcasted_iota(jnp.int32, shifted.shape, 0)
    local_ids = id_ref[...] - lax.axis_index("ref") * shifted.shape[0]
    shifted = jnp.where(row == local_ids, -jnp.inf, shifted)
    top = jnp.max(shifted, axis=0, keepdims=True)
    expd = jnp.exp(shifted - top)
    p_ref[...] = top - 0.5 * qnorm
    t_ref[...] = jnp.sum(expd, axis=0, keepdims=True)
    expd_low = expd.astype(jnp.bfloat16)
    e_ref[...] = expd_low
    ut_ref[...] = jnp.dot(rlt_sc[...], expd_low, preferred_element_type=jnp.float32)


def backward_kernel(n_bits, e_ref, sc_ref, qa_ref, ut_ref, q_ref, r_ref, inv_ref, rg_ref, pull_hbm, terms_ref,
                    acc_sc, qt_sc, pull_sc, sems):
    step = pl.program_id(0)
    n_feat = q_ref.shape[1]
    tile = pull_sc.shape[0]
    sub = pull_hbm.shape[0] // (2 ** n_bits)
    per = tile // sub

    @pl.when(step == 0)
    def _():
        acc_sc[...] = jnp.zeros_like(acc_sc)
        qt_sc[...] = jnp.zeros_like(qt_sc)

    scale = sc_ref[...]
    pulled = (ut_ref[...] * scale).T
    pull_sc[...] = pulled
    copies = []
    for j in range(per):
        dst = bit_reversed_index(step * per + j, n_bits) * sub
        copy = pltpu.make_async_copy(
            pull_sc.at[pl.ds(j * sub, sub)], pull_hbm.at[pl.ds(pl.multiple_of(dst, sub), sub)], sems.at[j]
        )
        copy.start()
        copies.append(copy)
    weight = (e_ref[...].astype(jnp.float32) * scale).astype(jnp.bfloat16)
    acc_sc[...] += jnp.dot(weight, qa_ref[...], preferred_element_type=jnp.float32)
    qt_sc[...] += jnp.sum(q_ref[...] * pulled, axis=0, keepdims=True)
    for copy in copies:
        copy.wait()

    @pl.when(step == pl.num_programs(0) - 1)
    def _():
        acc = acc_sc[...]
        refs = r_ref[...]
        rgrad = (acc[:, :n_feat] - refs * acc[:, n_feat:n_feat + 1]) * inv_ref[...]
        rg_ref[...] = rgrad
        rterm = jnp.sum(refs * rgrad, axis=0, keepdims=True)
        terms_ref[...] = jnp.concatenate([qt_sc[...], rterm, jnp.zeros((6, n_feat), jnp.float32)], axis=0)


def local_forward(queries, spread, query_ids, references):
    n_query, n_feat = queries.shape
    n_ref = references.shape[0]
    tile = min(TILE, n_query)
    return pl.pallas_call(
        forward_kernel,
        grid=(n_query // tile,),
        in_specs=[
            pl.BlockSpec((tile, n_feat), lambda i: (i, 0)),
            pl.BlockSpec((1, n_feat), lambda i: (0, 0)),
            pl.BlockSpec((1, tile), lambda i: (0, i)),
            pl.BlockSpec((n_ref, n_feat), lambda i: (0, 0)),
        ],
        out_specs=[
            pl.BlockSpec((n_ref, tile), lambda i: (0, i)),
            pl.BlockSpec((n_feat, tile), lambda i: (0, i)),
            pl.BlockSpec((1, tile), lambda i: (0, i)),
            pl.BlockSpec((1, tile), lambda i: (0, i)),
        ],
        out_shape=[
            jax.ShapeDtypeStruct((n_ref, n_query), jnp.bfloat16),
            jax.ShapeDtypeStruct((n_feat, n_query), jnp.float32),
            jax.ShapeDtypeStruct((1, n_query), jnp.float32),
            jax.ShapeDtypeStruct((1, n_query), jnp.float32),
        ],
        scratch_shapes=[
            pltpu.VMEM((n_ref, 1), jnp.float32),
            pltpu.VMEM((n_feat, n_ref), jnp.bfloat16),
            pltpu.VMEM((n_ref, 6 * n_feat), jnp.bfloat16),
        ],
        compiler_params=pltpu.CompilerParams(dimension_semantics=("arbitrary",)),
    )(queries, spread, query_ids, references)


def bit_reversed_index(p, n_bits):
    out = 0
    for b in range(n_bits):
        out = out + (p // (2 ** b)) % 2 * (2 ** (n_bits - 1 - b))
    return out


def local_backward(expd_low, scale, query_aug, unscaled_t, queries, references, inv, n_dev):
    n_ref, n_query = expd_low.shape
    n_feat = queries.shape[1]
    width = query_aug.shape[1]
    tile = min(TILE, n_query)
    sub = n_query // n_dev
    n_bits = n_dev.bit_length() - 1
    whole = lambda i: (0, 0)
    return pl.pallas_call(
        functools.partial(backward_kernel, n_bits),
        grid=(n_query // tile,),
        in_specs=[
            pl.BlockSpec((n_ref, tile), lambda i: (0, i)),
            pl.BlockSpec((1, tile), lambda i: (0, i)),
            pl.BlockSpec((tile, width), lambda i: (i, 0)),
            pl.BlockSpec((n_feat, tile), lambda i: (0, i)),
            pl.BlockSpec((tile, n_feat), lambda i: (i, 0)),
            pl.BlockSpec((n_ref, n_feat), whole),
            pl.BlockSpec((1, n_feat), whole),
        ],
        out_specs=[
            pl.BlockSpec((n_ref, n_feat), whole),
            pl.BlockSpec(memory_space=pl.ANY),
            pl.BlockSpec((8, n_feat), whole),
        ],
        out_shape=[
            jax.ShapeDtypeStruct((n_ref, n_feat), jnp.float32),
            jax.ShapeDtypeStruct((n_query, n_feat), jnp.float32),
            jax.ShapeDtypeStruct((8, n_feat), jnp.float32),
        ],
        scratch_shapes=[
            pltpu.VMEM((n_ref, width), jnp.float32),
            pltpu.VMEM((1, n_feat), jnp.float32),
            pltpu.VMEM((tile, n_feat), jnp.float32),
            pltpu.SemaphoreType.DMA((tile // sub,)),
        ],
        compiler_params=pltpu.CompilerParams(dimension_semantics=("arbitrary",)),
    )(expd_low, scale, query_aug, unscaled_t, queries, references, inv)


def bit_reversed(n):
    bits = n.bit_length() - 1
    return np.array([int(format(p, f"0{bits}b")[::-1], 2) if bits else 0 for p in range(n)], np.int32)


def exchange(x, n_dev, step):
    return lax.ppermute(x, "ref", [(i, i ^ step) for i in range(n_dev)])


def butterfly_stats(peak, total, n_dev):
    step = 1
    while step < n_dev:
        other = exchange(jnp.stack([peak, total]), n_dev, step)
        other_peak, other_total = other[0], other[1]
        new_peak = jnp.maximum(peak, other_peak)
        total = total * jnp.exp(peak - new_peak) + other_total * jnp.exp(other_peak - new_peak)
        peak = new_peak
        step *= 2
    return peak, total


def halving_scatter(rows, extra, n_dev):
    me = lax.axis_index("ref")
    n_feat = rows.shape[-1]
    blocks = rows.reshape(n_dev, -1, n_feat)
    step = 1
    while step < n_dev:
        half = blocks.shape[0] // 2
        bit = (me // step) % 2
        keep = lax.dynamic_slice_in_dim(blocks, bit * half, half, 0)
        send = lax.dynamic_slice_in_dim(blocks, (1 - bit) * half, half, 0)
        n_send = send.shape[0] * send.shape[1]
        got = exchange(jnp.concatenate([send.reshape(n_send, n_feat), extra]), n_dev, step)
        blocks = keep + got[:n_send].reshape(keep.shape)
        extra = extra + got[n_send:]
        step *= 2
    return blocks.reshape(-1, n_feat), extra


def on_device(queries, references, query_ids, spread, cotangent):
    n_query = queries.shape[0]
    n_feat = queries.shape[1]
    n_ref = references.shape[0]
    n_dev = lax.axis_size("ref")
    own_rows = n_query // n_dev
    inv = 1.0 / (spread * spread)
    expd_low, unscaled_t, local_peak, local_total = local_forward(queries, spread[None, :], query_ids[None, :], references)
    peak, total = butterfly_stats(local_peak[0], local_total[0], n_dev)
    scale = cotangent * jnp.exp(local_peak[0] - peak) / total
    query_low = queries.astype(jnp.bfloat16)
    query_aug = jnp.concatenate(
        [query_low, jnp.ones((n_query, 1), jnp.bfloat16), jnp.zeros((n_query, n_feat - 1), jnp.bfloat16)], axis=1
    )
    reference_grad, pulled, local_terms = local_backward(
        expd_low, scale[None, :], query_aug, unscaled_t, queries, references, inv[None, :], n_dev
    )
    own_pulled, summed_terms = halving_scatter(pulled, local_terms, n_dev)
    own_start = lax.axis_index("ref") * own_rows
    own_queries = lax.dynamic_slice_in_dim(queries, own_start, own_rows, 0)
    own_cot = lax.dynamic_slice_in_dim(cotangent, own_start, own_rows, 0)
    query_grad = (own_pulled - own_queries * own_cot[:, None]) * inv
    self_terms = jnp.sum(queries * queries * cotangent[:, None], axis=0)
    summed = (summed_terms[0] - self_terms) * inv + summed_terms[1]
    weight_total = jnp.sum(cotangent)
    spread_grad = -summed / spread - weight_total / spread
    return (query_grad, reference_grad, spread_grad)


def solution(mesh):
    placed = (P("parts", None), P(("parts", "ref"), None), P("parts"), P(), P("parts"))
    return jax.shard_map(
        on_device,
        mesh=mesh,
        in_specs=placed,
        out_specs=(P(("parts", "ref"), None), P(("parts", "ref"), None), P("parts")),
        check_vma=False,
    )
```

```python
import functools

import numpy as np
import jax
import jax.numpy as jnp
from jax import lax
from jax.experimental import pallas as pl
from jax.experimental.pallas import tpu as pltpu
from jax.sharding import PartitionSpec as P

TILE = 1024


def split3(x):
    x1 = x.astype(jnp.bfloat16)
    rest = x - x1.astype(jnp.float32)
    x2 = rest.astype(jnp.bfloat16)
    x3 = (rest - x2.astype(jnp.float32)).astype(jnp.bfloat16)
    return x1, x2, x3


def forward_kernel(q_ref, sp_ref, id_ref, r_ref, e_ref, ut_ref, st_ref, rn_sc, rlt_sc, rs_sc):
    spread = sp_ref[...]
    inv = 1.0 / (spread * spread)

    @pl.when(pl.program_id(0) == 0)
    def _():
        refs = r_ref[...]
        rn_sc[...] = 0.5 * jnp.sum(refs * refs * inv, axis=1, keepdims=True)
        rlt_sc[...] = refs.T.astype(jnp.bfloat16)
        r1, r2, r3 = split3(refs)
        rs_sc[...] = jnp.concatenate([r1, r1, r1, r2, r2, r3], axis=1)

    q = q_ref[...]
    ones = jnp.ones((8, q.shape[1]), jnp.float32)
    qnorm = lax.dot_general(
        ones, q * q * inv, (((1,), (1,)), ((), ())),
        precision=lax.Precision.HIGHEST, preferred_element_type=jnp.float32,
    )[0:1, :]
    q1, q2, q3 = split3(q * inv)
    cross = lax.dot_general(
        rs_sc[...], jnp.concatenate([q1, q2, q3, q1, q2, q1], axis=1), (((1,), (1,)), ((), ())),
        preferred_element_type=jnp.float32,
    )
    shifted = cross - rn_sc[...]
    row = lax.broadcasted_iota(jnp.int32, shifted.shape, 0)
    local_ids = id_ref[...] - lax.axis_index("ref") * shifted.shape[0]
    shifted = jnp.where(row == local_ids, -jnp.inf, shifted)
    top = jnp.max(shifted, axis=0, keepdims=True)
    expd = jnp.exp(shifted - top)
    st_ref[0:1, :] = top - 0.5 * qnorm
    st_ref[1:2, :] = jnp.sum(expd, axis=0, keepdims=True)
    expd_low = expd.astype(jnp.bfloat16)
    e_ref[...] = expd_low
    ut_ref[...] = jnp.dot(rlt_sc[...], expd_low, preferred_element_type=jnp.float32)


def backward_kernel(n_bits, e_ref, sc_ref, qa_ref, ut_ref, q_ref, r_ref, inv_ref, rg_ref, pull_hbm, terms_ref,
                    acc_sc, qt_sc, pull_sc, sems):
    step = pl.program_id(0)
    n_feat = q_ref.shape[1]
    tile = pull_sc.shape[0]
    sub = pull_hbm.shape[0] // (2 ** n_bits)
    per = tile // sub

    @pl.when(step == 0)
    def _():
        acc_sc[...] = jnp.zeros_like(acc_sc)
        qt_sc[...] = jnp.zeros_like(qt_sc)

    scale = sc_ref[...]
    pulled = (ut_ref[...] * scale).T
    pull_sc[...] = pulled
    copies = []
    for j in range(per):
        dst = bit_reversed_index(step * per + j, n_bits) * sub
        copy = pltpu.make_async_copy(
            pull_sc.at[pl.ds(j * sub, sub)], pull_hbm.at[pl.ds(pl.multiple_of(dst, sub), sub)], sems.at[j]
        )
        copy.start()
        copies.append(copy)
    weight = (e_ref[...].astype(jnp.float32) * scale).astype(jnp.bfloat16)
    acc_sc[...] += jnp.dot(weight, qa_ref[...], preferred_element_type=jnp.float32)
    qt_sc[...] += jnp.sum(q_ref[...] * pulled, axis=0, keepdims=True)
    for copy in copies:
        copy.wait()

    @pl.when(step == pl.num_programs(0) - 1)
    def _():
        acc = acc_sc[...]
        refs = r_ref[...]
        rgrad = (acc[:, :n_feat] - refs * acc[:, n_feat:n_feat + 1]) * inv_ref[...]
        rg_ref[...] = rgrad
        rterm = jnp.sum(refs * rgrad, axis=0, keepdims=True)
        terms_ref[...] = jnp.concatenate([qt_sc[...], rterm, jnp.zeros((6, n_feat), jnp.float32)], axis=0)


def local_forward(queries, spread, query_ids, references):
    n_query, n_feat = queries.shape
    n_ref = references.shape[0]
    tile = min(TILE, n_query)
    return pl.pallas_call(
        forward_kernel,
        grid=(n_query // tile,),
        in_specs=[
            pl.BlockSpec((tile, n_feat), lambda i: (i, 0)),
            pl.BlockSpec((1, n_feat), lambda i: (0, 0)),
            pl.BlockSpec((1, tile), lambda i: (0, i)),
            pl.BlockSpec((n_ref, n_feat), lambda i: (0, 0)),
        ],
        out_specs=[
            pl.BlockSpec((n_ref, tile), lambda i: (0, i)),
            pl.BlockSpec((n_feat, tile), lambda i: (0, i)),
            pl.BlockSpec((2, tile), lambda i: (0, i)),
        ],
        out_shape=[
            jax.ShapeDtypeStruct((n_ref, n_query), jnp.bfloat16),
            jax.ShapeDtypeStruct((n_feat, n_query), jnp.float32),
            jax.ShapeDtypeStruct((2, n_query), jnp.float32),
        ],
        scratch_shapes=[
            pltpu.VMEM((n_ref, 1), jnp.float32),
            pltpu.VMEM((n_feat, n_ref), jnp.bfloat16),
            pltpu.VMEM((n_ref, 6 * n_feat), jnp.bfloat16),
        ],
        compiler_params=pltpu.CompilerParams(dimension_semantics=("arbitrary",)),
    )(queries, spread, query_ids, references)


def bit_reversed_index(p, n_bits):
    out = 0
    for b in range(n_bits):
        out = out + (p // (2 ** b)) % 2 * (2 ** (n_bits - 1 - b))
    return out


def local_backward(expd_low, scale, query_aug, unscaled_t, queries, references, inv, n_dev):
    n_ref, n_query = expd_low.shape
    n_feat = queries.shape[1]
    width = query_aug.shape[1]
    tile = min(TILE, n_query)
    sub = n_query // n_dev
    n_bits = n_dev.bit_length() - 1
    whole = lambda i: (0, 0)
    return pl.pallas_call(
        functools.partial(backward_kernel, n_bits),
        grid=(n_query // tile,),
        in_specs=[
            pl.BlockSpec((n_ref, tile), lambda i: (0, i)),
            pl.BlockSpec((1, tile), lambda i: (0, i)),
            pl.BlockSpec((tile, width), lambda i: (i, 0)),
            pl.BlockSpec((n_feat, tile), lambda i: (0, i)),
            pl.BlockSpec((tile, n_feat), lambda i: (i, 0)),
            pl.BlockSpec((n_ref, n_feat), whole),
            pl.BlockSpec((1, n_feat), whole),
        ],
        out_specs=[
            pl.BlockSpec((n_ref, n_feat), whole),
            pl.BlockSpec(memory_space=pl.ANY),
            pl.BlockSpec((8, n_feat), whole),
        ],
        out_shape=[
            jax.ShapeDtypeStruct((n_ref, n_feat), jnp.float32),
            jax.ShapeDtypeStruct((n_query, n_feat), jnp.float32),
            jax.ShapeDtypeStruct((8, n_feat), jnp.float32),
        ],
        scratch_shapes=[
            pltpu.VMEM((n_ref, width), jnp.float32),
            pltpu.VMEM((1, n_feat), jnp.float32),
            pltpu.VMEM((tile, n_feat), jnp.float32),
            pltpu.SemaphoreType.DMA((tile // sub,)),
        ],
        compiler_params=pltpu.CompilerParams(dimension_semantics=("arbitrary",)),
    )(expd_low, scale, query_aug, unscaled_t, queries, references, inv)


def bit_reversed(n):
    bits = n.bit_length() - 1
    return np.array([int(format(p, f"0{bits}b")[::-1], 2) if bits else 0 for p in range(n)], np.int32)


def exchange(x, n_dev, step):
    return lax.ppermute(x, "ref", [(i, i ^ step) for i in range(n_dev)])


def butterfly_stats(stats, n_dev):
    peak, total = stats[0], stats[1]
    step = 1
    while step < n_dev:
        other = exchange(stats, n_dev, step)
        other_peak, other_total = other[0], other[1]
        new_peak = jnp.maximum(peak, other_peak)
        total = total * jnp.exp(peak - new_peak) + other_total * jnp.exp(other_peak - new_peak)
        peak = new_peak
        stats = jnp.stack([peak, total])
        step *= 2
    return peak, total


def halving_scatter(rows, extra, n_dev):
    me = lax.axis_index("ref")
    n_feat = rows.shape[-1]
    blocks = rows.reshape(n_dev, -1, n_feat)
    step = 1
    while step < n_dev:
        half = blocks.shape[0] // 2
        bit = (me // step) % 2
        keep = lax.dynamic_slice_in_dim(blocks, bit * half, half, 0)
        send = lax.dynamic_slice_in_dim(blocks, (1 - bit) * half, half, 0)
        n_send = send.shape[0] * send.shape[1]
        got = exchange(jnp.concatenate([send.reshape(n_send, n_feat), extra]), n_dev, step)
        blocks = keep + got[:n_send].reshape(keep.shape)
        extra = extra + got[n_send:]
        step *= 2
    return blocks.reshape(-1, n_feat), extra


def on_device(queries, references, query_ids, spread, cotangent):
    n_query = queries.shape[0]
    n_feat = queries.shape[1]
    n_ref = references.shape[0]
    n_dev = lax.axis_size("ref")
    own_rows = n_query // n_dev
    inv = 1.0 / (spread * spread)
    expd_low, unscaled_t, local_stats = local_forward(queries, spread[None, :], query_ids[None, :], references)
    peak, total = butterfly_stats(local_stats, n_dev)
    scale = cotangent * jnp.exp(local_stats[0] - peak) / total
    query_low = queries.astype(jnp.bfloat16)
    query_aug = jnp.concatenate(
        [query_low, jnp.ones((n_query, 1), jnp.bfloat16), jnp.zeros((n_query, n_feat - 1), jnp.bfloat16)], axis=1
    )
    reference_grad, pulled, local_terms = local_backward(
        expd_low, scale[None, :], query_aug, unscaled_t, queries, references, inv[None, :], n_dev
    )
    own_pulled, summed_terms = halving_scatter(pulled, local_terms, n_dev)
    own_start = lax.axis_index("ref") * own_rows
    own_queries = lax.dynamic_slice_in_dim(queries, own_start, own_rows, 0)
    own_cot = lax.dynamic_slice_in_dim(cotangent, own_start, own_rows, 0)
    query_grad = (own_pulled - own_queries * own_cot[:, None]) * inv
    self_terms = jnp.sum(queries * queries * cotangent[:, None], axis=0)
    summed = (summed_terms[0] - self_terms) * inv + summed_terms[1]
    weight_total = jnp.sum(cotangent)
    spread_grad = -summed / spread - weight_total / spread
    return (query_grad, reference_grad, spread_grad)


def solution(mesh):
    placed = (P("parts", None), P(("parts", "ref"), None), P("parts"), P(), P("parts"))
    return jax.shard_map(
        on_device,
        mesh=mesh,
        in_specs=placed,
        out_specs=(P(("parts", "ref"), None), P(("parts", "ref"), None), P("parts")),
        check_vma=False,
    )
```

```python
import functools

import numpy as np
import jax
import jax.numpy as jnp
from jax import lax
from jax.experimental import pallas as pl
from jax.experimental.pallas import tpu as pltpu
from jax.sharding import PartitionSpec as P

TILE = 1024


def split3(x):
    x1 = x.astype(jnp.bfloat16)
    rest = x - x1.astype(jnp.float32)
    x2 = rest.astype(jnp.bfloat16)
    x3 = (rest - x2.astype(jnp.float32)).astype(jnp.bfloat16)
    return x1, x2, x3


def forward_kernel(q_ref, sp_ref, id_ref, r_ref, e_ref, ut_ref, st_ref, rn_sc, rlt_sc, rs_sc):
    spread = sp_ref[...]
    inv = 1.0 / (spread * spread)

    @pl.when(pl.program_id(0) == 0)
    def _():
        refs = r_ref[...]
        rn_sc[...] = 0.5 * jnp.sum(refs * refs * inv, axis=1, keepdims=True)
        rlt_sc[...] = refs.T.astype(jnp.bfloat16)
        r1, r2, r3 = split3(refs)
        rs_sc[...] = jnp.concatenate([r1, r1, r1, r2, r2, r3], axis=1)

    q = q_ref[...]
    ones = jnp.ones((8, q.shape[1]), jnp.float32)
    qnorm = lax.dot_general(
        ones, q * q * inv, (((1,), (1,)), ((), ())),
        precision=lax.Precision.HIGHEST, preferred_element_type=jnp.float32,
    )[0:1, :]
    q1, q2, q3 = split3(q * inv)
    cross = lax.dot_general(
        rs_sc[...], jnp.concatenate([q1, q2, q3, q1, q2, q1], axis=1), (((1,), (1,)), ((), ())),
        preferred_element_type=jnp.float32,
    )
    shifted = cross - rn_sc[...]
    row = lax.broadcasted_iota(jnp.int32, shifted.shape, 0)
    local_ids = id_ref[...] - lax.axis_index("ref") * shifted.shape[0]
    shifted = jnp.where(row == local_ids, -jnp.inf, shifted)
    top = jnp.max(shifted, axis=0, keepdims=True)
    expd = jnp.exp(shifted - top)
    st_ref[0:1, :] = top - 0.5 * qnorm
    st_ref[1:2, :] = jnp.sum(expd, axis=0, keepdims=True)
    expd_low = expd.astype(jnp.bfloat16)
    e_ref[...] = expd_low
    ut_ref[...] = jnp.dot(rlt_sc[...], expd_low, preferred_element_type=jnp.float32)


def backward_kernel(n_bits, e_ref, cot_ref, ls_ref, gs_ref, qa_ref, ut_ref, q_ref, r_hbm, inv_ref, rg_ref, pull_hbm,
                    terms_ref, acc_sc, qt_sc, pull_sc, r_sc, sems, r_sem):
    step = pl.program_id(0)
    n_feat = q_ref.shape[1]
    tile = pull_sc.shape[0]
    sub = pull_hbm.shape[0] // (2 ** n_bits)
    per = tile // sub

    refs_copy = pltpu.make_async_copy(r_hbm, r_sc, r_sem)

    @pl.when(step == 0)
    def _():
        refs_copy.start()
        acc_sc[...] = jnp.zeros_like(acc_sc)
        qt_sc[...] = jnp.zeros_like(qt_sc)

    scale = cot_ref[...] * jnp.exp(ls_ref[0:1, :] - gs_ref[0:1, :]) / gs_ref[1:2, :]
    pulled = (ut_ref[...] * scale).T
    pull_sc[...] = pulled
    copies = []
    for j in range(per):
        dst = bit_reversed_index(step * per + j, n_bits) * sub
        copy = pltpu.make_async_copy(
            pull_sc.at[pl.ds(j * sub, sub)], pull_hbm.at[pl.ds(pl.multiple_of(dst, sub), sub)], sems.at[j]
        )
        copy.start()
        copies.append(copy)
    weight = (e_ref[...].astype(jnp.float32) * scale).astype(jnp.bfloat16)
    acc_sc[...] += jnp.dot(weight, qa_ref[...], preferred_element_type=jnp.float32)
    qt_sc[...] += jnp.sum(q_ref[...] * pulled, axis=0, keepdims=True)
    for copy in copies:
        copy.wait()

    @pl.when(step == pl.num_programs(0) - 1)
    def _():
        refs_copy.wait()
        acc = acc_sc[...]
        refs = r_sc[...]
        rgrad = (acc[:, :n_feat] - refs * acc[:, n_feat:n_feat + 1]) * inv_ref[...]
        rg_ref[...] = rgrad
        rterm = jnp.sum(refs * rgrad, axis=0, keepdims=True)
        terms_ref[...] = jnp.concatenate([qt_sc[...], rterm, jnp.zeros((6, n_feat), jnp.float32)], axis=0)


def local_forward(queries, spread, query_ids, references):
    n_query, n_feat = queries.shape
    n_ref = references.shape[0]
    tile = min(TILE, n_query)
    return pl.pallas_call(
        forward_kernel,
        grid=(n_query // tile,),
        in_specs=[
            pl.BlockSpec((tile, n_feat), lambda i: (i, 0)),
            pl.BlockSpec((1, n_feat), lambda i: (0, 0)),
            pl.BlockSpec((1, tile), lambda i: (0, i)),
            pl.BlockSpec((n_ref, n_feat), lambda i: (0, 0)),
        ],
        out_specs=[
            pl.BlockSpec((n_ref, tile), lambda i: (0, i)),
            pl.BlockSpec((n_feat, tile), lambda i: (0, i)),
            pl.BlockSpec((2, tile), lambda i: (0, i)),
        ],
        out_shape=[
            jax.ShapeDtypeStruct((n_ref, n_query), jnp.bfloat16),
            jax.ShapeDtypeStruct((n_feat, n_query), jnp.float32),
            jax.ShapeDtypeStruct((2, n_query), jnp.float32),
        ],
        scratch_shapes=[
            pltpu.VMEM((n_ref, 1), jnp.float32),
            pltpu.VMEM((n_feat, n_ref), jnp.bfloat16),
            pltpu.VMEM((n_ref, 6 * n_feat), jnp.bfloat16),
        ],
        compiler_params=pltpu.CompilerParams(dimension_semantics=("arbitrary",)),
    )(queries, spread, query_ids, references)


def bit_reversed_index(p, n_bits):
    out = 0
    for b in range(n_bits):
        out = out + (p // (2 ** b)) % 2 * (2 ** (n_bits - 1 - b))
    return out


def local_backward(expd_low, cot, local_stats, stats, query_aug, unscaled_t, queries, references, inv, n_dev):
    n_ref, n_query = expd_low.shape
    n_feat = queries.shape[1]
    width = query_aug.shape[1]
    tile = min(TILE, n_query)
    sub = n_query // n_dev
    n_bits = n_dev.bit_length() - 1
    whole = lambda i: (0, 0)
    return pl.pallas_call(
        functools.partial(backward_kernel, n_bits),
        grid=(n_query // tile,),
        in_specs=[
            pl.BlockSpec((n_ref, tile), lambda i: (0, i)),
            pl.BlockSpec((1, tile), lambda i: (0, i)),
            pl.BlockSpec((2, tile), lambda i: (0, i)),
            pl.BlockSpec((2, tile), lambda i: (0, i)),
            pl.BlockSpec((tile, width), lambda i: (i, 0)),
            pl.BlockSpec((n_feat, tile), lambda i: (0, i)),
            pl.BlockSpec((tile, n_feat), lambda i: (i, 0)),
            pl.BlockSpec(memory_space=pl.ANY),
            pl.BlockSpec((1, n_feat), whole),
        ],
        out_specs=[
            pl.BlockSpec((n_ref, n_feat), whole),
            pl.BlockSpec(memory_space=pl.ANY),
            pl.BlockSpec((8, n_feat), whole),
        ],
        out_shape=[
            jax.ShapeDtypeStruct((n_ref, n_feat), jnp.float32),
            jax.ShapeDtypeStruct((n_query, n_feat), jnp.float32),
            jax.ShapeDtypeStruct((8, n_feat), jnp.float32),
        ],
        scratch_shapes=[
            pltpu.VMEM((n_ref, width), jnp.float32),
            pltpu.VMEM((1, n_feat), jnp.float32),
            pltpu.VMEM((tile, n_feat), jnp.float32),
            pltpu.VMEM((n_ref, n_feat), jnp.float32),
            pltpu.SemaphoreType.DMA((tile // sub,)),
            pltpu.SemaphoreType.DMA(()),
        ],
        compiler_params=pltpu.CompilerParams(dimension_semantics=("arbitrary",)),
    )(expd_low, cot, local_stats, stats, query_aug, unscaled_t, queries, references, inv)


def bit_reversed(n):
    bits = n.bit_length() - 1
    return np.array([int(format(p, f"0{bits}b")[::-1], 2) if bits else 0 for p in range(n)], np.int32)


def exchange(x, n_dev, step):
    return lax.ppermute(x, "ref", [(i, i ^ step) for i in range(n_dev)])


def butterfly_stats(stats, n_dev):
    peak, total = stats[0], stats[1]
    step = 1
    while step < n_dev:
        other = exchange(stats, n_dev, step)
        other_peak, other_total = other[0], other[1]
        new_peak = jnp.maximum(peak, other_peak)
        total = total * jnp.exp(peak - new_peak) + other_total * jnp.exp(other_peak - new_peak)
        peak = new_peak
        stats = jnp.stack([peak, total])
        step *= 2
    return stats


def halving_scatter(rows, extra, n_dev):
    me = lax.axis_index("ref")
    n_feat = rows.shape[-1]
    blocks = rows.reshape(n_dev, -1, n_feat)
    step = 1
    while step < n_dev:
        half = blocks.shape[0] // 2
        bit = (me // step) % 2
        keep = lax.dynamic_slice_in_dim(blocks, bit * half, half, 0)
        send = lax.dynamic_slice_in_dim(blocks, (1 - bit) * half, half, 0)
        n_send = send.shape[0] * send.shape[1]
        got = exchange(jnp.concatenate([send.reshape(n_send, n_feat), extra]), n_dev, step)
        blocks = keep + got[:n_send].reshape(keep.shape)
        extra = extra + got[n_send:]
        step *= 2
    return blocks.reshape(-1, n_feat), extra


def on_device(queries, references, query_ids, spread, cotangent):
    n_query = queries.shape[0]
    n_feat = queries.shape[1]
    n_ref = references.shape[0]
    n_dev = lax.axis_size("ref")
    own_rows = n_query // n_dev
    inv = 1.0 / (spread * spread)
    expd_low, unscaled_t, local_stats = local_forward(queries, spread[None, :], query_ids[None, :], references)
    stats = butterfly_stats(local_stats, n_dev)
    query_low = queries.astype(jnp.bfloat16)
    query_aug = jnp.concatenate(
        [query_low, jnp.ones((n_query, 1), jnp.bfloat16), jnp.zeros((n_query, n_feat - 1), jnp.bfloat16)], axis=1
    )
    reference_grad, pulled, local_terms = local_backward(
        expd_low, cotangent[None, :], local_stats, stats, query_aug, unscaled_t, queries, references, inv[None, :], n_dev
    )
    own_pulled, summed_terms = halving_scatter(pulled, local_terms, n_dev)
    own_start = lax.axis_index("ref") * own_rows
    own_queries = lax.dynamic_slice_in_dim(queries, own_start, own_rows, 0)
    own_cot = lax.dynamic_slice_in_dim(cotangent, own_start, own_rows, 0)
    query_grad = (own_pulled - own_queries * own_cot[:, None]) * inv
    self_terms = jnp.sum(queries * queries * cotangent[:, None], axis=0)
    summed = (summed_terms[0] - self_terms) * inv + summed_terms[1]
    weight_total = jnp.sum(cotangent)
    spread_grad = -summed / spread - weight_total / spread
    return (query_grad, reference_grad, spread_grad)


def solution(mesh):
    placed = (P("parts", None), P(("parts", "ref"), None), P("parts"), P(), P("parts"))
    return jax.shard_map(
        on_device,
        mesh=mesh,
        in_specs=placed,
        out_specs=(P(("parts", "ref"), None), P(("parts", "ref"), None), P("parts")),
        check_vma=False,
    )
```

```python
import functools

import numpy as np
import jax
import jax.numpy as jnp
from jax import lax
from jax.experimental import pallas as pl
from jax.experimental.pallas import tpu as pltpu
from jax.sharding import PartitionSpec as P

TILE = 1024


def split3(x):
    x1 = x.astype(jnp.bfloat16)
    rest = x - x1.astype(jnp.float32)
    x2 = rest.astype(jnp.bfloat16)
    x3 = (rest - x2.astype(jnp.float32)).astype(jnp.bfloat16)
    return x1, x2, x3


def forward_kernel(q_ref, sp_ref, id_ref, r_ref, e_ref, ut_ref, st_ref, rn_sc, rlt_sc, rs_sc):
    spread = sp_ref[...]
    inv = 1.0 / (spread * spread)

    @pl.when(pl.program_id(0) == 0)
    def _():
        refs = r_ref[...]
        rn_sc[...] = 0.5 * jnp.sum(refs * refs * inv, axis=1, keepdims=True)
        rlt_sc[...] = refs.T.astype(jnp.bfloat16)
        r1, r2, r3 = split3(refs)
        rs_sc[...] = jnp.concatenate([r1, r1, r1, r2, r2, r3], axis=1)

    q = q_ref[...]
    ones = jnp.ones((8, q.shape[1]), jnp.float32)
    qnorm = lax.dot_general(
        ones, q * q * inv, (((1,), (1,)), ((), ())),
        precision=lax.Precision.HIGHEST, preferred_element_type=jnp.float32,
    )[0:1, :]
    q1, q2, q3 = split3(q * inv)
    cross = lax.dot_general(
        rs_sc[...], jnp.concatenate([q1, q2, q3, q1, q2, q1], axis=1), (((1,), (1,)), ((), ())),
        preferred_element_type=jnp.float32,
    )
    shifted = cross - rn_sc[...]
    row = lax.broadcasted_iota(jnp.int32, shifted.shape, 0)
    local_ids = id_ref[...] - lax.axis_index("ref") * shifted.shape[0]
    shifted = jnp.where(row == local_ids, -jnp.inf, shifted)
    top = jnp.max(shifted, axis=0, keepdims=True)
    expd = jnp.exp(shifted - top)
    st_ref[0:1, :] = top - 0.5 * qnorm
    st_ref[1:2, :] = jnp.sum(expd, axis=0, keepdims=True)
    expd_low = expd.astype(jnp.bfloat16)
    e_ref[...] = expd_low
    ut_ref[...] = jnp.dot(rlt_sc[...], expd_low, preferred_element_type=jnp.float32)


def backward_kernel(n_bits, e_ref, cot_ref, ls_ref, gp_ref, gt_ref, qa_ref, ut_ref, q_ref, r_hbm, inv_ref, rg_ref, pull_hbm,
                    terms_ref, acc_sc, qt_sc, pull_sc, r_sc, sems, r_sem):
    step = pl.program_id(0)
    n_feat = q_ref.shape[1]
    tile = pull_sc.shape[0]
    sub = pull_hbm.shape[0] // (2 ** n_bits)
    per = tile // sub

    refs_copy = pltpu.make_async_copy(r_hbm, r_sc, r_sem)

    @pl.when(step == 0)
    def _():
        refs_copy.start()
        acc_sc[...] = jnp.zeros_like(acc_sc)
        qt_sc[...] = jnp.zeros_like(qt_sc)

    scale = cot_ref[...] * jnp.exp(ls_ref[0:1, :] - gp_ref[...]) / gt_ref[...]
    pulled = (ut_ref[...] * scale).T
    pull_sc[...] = pulled
    copies = []
    for j in range(per):
        dst = bit_reversed_index(step * per + j, n_bits) * sub
        copy = pltpu.make_async_copy(
            pull_sc.at[pl.ds(j * sub, sub)], pull_hbm.at[pl.ds(pl.multiple_of(dst, sub), sub)], sems.at[j]
        )
        copy.start()
        copies.append(copy)
    weight = (e_ref[...].astype(jnp.float32) * scale).astype(jnp.bfloat16)
    acc_sc[...] += jnp.dot(weight, qa_ref[...], preferred_element_type=jnp.float32)
    qt_sc[...] += jnp.sum(q_ref[...] * pulled, axis=0, keepdims=True)
    for copy in copies:
        copy.wait()

    @pl.when(step == pl.num_programs(0) - 1)
    def _():
        refs_copy.wait()
        acc = acc_sc[...]
        refs = r_sc[...]
        rgrad = (acc[:, :n_feat] - refs * acc[:, n_feat:n_feat + 1]) * inv_ref[...]
        rg_ref[...] = rgrad
        rterm = jnp.sum(refs * rgrad, axis=0, keepdims=True)
        terms_ref[...] = jnp.concatenate([qt_sc[...], rterm, jnp.zeros((6, n_feat), jnp.float32)], axis=0)


def local_forward(queries, spread, query_ids, references):
    n_query, n_feat = queries.shape
    n_ref = references.shape[0]
    tile = min(TILE, n_query)
    return pl.pallas_call(
        forward_kernel,
        grid=(n_query // tile,),
        in_specs=[
            pl.BlockSpec((tile, n_feat), lambda i: (i, 0)),
            pl.BlockSpec((1, n_feat), lambda i: (0, 0)),
            pl.BlockSpec((1, tile), lambda i: (0, i)),
            pl.BlockSpec((n_ref, n_feat), lambda i: (0, 0)),
        ],
        out_specs=[
            pl.BlockSpec((n_ref, tile), lambda i: (0, i)),
            pl.BlockSpec((n_feat, tile), lambda i: (0, i)),
            pl.BlockSpec((2, tile), lambda i: (0, i)),
        ],
        out_shape=[
            jax.ShapeDtypeStruct((n_ref, n_query), jnp.bfloat16),
            jax.ShapeDtypeStruct((n_feat, n_query), jnp.float32),
            jax.ShapeDtypeStruct((2, n_query), jnp.float32),
        ],
        scratch_shapes=[
            pltpu.VMEM((n_ref, 1), jnp.float32),
            pltpu.VMEM((n_feat, n_ref), jnp.bfloat16),
            pltpu.VMEM((n_ref, 6 * n_feat), jnp.bfloat16),
        ],
        compiler_params=pltpu.CompilerParams(dimension_semantics=("arbitrary",)),
    )(queries, spread, query_ids, references)


def bit_reversed_index(p, n_bits):
    out = 0
    for b in range(n_bits):
        out = out + (p // (2 ** b)) % 2 * (2 ** (n_bits - 1 - b))
    return out


def local_backward(expd_low, cot, local_stats, peak, total, query_aug, unscaled_t, queries, references, inv, n_dev):
    n_ref, n_query = expd_low.shape
    n_feat = queries.shape[1]
    width = query_aug.shape[1]
    tile = min(TILE, n_query)
    sub = n_query // n_dev
    n_bits = n_dev.bit_length() - 1
    whole = lambda i: (0, 0)
    return pl.pallas_call(
        functools.partial(backward_kernel, n_bits),
        grid=(n_query // tile,),
        in_specs=[
            pl.BlockSpec((n_ref, tile), lambda i: (0, i)),
            pl.BlockSpec((1, tile), lambda i: (0, i)),
            pl.BlockSpec((2, tile), lambda i: (0, i)),
            pl.BlockSpec((1, tile), lambda i: (0, i)),
            pl.BlockSpec((1, tile), lambda i: (0, i)),
            pl.BlockSpec((tile, width), lambda i: (i, 0)),
            pl.BlockSpec((n_feat, tile), lambda i: (0, i)),
            pl.BlockSpec((tile, n_feat), lambda i: (i, 0)),
            pl.BlockSpec(memory_space=pl.ANY),
            pl.BlockSpec((1, n_feat), whole),
        ],
        out_specs=[
            pl.BlockSpec((n_ref, n_feat), whole),
            pl.BlockSpec(memory_space=pl.ANY),
            pl.BlockSpec((8, n_feat), whole),
        ],
        out_shape=[
            jax.ShapeDtypeStruct((n_ref, n_feat), jnp.float32),
            jax.ShapeDtypeStruct((n_query, n_feat), jnp.float32),
            jax.ShapeDtypeStruct((8, n_feat), jnp.float32),
        ],
        scratch_shapes=[
            pltpu.VMEM((n_ref, width), jnp.float32),
            pltpu.VMEM((1, n_feat), jnp.float32),
            pltpu.VMEM((tile, n_feat), jnp.float32),
            pltpu.VMEM((n_ref, n_feat), jnp.float32),
            pltpu.SemaphoreType.DMA((tile // sub,)),
            pltpu.SemaphoreType.DMA(()),
        ],
        compiler_params=pltpu.CompilerParams(dimension_semantics=("arbitrary",)),
    )(expd_low, cot, local_stats, peak, total, query_aug, unscaled_t, queries, references, inv)


def bit_reversed(n):
    bits = n.bit_length() - 1
    return np.array([int(format(p, f"0{bits}b")[::-1], 2) if bits else 0 for p in range(n)], np.int32)


def exchange(x, n_dev, step):
    return lax.ppermute(x, "ref", [(i, i ^ step) for i in range(n_dev)])


def butterfly_stats(stats, n_dev):
    peak, total = stats[0], stats[1]
    step = 1
    while step < n_dev:
        other = exchange(stats, n_dev, step)
        other_peak, other_total = other[0], other[1]
        new_peak = jnp.maximum(peak, other_peak)
        total = total * jnp.exp(peak - new_peak) + other_total * jnp.exp(other_peak - new_peak)
        peak = new_peak
        step *= 2
        if step < n_dev:
            stats = jnp.stack([peak, total])
    return peak[None, :], total[None, :]


def halving_scatter(rows, extra, n_dev):
    me = lax.axis_index("ref")
    n_feat = rows.shape[-1]
    blocks = rows.reshape(n_dev, -1, n_feat)
    step = 1
    while step < n_dev:
        half = blocks.shape[0] // 2
        bit = (me // step) % 2
        keep = lax.dynamic_slice_in_dim(blocks, bit * half, half, 0)
        send = lax.dynamic_slice_in_dim(blocks, (1 - bit) * half, half, 0)
        n_send = send.shape[0] * send.shape[1]
        got = exchange(jnp.concatenate([send.reshape(n_send, n_feat), extra]), n_dev, step)
        blocks = keep + got[:n_send].reshape(keep.shape)
        extra = extra + got[n_send:]
        step *= 2
    return blocks.reshape(-1, n_feat), extra


def on_device(queries, references, query_ids, spread, cotangent):
    n_query = queries.shape[0]
    n_feat = queries.shape[1]
    n_ref = references.shape[0]
    n_dev = lax.axis_size("ref")
    own_rows = n_query // n_dev
    inv = 1.0 / (spread * spread)
    expd_low, unscaled_t, local_stats = local_forward(queries, spread[None, :], query_ids[None, :], references)
    peak, total = butterfly_stats(local_stats, n_dev)
    query_low = queries.astype(jnp.bfloat16)
    query_aug = jnp.concatenate(
        [query_low, jnp.ones((n_query, 1), jnp.bfloat16), jnp.zeros((n_query, n_feat - 1), jnp.bfloat16)], axis=1
    )
    reference_grad, pulled, local_terms = local_backward(
        expd_low, cotangent[None, :], local_stats, peak, total, query_aug, unscaled_t, queries, references, inv[None, :], n_dev
    )
    own_pulled, summed_terms = halving_scatter(pulled, local_terms, n_dev)
    own_start = lax.axis_index("ref") * own_rows
    own_queries = lax.dynamic_slice_in_dim(queries, own_start, own_rows, 0)
    own_cot = lax.dynamic_slice_in_dim(cotangent, own_start, own_rows, 0)
    query_grad = (own_pulled - own_queries * own_cot[:, None]) * inv
    self_terms = jnp.sum(queries * queries * cotangent[:, None], axis=0)
    summed = (summed_terms[0] - self_terms) * inv + summed_terms[1]
    weight_total = jnp.sum(cotangent)
    spread_grad = -summed / spread - weight_total / spread
    return (query_grad, reference_grad, spread_grad)


def solution(mesh):
    placed = (P("parts", None), P(("parts", "ref"), None), P("parts"), P(), P("parts"))
    return jax.shard_map(
        on_device,
        mesh=mesh,
        in_specs=placed,
        out_specs=(P(("parts", "ref"), None), P(("parts", "ref"), None), P("parts")),
        check_vma=False,
    )
```

```python
import functools

import numpy as np
import jax
import jax.numpy as jnp
from jax import lax
from jax.experimental import pallas as pl
from jax.experimental.pallas import tpu as pltpu
from jax.sharding import PartitionSpec as P

TILE = 1024


def split3(x):
    x1 = x.astype(jnp.bfloat16)
    rest = x - x1.astype(jnp.float32)
    x2 = rest.astype(jnp.bfloat16)
    x3 = (rest - x2.astype(jnp.float32)).astype(jnp.bfloat16)
    return x1, x2, x3


def forward_kernel(q_ref, sp_ref, id_ref, r_ref, e_ref, ut_ref, st_ref, rn_sc, rlt_sc, rs_sc):
    spread = sp_ref[...]
    inv = 1.0 / (spread * spread)

    @pl.when(pl.program_id(0) == 0)
    def _():
        refs = r_ref[...]
        rn_sc[...] = 0.5 * jnp.sum(refs * refs * inv, axis=1, keepdims=True)
        rlt_sc[...] = refs.T.astype(jnp.bfloat16)
        r1, r2, r3 = split3(refs)
        rs_sc[...] = jnp.concatenate([r1, r1, r1, r2, r2, r3], axis=1)

    q = q_ref[...]
    ones = jnp.ones((8, q.shape[1]), jnp.float32)
    qnorm = lax.dot_general(
        ones, q * q * inv, (((1,), (1,)), ((), ())),
        precision=lax.Precision.HIGHEST, preferred_element_type=jnp.float32,
    )[0:1, :]
    q1, q2, q3 = split3(q * inv)
    cross = lax.dot_general(
        rs_sc[...], jnp.concatenate([q1, q2, q3, q1, q2, q1], axis=1), (((1,), (1,)), ((), ())),
        preferred_element_type=jnp.float32,
    )
    shifted = cross - rn_sc[...]
    row = lax.broadcasted_iota(jnp.int32, shifted.shape, 0)
    local_ids = id_ref[...] - lax.axis_index("ref") * shifted.shape[0]
    shifted = jnp.where(row == local_ids, -jnp.inf, shifted)
    top = jnp.max(shifted, axis=0, keepdims=True)
    expd = jnp.exp(shifted - top)
    st_ref[0:1, :] = top - 0.5 * qnorm
    st_ref[1:2, :] = jnp.sum(expd, axis=0, keepdims=True)
    expd_low = expd.astype(jnp.bfloat16)
    e_ref[...] = expd_low
    ut_ref[...] = jnp.dot(rlt_sc[...], expd_low, preferred_element_type=jnp.float32)


def backward_kernel(n_bits, e_ref, cot_ref, ls_ref, gs_ref, qa_ref, ut_ref, q_ref, r_hbm, inv_ref, rg_ref, pull_hbm,
                    terms_ref, acc_sc, qt_sc, pull_sc, r_sc, sems, r_sem):
    step = pl.program_id(0)
    n_feat = q_ref.shape[1]
    tile = pull_sc.shape[0]
    sub = pull_hbm.shape[0] // (2 ** n_bits)
    per = tile // sub

    refs_copy = pltpu.make_async_copy(r_hbm, r_sc, r_sem)

    @pl.when(step == 0)
    def _():
        refs_copy.start()
        acc_sc[...] = jnp.zeros_like(acc_sc)
        qt_sc[...] = jnp.zeros_like(qt_sc)

    scale = cot_ref[...] * jnp.exp(ls_ref[0:1, :] - gs_ref[0:1, :]) / gs_ref[1:2, :]
    pulled = (ut_ref[...] * scale).T
    pull_sc[...] = pulled
    copies = []
    for j in range(per):
        dst = bit_reversed_index(step * per + j, n_bits) * sub
        copy = pltpu.make_async_copy(
            pull_sc.at[pl.ds(j * sub, sub)], pull_hbm.at[pl.ds(pl.multiple_of(dst, sub), sub)], sems.at[j]
        )
        copy.start()
        copies.append(copy)
    weight = (e_ref[...].astype(jnp.float32) * scale).astype(jnp.bfloat16)
    acc_sc[...] += jnp.dot(weight, qa_ref[...], preferred_element_type=jnp.float32)
    qt_sc[...] += jnp.sum(q_ref[...] * pulled, axis=0, keepdims=True)
    for copy in copies:
        copy.wait()

    @pl.when(step == pl.num_programs(0) - 1)
    def _():
        refs_copy.wait()
        acc = acc_sc[...]
        refs = r_sc[...]
        rgrad = (acc[:, :n_feat] - refs * acc[:, n_feat:n_feat + 1]) * inv_ref[...]
        rg_ref[...] = rgrad
        rterm = jnp.sum(refs * rgrad, axis=0, keepdims=True)
        terms_ref[...] = jnp.concatenate([qt_sc[...], rterm, jnp.zeros((6, n_feat), jnp.float32)], axis=0)


def local_forward(queries, spread, query_ids, references):
    n_query, n_feat = queries.shape
    n_ref = references.shape[0]
    tile = min(TILE // 2, n_query)
    return pl.pallas_call(
        forward_kernel,
        grid=(n_query // tile,),
        in_specs=[
            pl.BlockSpec((tile, n_feat), lambda i: (i, 0)),
            pl.BlockSpec((1, n_feat), lambda i: (0, 0)),
            pl.BlockSpec((1, tile), lambda i: (0, i)),
            pl.BlockSpec((n_ref, n_feat), lambda i: (0, 0)),
        ],
        out_specs=[
            pl.BlockSpec((n_ref, tile), lambda i: (0, i)),
            pl.BlockSpec((n_feat, tile), lambda i: (0, i)),
            pl.BlockSpec((2, tile), lambda i: (0, i)),
        ],
        out_shape=[
            jax.ShapeDtypeStruct((n_ref, n_query), jnp.bfloat16),
            jax.ShapeDtypeStruct((n_feat, n_query), jnp.float32),
            jax.ShapeDtypeStruct((2, n_query), jnp.float32),
        ],
        scratch_shapes=[
            pltpu.VMEM((n_ref, 1), jnp.float32),
            pltpu.VMEM((n_feat, n_ref), jnp.bfloat16),
            pltpu.VMEM((n_ref, 6 * n_feat), jnp.bfloat16),
        ],
        compiler_params=pltpu.CompilerParams(
            dimension_semantics=("arbitrary",)
        ),
    )(queries, spread, query_ids, references)


def bit_reversed_index(p, n_bits):
    out = 0
    for b in range(n_bits):
        out = out + (p // (2 ** b)) % 2 * (2 ** (n_bits - 1 - b))
    return out


def local_backward(expd_low, cot, local_stats, stats, query_aug, unscaled_t, queries, references, inv, n_dev):
    n_ref, n_query = expd_low.shape
    n_feat = queries.shape[1]
    width = query_aug.shape[1]
    tile = min(TILE, n_query)
    sub = n_query // n_dev
    n_bits = n_dev.bit_length() - 1
    whole = lambda i: (0, 0)
    return pl.pallas_call(
        functools.partial(backward_kernel, n_bits),
        grid=(n_query // tile,),
        in_specs=[
            pl.BlockSpec((n_ref, tile), lambda i: (0, i)),
            pl.BlockSpec((1, tile), lambda i: (0, i)),
            pl.BlockSpec((2, tile), lambda i: (0, i)),
            pl.BlockSpec((2, tile), lambda i: (0, i)),
            pl.BlockSpec((tile, width), lambda i: (i, 0)),
            pl.BlockSpec((n_feat, tile), lambda i: (0, i)),
            pl.BlockSpec((tile, n_feat), lambda i: (i, 0)),
            pl.BlockSpec(memory_space=pl.ANY),
            pl.BlockSpec((1, n_feat), whole),
        ],
        out_specs=[
            pl.BlockSpec((n_ref, n_feat), whole),
            pl.BlockSpec(memory_space=pl.ANY),
            pl.BlockSpec((8, n_feat), whole),
        ],
        out_shape=[
            jax.ShapeDtypeStruct((n_ref, n_feat), jnp.float32),
            jax.ShapeDtypeStruct((n_query, n_feat), jnp.float32),
            jax.ShapeDtypeStruct((8, n_feat), jnp.float32),
        ],
        scratch_shapes=[
            pltpu.VMEM((n_ref, width), jnp.float32),
            pltpu.VMEM((1, n_feat), jnp.float32),
            pltpu.VMEM((tile, n_feat), jnp.float32),
            pltpu.VMEM((n_ref, n_feat), jnp.float32),
            pltpu.SemaphoreType.DMA((tile // sub,)),
            pltpu.SemaphoreType.DMA(()),
        ],
        compiler_params=pltpu.CompilerParams(
            dimension_semantics=("arbitrary",)
        ),
    )(expd_low, cot, local_stats, stats, query_aug, unscaled_t, queries, references, inv)


def bit_reversed(n):
    bits = n.bit_length() - 1
    return np.array([int(format(p, f"0{bits}b")[::-1], 2) if bits else 0 for p in range(n)], np.int32)


def exchange(x, n_dev, step):
    return lax.ppermute(x, "ref", [(i, i ^ step) for i in range(n_dev)])


def butterfly_stats(stats, n_dev):
    peak, total = stats[0], stats[1]
    step = 1
    while step < n_dev:
        other = exchange(stats, n_dev, step)
        other_peak, other_total = other[0], other[1]
        new_peak = jnp.maximum(peak, other_peak)
        total = total * jnp.exp(peak - new_peak) + other_total * jnp.exp(other_peak - new_peak)
        peak = new_peak
        stats = jnp.stack([peak, total])
        step *= 2
    return stats


def halving_scatter(rows, extra, n_dev):
    me = lax.axis_index("ref")
    n_feat = rows.shape[-1]
    blocks = rows.reshape(n_dev, -1, n_feat)
    step = 1
    while step < n_dev:
        half = blocks.shape[0] // 2
        bit = (me // step) % 2
        keep = lax.dynamic_slice_in_dim(blocks, bit * half, half, 0)
        send = lax.dynamic_slice_in_dim(blocks, (1 - bit) * half, half, 0)
        n_send = send.shape[0] * send.shape[1]
        got = exchange(jnp.concatenate([send.reshape(n_send, n_feat), extra]), n_dev, step)
        blocks = keep + got[:n_send].reshape(keep.shape)
        extra = extra + got[n_send:]
        step *= 2
    return blocks.reshape(-1, n_feat), extra


def on_device(queries, references, query_ids, spread, cotangent):
    n_query = queries.shape[0]
    n_feat = queries.shape[1]
    n_ref = references.shape[0]
    n_dev = lax.axis_size("ref")
    own_rows = n_query // n_dev
    inv = 1.0 / (spread * spread)
    expd_low, unscaled_t, local_stats = local_forward(queries, spread[None, :], query_ids[None, :], references)
    stats = butterfly_stats(local_stats, n_dev)
    query_low = queries.astype(jnp.bfloat16)
    query_aug = jnp.concatenate(
        [query_low, jnp.ones((n_query, 1), jnp.bfloat16), jnp.zeros((n_query, n_feat - 1), jnp.bfloat16)], axis=1
    )
    reference_grad, pulled, local_terms = local_backward(
        expd_low, cotangent[None, :], local_stats, stats, query_aug, unscaled_t, queries, references, inv[None, :], n_dev
    )
    own_pulled, summed_terms = halving_scatter(pulled, local_terms, n_dev)
    own_start = lax.axis_index("ref") * own_rows
    own_queries = lax.dynamic_slice_in_dim(queries, own_start, own_rows, 0)
    own_cot = lax.dynamic_slice_in_dim(cotangent, own_start, own_rows, 0)
    query_grad = (own_pulled - own_queries * own_cot[:, None]) * inv
    self_terms = jnp.sum(queries * queries * cotangent[:, None], axis=0)
    summed = (summed_terms[0] - self_terms) * inv + summed_terms[1]
    weight_total = jnp.sum(cotangent)
    spread_grad = -summed / spread - weight_total / spread
    return (query_grad, reference_grad, spread_grad)


def solution(mesh):
    placed = (P("parts", None), P(("parts", "ref"), None), P("parts"), P(), P("parts"))
    return jax.shard_map(
        on_device,
        mesh=mesh,
        in_specs=placed,
        out_specs=(P(("parts", "ref"), None), P(("parts", "ref"), None), P("parts")),
        check_vma=False,
    )
```

```python
import functools

import numpy as np
import jax
import jax.numpy as jnp
from jax import lax
from jax.experimental import pallas as pl
from jax.experimental.pallas import tpu as pltpu
from jax.sharding import PartitionSpec as P

TILE = 1024


def split3(x):
    x1 = x.astype(jnp.bfloat16)
    rest = x - x1.astype(jnp.float32)
    x2 = rest.astype(jnp.bfloat16)
    x3 = (rest - x2.astype(jnp.float32)).astype(jnp.bfloat16)
    return x1, x2, x3


def forward_kernel(q_ref, sp_ref, id_ref, r_ref, e_ref, ut_ref, st_ref, rn_sc, rlt_sc, rs_sc):
    spread = sp_ref[...]
    inv = 1.0 / (spread * spread)

    @pl.when(pl.program_id(0) == 0)
    def _():
        refs = r_ref[...]
        rn_sc[...] = 0.5 * jnp.sum(refs * refs * inv, axis=1, keepdims=True)
        rlt_sc[...] = refs.T.astype(jnp.bfloat16)
        r1, r2, r3 = split3(refs)
        rs_sc[...] = jnp.concatenate([r1, r1, r1, r2, r2, r3], axis=1)

    q = q_ref[...]
    ones = jnp.ones((8, q.shape[1]), jnp.float32)
    qnorm = lax.dot_general(
        ones, q * q * inv, (((1,), (1,)), ((), ())),
        precision=lax.Precision.HIGHEST, preferred_element_type=jnp.float32,
    )[0:1, :]
    q1, q2, q3 = split3(q * inv)
    cross = lax.dot_general(
        rs_sc[...], jnp.concatenate([q1, q2, q3, q1, q2, q1], axis=1), (((1,), (1,)), ((), ())),
        preferred_element_type=jnp.float32,
    )
    shifted = cross - rn_sc[...]
    row = lax.broadcasted_iota(jnp.int32, shifted.shape, 0)
    local_ids = id_ref[...] - lax.axis_index("ref") * shifted.shape[0]
    shifted = jnp.where(row == local_ids, -jnp.inf, shifted)
    top = jnp.max(shifted, axis=0, keepdims=True)
    expd = jnp.exp(shifted - top)
    st_ref[0:1, :] = top - 0.5 * qnorm
    st_ref[1:2, :] = jnp.sum(expd, axis=0, keepdims=True)
    expd_low = expd.astype(jnp.bfloat16)
    e_ref[...] = expd_low
    ut_ref[...] = jnp.dot(rlt_sc[...], expd_low, preferred_element_type=jnp.float32)


def backward_kernel(n_bits, e_ref, cot_ref, ls_ref, gs_ref, qa_ref, ut_ref, q_ref, r_hbm, inv_ref, rg_ref, pull_hbm,
                    terms_ref, acc_sc, qt_sc, pull_sc, r_sc, sems, r_sem):
    step = pl.program_id(0)
    n_feat = q_ref.shape[1]
    tile = pull_sc.shape[0]
    sub = pull_hbm.shape[0] // (2 ** n_bits)
    per = tile // sub

    refs_copy = pltpu.make_async_copy(r_hbm, r_sc, r_sem)

    @pl.when(step == 0)
    def _():
        refs_copy.start()
        acc_sc[...] = jnp.zeros_like(acc_sc)
        qt_sc[...] = jnp.zeros_like(qt_sc)

    scale = cot_ref[...] * jnp.exp(ls_ref[0:1, :] - gs_ref[0:1, :]) / gs_ref[1:2, :]
    pulled = (ut_ref[...] * scale).T
    pull_sc[...] = pulled
    copies = []
    for j in range(per):
        dst = bit_reversed_index(step * per + j, n_bits) * sub
        copy = pltpu.make_async_copy(
            pull_sc.at[pl.ds(j * sub, sub)], pull_hbm.at[pl.ds(pl.multiple_of(dst, sub), sub)], sems.at[j]
        )
        copy.start()
        copies.append(copy)
    weight = (e_ref[...].astype(jnp.float32) * scale).astype(jnp.bfloat16)
    acc_sc[...] += jnp.dot(weight, qa_ref[...], preferred_element_type=jnp.float32)
    qt_sc[...] += jnp.sum(q_ref[...] * pulled, axis=0, keepdims=True)
    for copy in copies:
        copy.wait()

    @pl.when(step == pl.num_programs(0) - 1)
    def _():
        refs_copy.wait()
        acc = acc_sc[...]
        refs = r_sc[...]
        rgrad = (acc[:, :n_feat] - refs * acc[:, n_feat:n_feat + 1]) * inv_ref[...]
        rg_ref[...] = rgrad
        rterm = jnp.sum(refs * rgrad, axis=0, keepdims=True)
        terms_ref[...] = jnp.concatenate([qt_sc[...], rterm, jnp.zeros((6, n_feat), jnp.float32)], axis=0)


def local_forward(queries, spread, query_ids, references):
    n_query, n_feat = queries.shape
    n_ref = references.shape[0]
    tile = min(TILE // 2, n_query)
    return pl.pallas_call(
        forward_kernel,
        grid=(n_query // tile,),
        in_specs=[
            pl.BlockSpec((tile, n_feat), lambda i: (i, 0)),
            pl.BlockSpec((1, n_feat), lambda i: (0, 0)),
            pl.BlockSpec((1, tile), lambda i: (0, i)),
            pl.BlockSpec((n_ref, n_feat), lambda i: (0, 0)),
        ],
        out_specs=[
            pl.BlockSpec((n_ref, tile), lambda i: (0, i)),
            pl.BlockSpec((n_feat, tile), lambda i: (0, i)),
            pl.BlockSpec((2, tile), lambda i: (0, i)),
        ],
        out_shape=[
            jax.ShapeDtypeStruct((n_ref, n_query), jnp.bfloat16),
            jax.ShapeDtypeStruct((n_feat, n_query), jnp.float32),
            jax.ShapeDtypeStruct((2, n_query), jnp.float32),
        ],
        scratch_shapes=[
            pltpu.VMEM((n_ref, 1), jnp.float32),
            pltpu.VMEM((n_feat, n_ref), jnp.bfloat16),
            pltpu.VMEM((n_ref, 6 * n_feat), jnp.bfloat16),
        ],
        compiler_params=pltpu.CompilerParams(
            dimension_semantics=("arbitrary",)
        ),
    )(queries, spread, query_ids, references)


def bit_reversed_index(p, n_bits):
    out = 0
    for b in range(n_bits):
        out = out + (p // (2 ** b)) % 2 * (2 ** (n_bits - 1 - b))
    return out


def local_backward(expd_low, cot, local_stats, stats, query_aug, unscaled_t, queries, references, inv, n_dev):
    n_ref, n_query = expd_low.shape
    n_feat = queries.shape[1]
    width = query_aug.shape[1]
    tile = min(2 * TILE, n_query)
    sub = n_query // n_dev
    n_bits = n_dev.bit_length() - 1
    whole = lambda i: (0, 0)
    return pl.pallas_call(
        functools.partial(backward_kernel, n_bits),
        grid=(n_query // tile,),
        in_specs=[
            pl.BlockSpec((n_ref, tile), lambda i: (0, i)),
            pl.BlockSpec((1, tile), lambda i: (0, i)),
            pl.BlockSpec((2, tile), lambda i: (0, i)),
            pl.BlockSpec((2, tile), lambda i: (0, i)),
            pl.BlockSpec((tile, width), lambda i: (i, 0)),
            pl.BlockSpec((n_feat, tile), lambda i: (0, i)),
            pl.BlockSpec((tile, n_feat), lambda i: (i, 0)),
            pl.BlockSpec(memory_space=pl.ANY),
            pl.BlockSpec((1, n_feat), whole),
        ],
        out_specs=[
            pl.BlockSpec((n_ref, n_feat), whole),
            pl.BlockSpec(memory_space=pl.ANY),
            pl.BlockSpec((8, n_feat), whole),
        ],
        out_shape=[
            jax.ShapeDtypeStruct((n_ref, n_feat), jnp.float32),
            jax.ShapeDtypeStruct((n_query, n_feat), jnp.float32),
            jax.ShapeDtypeStruct((8, n_feat), jnp.float32),
        ],
        scratch_shapes=[
            pltpu.VMEM((n_ref, width), jnp.float32),
            pltpu.VMEM((1, n_feat), jnp.float32),
            pltpu.VMEM((tile, n_feat), jnp.float32),
            pltpu.VMEM((n_ref, n_feat), jnp.float32),
            pltpu.SemaphoreType.DMA((tile // sub,)),
            pltpu.SemaphoreType.DMA(()),
        ],
        compiler_params=pltpu.CompilerParams(
            dimension_semantics=("arbitrary",)
        ),
    )(expd_low, cot, local_stats, stats, query_aug, unscaled_t, queries, references, inv)


def bit_reversed(n):
    bits = n.bit_length() - 1
    return np.array([int(format(p, f"0{bits}b")[::-1], 2) if bits else 0 for p in range(n)], np.int32)


def exchange(x, n_dev, step):
    return lax.ppermute(x, "ref", [(i, i ^ step) for i in range(n_dev)])


def butterfly_stats(stats, n_dev):
    peak, total = stats[0], stats[1]
    step = 1
    while step < n_dev:
        other = exchange(stats, n_dev, step)
        other_peak, other_total = other[0], other[1]
        new_peak = jnp.maximum(peak, other_peak)
        total = total * jnp.exp(peak - new_peak) + other_total * jnp.exp(other_peak - new_peak)
        peak = new_peak
        stats = jnp.stack([peak, total])
        step *= 2
    return stats


def halving_scatter(rows, extra, n_dev):
    me = lax.axis_index("ref")
    n_feat = rows.shape[-1]
    blocks = rows.reshape(n_dev, -1, n_feat)
    step = 1
    while step < n_dev:
        half = blocks.shape[0] // 2
        bit = (me // step) % 2
        keep = lax.dynamic_slice_in_dim(blocks, bit * half, half, 0)
        send = lax.dynamic_slice_in_dim(blocks, (1 - bit) * half, half, 0)
        n_send = send.shape[0] * send.shape[1]
        got = exchange(jnp.concatenate([send.reshape(n_send, n_feat), extra]), n_dev, step)
        blocks = keep + got[:n_send].reshape(keep.shape)
        extra = extra + got[n_send:]
        step *= 2
    return blocks.reshape(-1, n_feat), extra


def on_device(queries, references, query_ids, spread, cotangent):
    n_query = queries.shape[0]
    n_feat = queries.shape[1]
    n_ref = references.shape[0]
    n_dev = lax.axis_size("ref")
    own_rows = n_query // n_dev
    inv = 1.0 / (spread * spread)
    expd_low, unscaled_t, local_stats = local_forward(queries, spread[None, :], query_ids[None, :], references)
    stats = butterfly_stats(local_stats, n_dev)
    query_low = queries.astype(jnp.bfloat16)
    query_aug = jnp.concatenate(
        [query_low, jnp.ones((n_query, 1), jnp.bfloat16), jnp.zeros((n_query, n_feat - 1), jnp.bfloat16)], axis=1
    )
    reference_grad, pulled, local_terms = local_backward(
        expd_low, cotangent[None, :], local_stats, stats, query_aug, unscaled_t, queries, references, inv[None, :], n_dev
    )
    own_pulled, summed_terms = halving_scatter(pulled, local_terms, n_dev)
    own_start = lax.axis_index("ref") * own_rows
    own_queries = lax.dynamic_slice_in_dim(queries, own_start, own_rows, 0)
    own_cot = lax.dynamic_slice_in_dim(cotangent, own_start, own_rows, 0)
    query_grad = (own_pulled - own_queries * own_cot[:, None]) * inv
    self_terms = jnp.sum(queries * queries * cotangent[:, None], axis=0)
    summed = (summed_terms[0] - self_terms) * inv + summed_terms[1]
    weight_total = jnp.sum(cotangent)
    spread_grad = -summed / spread - weight_total / spread
    return (query_grad, reference_grad, spread_grad)


def solution(mesh):
    placed = (P("parts", None), P(("parts", "ref"), None), P("parts"), P(), P("parts"))
    return jax.shard_map(
        on_device,
        mesh=mesh,
        in_specs=placed,
        out_specs=(P(("parts", "ref"), None), P(("parts", "ref"), None), P("parts")),
        check_vma=False,
    )
```
